32 devices in a mesh: grp: 2 (over y), seq: 4 (over z), kvh: 2 (over x), sub: 2 (over core).
Axes of the slice: x: 2, y: 2, z: 4, core: 2. Of those that a mesh axis runs over, the one named last changes fastest.
Arguments:
- tokens: bfloat16 [4096, 4096], P(('grp', 'seq'), ('kvh', 'sub')), parts along dimension 0, may hold values from -6 to 6
- norm_gain: float32 [4096], replicated, may hold values from 0.5 to 1.5
- w_query: bfloat16 [4096, 8, 512], P(None, 'kvh', 'sub')
- w_key: bfloat16 [4096, 8, 128], P('sub', 'kvh')
- w_value: bfloat16 [4096, 8, 128], P('sub', 'kvh'), may hold values from -0.09375 to 0.09375
- links: int32 [3, 8], replicated, may hold values from 0 to 7, as said below
Outputs:
- attended: bfloat16 [4096, 8, 512], P(('grp', 'seq'), 'kvh', 'sub'), parts along dimension 0
- gram: float32 [8192, 4096], P(('grp', 'seq'), ('kvh', 'sub')), parts along dimension 0
The draws below stay inside these ranges and needn't reach their ends.
There are 2 independent parts, one for each index of `grp`. The reference program is written for one: setup_inputs(seed, part) draws one part's arguments, and reference() takes and returns one part's arrays. A program takes and returns all parts, laid end to end along the dimension named above; an argument that names none is the same for every part. Nothing has to cross between parts.
Inputs may be any that keep to these rules, and one draw needn't show every extreme that they name: links[b, i] is either i or i xor 2 ** b; the pattern is symmetric: block i names its section-b partner exactly when that partner names i; block 0 names its partner at every section.
All inputs are finite; a program needn't handle non-finite values.
Results may differ from the reference program's by a relative error of at most 0.0095.
Values may be sent and summed in bfloat16 or wider, within the bound.
No kernel may reach another device: no remote copies, remote signals or barrier semaphores. Data moves between devices by JAX's collectives and lax.ppermute only.
A program may use at most 128 MiB of HBM per device.

```python
import math
import jax
import jax.numpy as jnp
from jax import lax

D = 4096
KV_HEADS = 8
HD = 128
BLK = 256
GROUP = 4
NBLK = 8
TOKENS = 2048
SECTIONS = 3


def projection_pair(key):
    key_part = jax.random.truncated_normal(jax.random.fold_in(key, 11), -4.0, 4.0, (D, KV_HEADS, HD), jnp.float32) / D ** 0.5
    query_part = jax.random.truncated_normal(jax.random.fold_in(key, 12), -4.0, 4.0, (D, KV_HEADS, GROUP, HD), jnp.float32) / D ** 0.5
    return (query_part.reshape(D, KV_HEADS, GROUP * HD), key_part)


def draw_w_query(key, part):
    return projection_pair(key)[0].astype(jnp.bfloat16)


def draw_w_key(key, part):
    return projection_pair(key)[1].astype(jnp.bfloat16)


def draw_links(key, part):
    coins = jax.random.randint(jax.random.fold_in(key, 21), (SECTIONS, NBLK), 0, 2)
    blocks = jnp.arange(NBLK, dtype=jnp.int32)
    rows = []
    for section in range(SECTIONS):
        base = blocks & ~(1 << section)
        partner = blocks ^ 1 << section
        linked = (coins[section][base] == 1) | (base == 0)
        rows.append(jnp.where(linked, partner, blocks))
    return jnp.stack(rows, axis=0).astype(jnp.int32)


def raised(entries, key, source, target, parts, factor):
    def block_of(axis_at):
        return (jnp.arange(entries.shape[axis_at]) // (entries.shape[axis_at] // parts)).reshape((-1,) + (1,) * (entries.ndim - 1 - axis_at))

    one_side = jax.random.permutation(key, parts)[block_of(target)]
    second = (block_of(target) + parts // 2) % parts
    return jnp.where((block_of(source) == one_side) | (block_of(source) == second), factor * entries, entries)


def shard_levels(own_key, shape, split, least, high):
    def one(position, shards_of):
        heights = jax.random.uniform(jax.random.fold_in(jax.random.fold_in(own_key, 6), position), (shards_of,), jnp.float32, least / len(split), high / len(split))
        return jnp.repeat(jnp.exp(heights), shape[position] // shards_of).reshape((-1,) + (1,) * (len(shape) - position - 1))

    gain = one(*split[0])
    for cut in split[1:]:
        gain = gain * one(*cut)
    return gain


def centred(rng, extent, spread, reach, split=(), kind=jnp.bfloat16):
    values = spread * jax.random.normal(rng, extent, jnp.float32)
    if split:
        values = values * shard_levels(rng, extent, split, -0.22, 0.18)
    return jnp.clip(values, -reach, reach).astype(kind)


def heavy_noise(own_key, shape, scale, limit, pieces, heavy, held_as=jnp.bfloat16):
    array = scale * jax.random.normal(own_key, shape, jnp.float32)
    if pieces:
        array = array * shard_levels(own_key, shape, pieces, -0.22, 0.18)
    return jnp.clip(raised(array, jax.random.fold_in(own_key, 3), *heavy), -limit, limit).astype(held_as)


def setup_inputs(seed: int = 0, part: int = 0) -> dict:
    key_of = jax.random.split(jax.random.key(seed), 7)
    part_splits = jax.random.split(jax.random.fold_in(key_of[6], part), 7)
    return {
        "tokens": heavy_noise(part_splits[0], (TOKENS, D), 1.0, 6.0, ((0, 4), (1, 4)), (0, 1, 4, 2.0)),
        "norm_gain": jnp.clip(1.0 + 0.1 * jax.random.normal(key_of[1], (D,), jnp.float32), 0.5, 1.5),
        "w_query": draw_w_query(jax.random.fold_in(key_of[6], 71), part),
        "w_key": draw_w_key(jax.random.fold_in(key_of[6], 71), part),
        "w_value": centred(key_of[4], (D, KV_HEADS, HD), D ** -0.5, 0.09375, ((0, 2), (1, 2))),
        "links": draw_links(jax.random.fold_in(key_of[6], 71), part),
    }


rope_base = 500000.0

def rotate(vectors, positions):
    width = vectors.shape[-1]
    half = width // 2
    inverse = jnp.exp(jnp.arange(half, dtype=jnp.float32) * (-2.0 * math.log(rope_base) / width))
    angles = positions.astype(jnp.float32)[:, None] * inverse[None, :]
    shape = (angles.shape[0],) + (1,) * (vectors.ndim - 2) + (half,)
    cosine = jnp.cos(angles).reshape(shape)
    sine = jnp.sin(angles).reshape(shape)
    first = vectors[..., :half]
    second = vectors[..., half:]
    return jnp.concatenate([first * cosine - second * sine, second * cosine + first * sine], axis=-1)

def reference(tokens, norm_gain, w_query, w_key, w_value, links):
    widened = tokens.astype(jnp.float32)
    mean_square = lax.optimization_barrier(jnp.mean(widened * widened, axis=-1, keepdims=True))
    normed = (widened * lax.rsqrt(mean_square + 1e-05) * norm_gain).astype(jnp.bfloat16)
    positions = jnp.arange(TOKENS, dtype=jnp.int32)
    queries = jnp.dot(normed, w_query.reshape(D, -1), preferred_element_type=jnp.float32)
    queries = rotate(queries.reshape(TOKENS, KV_HEADS, GROUP, HD), positions).astype(jnp.bfloat16)
    keys = jnp.dot(normed, w_key.reshape(D, -1), preferred_element_type=jnp.float32)
    keys = rotate(keys.reshape(TOKENS, KV_HEADS, HD), positions).astype(jnp.bfloat16)
    values = jnp.dot(normed, w_value.reshape(D, -1), preferred_element_type=jnp.float32)
    values = values.reshape(TOKENS, KV_HEADS, HD).astype(jnp.bfloat16)
    key_blocks = keys.astype(jnp.float32).reshape(NBLK, BLK, KV_HEADS, HD)
    value_blocks = values.astype(jnp.float32).reshape(NBLK, BLK, KV_HEADS, HD)
    local_rows = jnp.arange(BLK, dtype=jnp.int32)
    causal = local_rows[None, :] <= local_rows[:, None]

    def one_block(block_index):
        block_index = block_index.astype(jnp.int32)
        start_row = (block_index * BLK).astype(jnp.int32)
        query_rows = lax.dynamic_slice_in_dim(queries, start_row, BLK, 0).astype(jnp.float32)
        partner_list = links[:, block_index].astype(jnp.int32)
        chosen = jnp.concatenate([block_index[None], partner_list], axis=0)
        seen_keys = key_blocks[chosen].reshape((SECTIONS + 1) * BLK, KV_HEADS, HD)
        seen_values = value_blocks[chosen].reshape((SECTIONS + 1) * BLK, KV_HEADS, HD)
        scores = jnp.einsum('tgrh,ugh->grtu', query_rows, seen_keys) / math.sqrt(HD)
        linked = partner_list != block_index
        far_mask = jnp.broadcast_to(linked[:, None, None], (SECTIONS, BLK, BLK))
        far_mask = jnp.transpose(far_mask, (1, 0, 2)).reshape(BLK, SECTIONS * BLK)
        allowed = jnp.concatenate([causal, far_mask], axis=1)
        scores = jnp.where(allowed[None, None], scores, -jnp.inf)
        top = lax.optimization_barrier(jnp.max(scores, axis=-1, keepdims=True))
        weights = jnp.exp(scores - top)
        total = lax.optimization_barrier(jnp.sum(weights, axis=-1))
        rounded = weights.astype(jnp.bfloat16).astype(jnp.float32)
        summed = jnp.einsum('grtu,ugh->tgrh', rounded, seen_values)
        result = summed / jnp.transpose(total, (2, 0, 1))[..., None]
        return result.astype(jnp.bfloat16).reshape(BLK, KV_HEADS, GROUP * HD)
    blocks = lax.map(one_block, jnp.arange(NBLK, dtype=jnp.int32))
    attended = blocks.reshape(TOKENS, KV_HEADS, GROUP * HD)
    gram = jnp.dot(normed.T, normed, preferred_element_type=jnp.float32) / TOKENS
    return (attended, gram)
```

```python
import math

import jax
import jax.numpy as jnp
from jax import lax
from jax.sharding import PartitionSpec as P

rope_base = 500000.0


def from_partner(block, axis, bit):
    count = lax.axis_size(axis)
    route = []
    for low in range(count):
        high = low | 1 << bit
        if high != low and high < count:
            route += [(low, high), (high, low)]
    return lax.ppermute(block, axis, route)


def rotate(vectors, positions):
    width = vectors.shape[-1]
    half = width // 2
    inverse = jnp.exp(jnp.arange(half, dtype=jnp.float32) * (-2.0 * math.log(rope_base) / width))
    angles = positions.astype(jnp.float32)[:, None] * inverse[None, :]
    shape = (angles.shape[0],) + (1,) * (vectors.ndim - 2) + (half,)
    cosine = jnp.cos(angles).reshape(shape)
    sine = jnp.sin(angles).reshape(shape)
    first = vectors[..., :half]
    second = vectors[..., half:]
    return jnp.concatenate(
        [first * cosine - second * sine, second * cosine + first * sine], axis=-1
    )


def body(tokens, norm_gain, w_query, w_key, w_value, links):
    gathered = lax.all_gather(tokens, ("kvh", "sub"), axis=1, tiled=True)
    widened = gathered.astype(jnp.float32)
    mean_square = jnp.mean(widened * widened, axis=-1, keepdims=True)
    normed = (widened * lax.rsqrt(mean_square + 1e-05) * norm_gain).astype(jnp.bfloat16)
    row_count = normed.shape[0]
    block_len = row_count // 2
    width = normed.shape[1]
    seq_index = lax.axis_index("seq")
    local_rows = jnp.arange(row_count, dtype=jnp.int32)
    positions = seq_index * row_count + local_rows
    head_size = w_key.shape[2]
    local_groups = w_key.shape[1]
    per_group = w_query.shape[2] // head_size
    queries = jnp.einsum("td,dgc->tgc", normed, w_query, preferred_element_type=jnp.float32)
    queries = rotate(
        queries.reshape(row_count, local_groups, per_group, head_size), positions
    ).astype(jnp.bfloat16)
    sub_count = lax.axis_size("sub")
    sub_index = lax.axis_index("sub")
    row_share = w_key.shape[0]
    key_more = None
    value_more = None
    for shift in range(sub_count):
        if shift == 0:
            key_part, value_part = w_key, w_value
        else:
            route = [(j, (j + shift) % sub_count) for j in range(sub_count)]
            key_part, value_part = lax.ppermute((w_key, w_value), "sub", route)
        source = (sub_index - shift) % sub_count
        rows = lax.dynamic_slice_in_dim(normed, source * row_share, row_share, 1)
        key_step = jnp.einsum("td,dgh->tgh", rows, key_part, preferred_element_type=jnp.float32)
        value_step = jnp.einsum("td,dgh->tgh", rows, value_part, preferred_element_type=jnp.float32)
        key_more = key_step if key_more is None else key_more + key_step
        value_more = value_step if value_more is None else value_more + value_step
    keys = rotate(key_more, positions).astype(jnp.bfloat16)
    values = value_more.astype(jnp.bfloat16)
    block_ids = seq_index * 2 + jnp.arange(2, dtype=jnp.int32)
    query_block = local_rows // block_len
    scale = 1.0 / math.sqrt(head_size)
    scores = jnp.einsum("tgrh,ugh->grtu", queries, keys, preferred_element_type=jnp.float32) * scale
    near_linked = lax.dynamic_slice_in_dim(links[0], seq_index * 2, 2) != block_ids
    same_block = query_block[:, None] == query_block[None, :]
    causal = same_block & (local_rows[None, :] <= local_rows[:, None])
    across = ~same_block & near_linked[query_block][:, None]
    allowed = causal | across
    scores = jnp.where(allowed[None, None], scores, -jnp.inf)
    running_max = jnp.max(scores, axis=-1)
    weights = jnp.exp(scores - running_max[..., None])
    total = jnp.sum(weights, axis=-1)
    accum = jnp.einsum(
        "grtu,ugh->tgrh", weights.astype(jnp.bfloat16), values, preferred_element_type=jnp.float32
    )
    query_pairs = queries.reshape(2, block_len, local_groups, per_group, head_size)
    for section in range(1, lax.axis_size("seq").bit_length()):
        far_keys, far_values = from_partner((keys, values), "seq", section - 1)
        far_keys = far_keys.reshape(2, block_len, local_groups, head_size)
        far_values = far_values.reshape(2, block_len, local_groups, head_size)
        linked = lax.dynamic_slice_in_dim(links[section], seq_index * 2, 2) != block_ids
        offset = jnp.where(linked, 0.0, -1e30).astype(jnp.float32)[query_block]
        far_scores = jnp.einsum(
            "jtgrh,jugh->grjtu", query_pairs, far_keys, preferred_element_type=jnp.float32
        )
        far_scores = (
            far_scores.reshape(local_groups, per_group, row_count, block_len) * scale
            + offset[None, None, :, None]
        )
        new_max = jnp.maximum(running_max, jnp.max(far_scores, axis=-1))
        shrink = jnp.exp(running_max - new_max)
        far_weights = jnp.exp(far_scores - new_max[..., None])
        total = total * shrink + jnp.sum(far_weights, axis=-1)
        paired = far_weights.astype(jnp.bfloat16).reshape(
            local_groups, per_group, 2, block_len, block_len
        )
        far_sum = jnp.einsum(
            "grjtu,jugh->jtgrh", paired, far_values, preferred_element_type=jnp.float32
        )
        far_sum = far_sum.reshape(row_count, local_groups, per_group, head_size)
        accum = accum * jnp.transpose(shrink, (2, 0, 1))[..., None] + far_sum
        running_max = new_max
    attended = (accum / jnp.transpose(total, (2, 0, 1))[..., None]).astype(jnp.bfloat16)
    attended = attended.reshape(row_count, local_groups, per_group * head_size)
    tile_count = lax.axis_size("kvh") * lax.axis_size("sub")
    tile_cols = width // tile_count
    owner_index = lax.axis_index("kvh") * lax.axis_size("sub") + lax.axis_index("sub")
    owned = lax.dynamic_slice_in_dim(normed, owner_index * tile_cols, tile_cols, 1)
    seq_count = lax.axis_size("seq")
    band = width // seq_count
    inverse_count = 1.0 / (row_count * seq_count)
    all_owned = lax.all_gather(owned, "seq", axis=0, tiled=True)
    mine = lax.dynamic_slice_in_dim(normed, seq_index * band, band, 1)
    gram_sum = jnp.einsum("tc,tr->cr", mine, owned, preferred_element_type=jnp.float32)
    for shift in range(1, seq_count):
        target = (seq_index + shift) % seq_count
        outgoing = lax.dynamic_slice_in_dim(normed, target * band, band, 1)
        route = [(j, (j + shift) % seq_count) for j in range(seq_count)]
        incoming = lax.ppermute(outgoing, "seq", route)
        source = (seq_index - shift) % seq_count
        their_owned = lax.dynamic_slice_in_dim(all_owned, source * row_count, row_count, 0)
        gram_sum = gram_sum + jnp.einsum(
            "tc,tr->cr", incoming, their_owned, preferred_element_type=jnp.float32
        )
    gram_tile = gram_sum * inverse_count
    return (attended, gram_tile)


def solution(mesh):
    placed = (
        P(("grp", "seq"), ("kvh", "sub")),
        P(),
        P(None, "kvh", "sub"),
        P("sub", "kvh", None),
        P("sub", "kvh", None),
        P(),
    )
    return jax.shard_map(
        body,
        mesh=mesh,
        in_specs=placed,
        out_specs=(P(("grp", "seq"), "kvh", "sub"), P(("grp", "seq"), ("kvh", "sub"))),
        check_vma=False,
    )
```

```python
import math

import jax
import jax.numpy as jnp
from jax import lax
from jax.sharding import PartitionSpec as P

rope_base = 500000.0


def from_partner(block, axis, bit):
    count = lax.axis_size(axis)
    route = []
    for low in range(count):
        high = low | 1 << bit
        if high != low and high < count:
            route += [(low, high), (high, low)]
    return lax.ppermute(block, axis, route)


def swap_halves(pieces, count, index):
    whole = [None] * count
    whole[0] = pieces
    for shift in range(1, count):
        route = [(j, (j + shift) % count) for j in range(count)]
        whole[shift] = lax.ppermute(pieces, "sub", route)
    return whole


def split_send(blocks, axis, bit):
    count = lax.axis_size("sub")
    index = lax.axis_index("sub")
    share = blocks[0].shape[0] // count
    mine = tuple(lax.dynamic_slice_in_dim(b, index * share, share, 0) for b in blocks)
    got = from_partner(mine, axis, bit)
    whole = swap_halves(got, count, index)
    out = []
    for n, b in enumerate(blocks):
        full = jnp.zeros_like(b)
        for shift in range(count):
            source = (index - shift) % count
            full = lax.dynamic_update_slice_in_dim(full, whole[shift][n], source * share, 0)
        out.append(full)
    return tuple(out)


def rotate(vectors, positions):
    width = vectors.shape[-1]
    half = width // 2
    inverse = jnp.exp(jnp.arange(half, dtype=jnp.float32) * (-2.0 * math.log(rope_base) / width))
    angles = positions.astype(jnp.float32)[:, None] * inverse[None, :]
    shape = (angles.shape[0],) + (1,) * (vectors.ndim - 2) + (half,)
    cosine = jnp.cos(angles).reshape(shape)
    sine = jnp.sin(angles).reshape(shape)
    first = vectors[..., :half]
    second = vectors[..., half:]
    return jnp.concatenate(
        [first * cosine - second * sine, second * cosine + first * sine], axis=-1
    )


def body(tokens, norm_gain, w_query, w_key, w_value, links):
    gathered = lax.all_gather(tokens, ("kvh", "sub"), axis=1, tiled=True)
    widened = gathered.astype(jnp.float32)
    mean_square = jnp.mean(widened * widened, axis=-1, keepdims=True)
    normed = (widened * lax.rsqrt(mean_square + 1e-05) * norm_gain).astype(jnp.bfloat16)
    row_count = normed.shape[0]
    block_len = row_count // 2
    width = normed.shape[1]
    seq_index = lax.axis_index("seq")
    local_rows = jnp.arange(row_count, dtype=jnp.int32)
    positions = seq_index * row_count + local_rows
    head_size = w_key.shape[2]
    local_groups = w_key.shape[1]
    per_group = w_query.shape[2] // head_size
    queries = jnp.einsum("td,dgc->tgc", normed, w_query, preferred_element_type=jnp.float32)
    queries = rotate(
        queries.reshape(row_count, local_groups, per_group, head_size), positions
    ).astype(jnp.bfloat16)
    sub_count = lax.axis_size("sub")
    sub_index = lax.axis_index("sub")
    row_share = w_key.shape[0]
    key_more = None
    value_more = None
    for shift in range(sub_count):
        if shift == 0:
            key_part, value_part = w_key, w_value
        else:
            route = [(j, (j + shift) % sub_count) for j in range(sub_count)]
            key_part, value_part = lax.ppermute((w_key, w_value), "sub", route)
        source = (sub_index - shift) % sub_count
        rows = lax.dynamic_slice_in_dim(normed, source * row_share, row_share, 1)
        key_step = jnp.einsum("td,dgh->tgh", rows, key_part, preferred_element_type=jnp.float32)
        value_step = jnp.einsum("td,dgh->tgh", rows, value_part, preferred_element_type=jnp.float32)
        key_more = key_step if key_more is None else key_more + key_step
        value_more = value_step if value_more is None else value_more + value_step
    keys = rotate(key_more, positions).astype(jnp.bfloat16)
    values = value_more.astype(jnp.bfloat16)
    block_ids = seq_index * 2 + jnp.arange(2, dtype=jnp.int32)
    query_block = local_rows // block_len
    scale = 1.0 / math.sqrt(head_size)
    scores = jnp.einsum("tgrh,ugh->grtu", queries, keys, preferred_element_type=jnp.float32) * scale
    near_linked = lax.dynamic_slice_in_dim(links[0], seq_index * 2, 2) != block_ids
    same_block = query_block[:, None] == query_block[None, :]
    causal = same_block & (local_rows[None, :] <= local_rows[:, None])
    across = ~same_block & near_linked[query_block][:, None]
    allowed = causal | across
    scores = jnp.where(allowed[None, None], scores, -jnp.inf)
    running_max = jnp.max(scores, axis=-1)
    weights = jnp.exp(scores - running_max[..., None])
    total = jnp.sum(weights, axis=-1)
    accum = jnp.einsum(
        "grtu,ugh->tgrh", weights.astype(jnp.bfloat16), values, preferred_element_type=jnp.float32
    )
    query_pairs = queries.reshape(2, block_len, local_groups, per_group, head_size)
    for section in range(1, lax.axis_size("seq").bit_length()):
        far_keys, far_values = split_send((keys, values), "seq", section - 1)
        far_keys = far_keys.reshape(2, block_len, local_groups, head_size)
        far_values = far_values.reshape(2, block_len, local_groups, head_size)
        linked = lax.dynamic_slice_in_dim(links[section], seq_index * 2, 2) != block_ids
        offset = jnp.where(linked, 0.0, -1e30).astype(jnp.float32)[query_block]
        far_scores = jnp.einsum(
            "jtgrh,jugh->grjtu", query_pairs, far_keys, preferred_element_type=jnp.float32
        )
        far_scores = (
            far_scores.reshape(local_groups, per_group, row_count, block_len) * scale
            + offset[None, None, :, None]
        )
        new_max = jnp.maximum(running_max, jnp.max(far_scores, axis=-1))
        shrink = jnp.exp(running_max - new_max)
        far_weights = jnp.exp(far_scores - new_max[..., None])
        total = total * shrink + jnp.sum(far_weights, axis=-1)
        paired = far_weights.astype(jnp.bfloat16).reshape(
            local_groups, per_group, 2, block_len, block_len
        )
        far_sum = jnp.einsum(
            "grjtu,jugh->jtgrh", paired, far_values, preferred_element_type=jnp.float32
        )
        far_sum = far_sum.reshape(row_count, local_groups, per_group, head_size)
        accum = accum * jnp.transpose(shrink, (2, 0, 1))[..., None] + far_sum
        running_max = new_max
    attended = (accum / jnp.transpose(total, (2, 0, 1))[..., None]).astype(jnp.bfloat16)
    attended = attended.reshape(row_count, local_groups, per_group * head_size)
    tile_count = lax.axis_size("kvh") * lax.axis_size("sub")
    tile_cols = width // tile_count
    owner_index = lax.axis_index("kvh") * lax.axis_size("sub") + lax.axis_index("sub")
    owned = lax.dynamic_slice_in_dim(normed, owner_index * tile_cols, tile_cols, 1)
    seq_count = lax.axis_size("seq")
    band = width // seq_count
    inverse_count = 1.0 / (row_count * seq_count)
    sub_count = lax.axis_size("sub")
    share = row_count // sub_count
    mine = lax.dynamic_slice_in_dim(normed, seq_index * band, band, 1)
    gram_sum = jnp.einsum("tc,tr->cr", mine, owned, preferred_element_type=jnp.float32)
    up_route = [(j, j + 1) for j in range(seq_count - 1)]
    down_route = [(j + 1, j) for j in range(seq_count - 1)]
    from_below = owned
    from_above = owned
    for step in range(1, seq_count):
        from_below = lax.ppermute(from_below, "seq", up_route)
        from_above = lax.ppermute(from_above, "seq", down_route)
        for offset, their_owned in ((-step, from_below), (step, from_above)):
            target = seq_index - offset
            outgoing = lax.dynamic_slice_in_dim(normed, sub_index * share, share, 0)
            outgoing = lax.dynamic_slice_in_dim(outgoing, jnp.clip(target, 0, seq_count - 1) * band, band, 1)
            route = [(j, j - offset) for j in range(seq_count) if 0 <= j - offset < seq_count]
            incoming = lax.ppermute(outgoing, "seq", route)
            halves = swap_halves(incoming, sub_count, sub_index)
            for shift in range(sub_count):
                source = (sub_index - shift) % sub_count
                their_rows = lax.dynamic_slice_in_dim(their_owned, source * share, share, 0)
                gram_sum = gram_sum + jnp.einsum(
                    "tc,tr->cr", halves[shift], their_rows, preferred_element_type=jnp.float32
                )
    gram_tile = gram_sum * inverse_count
    return (attended, gram_tile)


def solution(mesh):
    placed = (
        P(("grp", "seq"), ("kvh", "sub")),
        P(),
        P(None, "kvh", "sub"),
        P("sub", "kvh", None),
        P("sub", "kvh", None),
        P(),
    )
    return jax.shard_map(
        body,
        mesh=mesh,
        in_specs=placed,
        out_specs=(P(("grp", "seq"), "kvh", "sub"), P(("grp", "seq"), ("kvh", "sub"))),
        check_vma=False,
    )
```

```python
import math

import jax
import jax.numpy as jnp
from jax import lax
from jax.sharding import PartitionSpec as P

rope_base = 500000.0


def from_partner(block, axis, bit):
    count = lax.axis_size(axis)
    route = []
    for low in range(count):
        high = low | 1 << bit
        if high != low and high < count:
            route += [(low, high), (high, low)]
    return lax.ppermute(block, axis, route)


def swap_halves(pieces, count, index):
    whole = [None] * count
    whole[0] = pieces
    for shift in range(1, count):
        route = [(j, (j + shift) % count) for j in range(count)]
        whole[shift] = lax.ppermute(pieces, "sub", route)
    return whole


def split_send(blocks, axis, bit):
    count = lax.axis_size("sub")
    index = lax.axis_index("sub")
    share = blocks[0].shape[0] // count
    mine = tuple(lax.dynamic_slice_in_dim(b, index * share, share, 0) for b in blocks)
    got = from_partner(mine, axis, bit)
    whole = swap_halves(got, count, index)
    out = []
    for n, b in enumerate(blocks):
        full = jnp.zeros_like(b)
        for shift in range(count):
            source = (index - shift) % count
            full = lax.dynamic_update_slice_in_dim(full, whole[shift][n], source * share, 0)
        out.append(full)
    return tuple(out)


def rotate(vectors, positions):
    width = vectors.shape[-1]
    half = width // 2
    inverse = jnp.exp(jnp.arange(half, dtype=jnp.float32) * (-2.0 * math.log(rope_base) / width))
    angles = positions.astype(jnp.float32)[:, None] * inverse[None, :]
    shape = (angles.shape[0],) + (1,) * (vectors.ndim - 2) + (half,)
    cosine = jnp.cos(angles).reshape(shape)
    sine = jnp.sin(angles).reshape(shape)
    first = vectors[..., :half]
    second = vectors[..., half:]
    return jnp.concatenate(
        [first * cosine - second * sine, second * cosine + first * sine], axis=-1
    )


def body(tokens, norm_gain, w_query, w_key, w_value, links):
    gathered = lax.all_gather(tokens, ("kvh", "sub"), axis=1, tiled=True)
    widened = gathered.astype(jnp.float32)
    mean_square = jnp.mean(widened * widened, axis=-1, keepdims=True)
    normed = (widened * lax.rsqrt(mean_square + 1e-05) * norm_gain).astype(jnp.bfloat16)
    row_count = normed.shape[0]
    block_len = row_count // 2
    width = normed.shape[1]
    seq_index = lax.axis_index("seq")
    local_rows = jnp.arange(row_count, dtype=jnp.int32)
    positions = seq_index * row_count + local_rows
    head_size = w_key.shape[2]
    local_groups = w_key.shape[1]
    per_group = w_query.shape[2] // head_size
    queries = jnp.einsum("td,dgc->tgc", normed, w_query, preferred_element_type=jnp.float32)
    queries = rotate(
        queries.reshape(row_count, local_groups, per_group, head_size), positions
    ).astype(jnp.bfloat16)
    sub_count = lax.axis_size("sub")
    sub_index = lax.axis_index("sub")
    row_share = w_key.shape[0]
    key_more = None
    value_more = None
    for shift in range(sub_count):
        if shift == 0:
            key_part, value_part = w_key, w_value
        else:
            route = [(j, (j + shift) % sub_count) for j in range(sub_count)]
            key_part, value_part = lax.ppermute((w_key, w_value), "sub", route)
        source = (sub_index - shift) % sub_count
        rows = lax.dynamic_slice_in_dim(normed, source * row_share, row_share, 1)
        key_step = jnp.einsum("td,dgh->tgh", rows, key_part, preferred_element_type=jnp.float32)
        value_step = jnp.einsum("td,dgh->tgh", rows, value_part, preferred_element_type=jnp.float32)
        key_more = key_step if key_more is None else key_more + key_step
        value_more = value_step if value_more is None else value_more + value_step
    keys = rotate(key_more, positions).astype(jnp.bfloat16)
    values = value_more.astype(jnp.bfloat16)
    block_ids = seq_index * 2 + jnp.arange(2, dtype=jnp.int32)
    query_block = local_rows // block_len
    scale = 1.0 / math.sqrt(head_size)
    scores = jnp.einsum("tgrh,ugh->grtu", queries, keys, preferred_element_type=jnp.float32) * scale
    near_linked = lax.dynamic_slice_in_dim(links[0], seq_index * 2, 2) != block_ids
    same_block = query_block[:, None] == query_block[None, :]
    causal = same_block & (local_rows[None, :] <= local_rows[:, None])
    across = ~same_block & near_linked[query_block][:, None]
    allowed = causal | across
    scores = jnp.where(allowed[None, None], scores, -jnp.inf)
    running_max = jnp.max(scores, axis=-1)
    weights = jnp.exp(scores - running_max[..., None])
    total = jnp.sum(weights, axis=-1)
    accum = jnp.einsum(
        "grtu,ugh->tgrh", weights.astype(jnp.bfloat16), values, preferred_element_type=jnp.float32
    )
    query_pairs = queries.reshape(2, block_len, local_groups, per_group, head_size)
    for section in range(1, lax.axis_size("seq").bit_length()):
        far_keys, far_values = split_send((keys, values), "seq", section - 1)
        far_keys = far_keys.reshape(2, block_len, local_groups, head_size)
        far_values = far_values.reshape(2, block_len, local_groups, head_size)
        linked = lax.dynamic_slice_in_dim(links[section], seq_index * 2, 2) != block_ids
        offset = jnp.where(linked, 0.0, -1e30).astype(jnp.float32)[query_block]
        far_scores = jnp.einsum(
            "jtgrh,jugh->grjtu", query_pairs, far_keys, preferred_element_type=jnp.float32
        )
        far_scores = (
            far_scores.reshape(local_groups, per_group, row_count, block_len) * scale
            + offset[None, None, :, None]
        )
        new_max = jnp.maximum(running_max, jnp.max(far_scores, axis=-1))
        shrink = jnp.exp(running_max - new_max)
        far_weights = jnp.exp(far_scores - new_max[..., None])
        total = total * shrink + jnp.sum(far_weights, axis=-1)
        paired = far_weights.astype(jnp.bfloat16).reshape(
            local_groups, per_group, 2, block_len, block_len
        )
        far_sum = jnp.einsum(
            "grjtu,jugh->jtgrh", paired, far_values, preferred_element_type=jnp.float32
        )
        far_sum = far_sum.reshape(row_count, local_groups, per_group, head_size)
        accum = accum * jnp.transpose(shrink, (2, 0, 1))[..., None] + far_sum
        running_max = new_max
    attended = (accum / jnp.transpose(total, (2, 0, 1))[..., None]).astype(jnp.bfloat16)
    attended = attended.reshape(row_count, local_groups, per_group * head_size)
    tile_count = lax.axis_size("kvh") * lax.axis_size("sub")
    tile_cols = width // tile_count
    owner_index = lax.axis_index("kvh") * lax.axis_size("sub") + lax.axis_index("sub")
    owned = lax.dynamic_slice_in_dim(normed, owner_index * tile_cols, tile_cols, 1)
    seq_count = lax.axis_size("seq")
    band = width // seq_count
    inverse_count = 1.0 / (row_count * seq_count)
    partial = jnp.einsum("tc,tr->cr", normed, owned, preferred_element_type=jnp.float32)

    def piece(dest):
        dest = jnp.clip(dest, 0, seq_count - 1)
        return lax.dynamic_slice_in_dim(partial, dest * band, band, 0)

    from_left = jnp.zeros((band, tile_cols), jnp.bfloat16)
    from_right = jnp.zeros((band, tile_cols), jnp.bfloat16)
    for step in range(1, seq_count):
        up = piece(seq_index + seq_count - step) + from_left.astype(jnp.float32)
        down = piece(seq_index - seq_count + step) + from_right.astype(jnp.float32)
        up_route = [(c, c + 1) for c in range(step) if c + 1 < seq_count]
        down_route = [(c, c - 1) for c in range(seq_count - step, seq_count) if c >= 1]
        from_left = lax.ppermute(up.astype(jnp.bfloat16), "seq", up_route)
        from_right = lax.ppermute(down.astype(jnp.bfloat16), "seq", down_route)
    gram_sum = (
        piece(seq_index) + from_left.astype(jnp.float32) + from_right.astype(jnp.float32)
    )
    gram_tile = gram_sum * inverse_count
    return (attended, gram_tile)


def solution(mesh):
    placed = (
        P(("grp", "seq"), ("kvh", "sub")),
        P(),
        P(None, "kvh", "sub"),
        P("sub", "kvh", None),
        P("sub", "kvh", None),
        P(),
    )
    return jax.shard_map(
        body,
        mesh=mesh,
        in_specs=placed,
        out_specs=(P(("grp", "seq"), "kvh", "sub"), P(("grp", "seq"), ("kvh", "sub"))),
        check_vma=False,
    )
```

```python
import math

import jax
import jax.numpy as jnp
from jax import lax
from jax.sharding import PartitionSpec as P

rope_base = 500000.0


def from_partner(block, axis, bit):
    count = lax.axis_size(axis)
    route = []
    for low in range(count):
        high = low | 1 << bit
        if high != low and high < count:
            route += [(low, high), (high, low)]
    return lax.ppermute(block, axis, route)


def swap_halves(pieces, count, index):
    whole = [None] * count
    whole[0] = pieces
    for shift in range(1, count):
        route = [(j, (j + shift) % count) for j in range(count)]
        whole[shift] = lax.ppermute(pieces, "sub", route)
    return whole


def split_send(blocks, axis, bit):
    count = lax.axis_size("sub")
    index = lax.axis_index("sub")
    share = blocks[0].shape[0] // count
    mine = tuple(lax.dynamic_slice_in_dim(b, index * share, share, 0) for b in blocks)
    got = from_partner(mine, axis, bit)
    whole = swap_halves(got, count, index)
    out = []
    for n, b in enumerate(blocks):
        full = jnp.zeros_like(b)
        for shift in range(count):
            source = (index - shift) % count
            full = lax.dynamic_update_slice_in_dim(full, whole[shift][n], source * share, 0)
        out.append(full)
    return tuple(out)


def rotate(vectors, positions):
    width = vectors.shape[-1]
    half = width // 2
    inverse = jnp.exp(jnp.arange(half, dtype=jnp.float32) * (-2.0 * math.log(rope_base) / width))
    angles = positions.astype(jnp.float32)[:, None] * inverse[None, :]
    shape = (angles.shape[0],) + (1,) * (vectors.ndim - 2) + (half,)
    cosine = jnp.cos(angles).reshape(shape)
    sine = jnp.sin(angles).reshape(shape)
    first = vectors[..., :half]
    second = vectors[..., half:]
    return jnp.concatenate(
        [first * cosine - second * sine, second * cosine + first * sine], axis=-1
    )


def body(tokens, norm_gain, w_query, w_key, w_value, links):
    gathered = lax.all_gather(tokens, ("kvh", "sub"), axis=1, tiled=True)
    widened = gathered.astype(jnp.float32)
    mean_square = jnp.mean(widened * widened, axis=-1, keepdims=True)
    normed = (widened * lax.rsqrt(mean_square + 1e-05) * norm_gain).astype(jnp.bfloat16)
    row_count = normed.shape[0]
    block_len = row_count // 2
    width = normed.shape[1]
    seq_index = lax.axis_index("seq")
    local_rows = jnp.arange(row_count, dtype=jnp.int32)
    positions = seq_index * row_count + local_rows
    head_size = w_key.shape[2]
    local_groups = w_key.shape[1]
    per_group = w_query.shape[2] // head_size
    queries = jnp.einsum("td,dgc->tgc", normed, w_query, preferred_element_type=jnp.float32)
    queries = rotate(
        queries.reshape(row_count, local_groups, per_group, head_size), positions
    ).astype(jnp.bfloat16)
    sub_count = lax.axis_size("sub")
    sub_index = lax.axis_index("sub")
    row_share = w_key.shape[0]
    key_more = None
    value_more = None
    for shift in range(sub_count):
        if shift == 0:
            key_part, value_part = w_key, w_value
        else:
            route = [(j, (j + shift) % sub_count) for j in range(sub_count)]
            key_part, value_part = lax.ppermute((w_key, w_value), "sub", route)
        source = (sub_index - shift) % sub_count
        rows = lax.dynamic_slice_in_dim(normed, source * row_share, row_share, 1)
        key_step = jnp.einsum("td,dgh->tgh", rows, key_part, preferred_element_type=jnp.float32)
        value_step = jnp.einsum("td,dgh->tgh", rows, value_part, preferred_element_type=jnp.float32)
        key_more = key_step if key_more is None else key_more + key_step
        value_more = value_step if value_more is None else value_more + value_step
    keys = rotate(key_more, positions).astype(jnp.bfloat16)
    values = value_more.astype(jnp.bfloat16)
    block_ids = seq_index * 2 + jnp.arange(2, dtype=jnp.int32)
    query_block = local_rows // block_len
    scale = 1.0 / math.sqrt(head_size)
    scores = jnp.einsum("tgrh,ugh->grtu", queries, keys, preferred_element_type=jnp.float32) * scale
    near_linked = lax.dynamic_slice_in_dim(links[0], seq_index * 2, 2) != block_ids
    same_block = query_block[:, None] == query_block[None, :]
    causal = same_block & (local_rows[None, :] <= local_rows[:, None])
    across = ~same_block & near_linked[query_block][:, None]
    allowed = causal | across
    scores = jnp.where(allowed[None, None], scores, -jnp.inf)
    running_max = jnp.max(scores, axis=-1)
    weights = jnp.exp(scores - running_max[..., None])
    total = jnp.sum(weights, axis=-1)
    accum = jnp.einsum(
        "grtu,ugh->tgrh", weights.astype(jnp.bfloat16), values, preferred_element_type=jnp.float32
    )
    query_pairs = queries.reshape(2, block_len, local_groups, per_group, head_size)
    for section in range(1, lax.axis_size("seq").bit_length()):
        far_keys, far_values = split_send((keys, values), "seq", section - 1)
        far_keys = far_keys.reshape(2, block_len, local_groups, head_size)
        far_values = far_values.reshape(2, block_len, local_groups, head_size)
        linked = lax.dynamic_slice_in_dim(links[section], seq_index * 2, 2) != block_ids
        offset = jnp.where(linked, 0.0, -1e30).astype(jnp.float32)[query_block]
        far_scores = jnp.einsum(
            "jtgrh,jugh->grjtu", query_pairs, far_keys, preferred_element_type=jnp.float32
        )
        far_scores = (
            far_scores.reshape(local_groups, per_group, row_count, block_len) * scale
            + offset[None, None, :, None]
        )
        new_max = jnp.maximum(running_max, jnp.max(far_scores, axis=-1))
        shrink = jnp.exp(running_max - new_max)
        far_weights = jnp.exp(far_scores - new_max[..., None])
        total = total * shrink + jnp.sum(far_weights, axis=-1)
        paired = far_weights.astype(jnp.bfloat16).reshape(
            local_groups, per_group, 2, block_len, block_len
        )
        far_sum = jnp.einsum(
            "grjtu,jugh->jtgrh", paired, far_values, preferred_element_type=jnp.float32
        )
        far_sum = far_sum.reshape(row_count, local_groups, per_group, head_size)
        accum = accum * jnp.transpose(shrink, (2, 0, 1))[..., None] + far_sum
        running_max = new_max
    attended = (accum / jnp.transpose(total, (2, 0, 1))[..., None]).astype(jnp.bfloat16)
    attended = attended.reshape(row_count, local_groups, per_group * head_size)
    tile_count = lax.axis_size("kvh") * lax.axis_size("sub")
    tile_cols = width // tile_count
    owner_index = lax.axis_index("kvh") * lax.axis_size("sub") + lax.axis_index("sub")
    owned = lax.dynamic_slice_in_dim(normed, owner_index * tile_cols, tile_cols, 1)
    seq_count = lax.axis_size("seq")
    inverse_count = 1.0 / (row_count * seq_count)
    gram_sum = lax.psum_scatter(
        (
            jnp.einsum("tc,tr->cr", normed, owned, preferred_element_type=jnp.float32)
            * inverse_count
        ).astype(jnp.bfloat16),
        "seq",
        scatter_dimension=0,
        tiled=True,
    ).astype(jnp.float32)
    gram_tile = gram_sum
    return (attended, gram_tile)


def solution(mesh):
    placed = (
        P(("grp", "seq"), ("kvh", "sub")),
        P(),
        P(None, "kvh", "sub"),
        P("sub", "kvh", None),
        P("sub", "kvh", None),
        P(),
    )
    return jax.shard_map(
        body,
        mesh=mesh,
        in_specs=placed,
        out_specs=(P(("grp", "seq"), "kvh", "sub"), P(("grp", "seq"), ("kvh", "sub"))),
        check_vma=False,
    )
```

```python
import math

import jax
import jax.numpy as jnp
from jax import lax
from jax.sharding import PartitionSpec as P

rope_base = 500000.0


def from_partner(block, axis, bit):
    count = lax.axis_size(axis)
    route = []
    for low in range(count):
        high = low | 1 << bit
        if high != low and high < count:
            route += [(low, high), (high, low)]
    return lax.ppermute(block, axis, route)


def swap_halves(pieces, count, index):
    whole = [None] * count
    whole[0] = pieces
    for shift in range(1, count):
        route = [(j, (j + shift) % count) for j in range(count)]
        whole[shift] = lax.ppermute(pieces, "sub", route)
    return whole


def split_send(blocks, axis, bit):
    count = lax.axis_size("sub")
    index = lax.axis_index("sub")
    share = blocks[0].shape[0] // count
    mine = tuple(lax.dynamic_slice_in_dim(b, index * share, share, 0) for b in blocks)
    got = from_partner(mine, axis, bit)
    whole = swap_halves(got, count, index)
    out = []
    for n, b in enumerate(blocks):
        full = jnp.zeros_like(b)
        for shift in range(count):
            source = (index - shift) % count
            full = lax.dynamic_update_slice_in_dim(full, whole[shift][n], source * share, 0)
        out.append(full)
    return tuple(out)


def rotate(vectors, positions):
    width = vectors.shape[-1]
    half = width // 2
    inverse = jnp.exp(jnp.arange(half, dtype=jnp.float32) * (-2.0 * math.log(rope_base) / width))
    angles = positions.astype(jnp.float32)[:, None] * inverse[None, :]
    shape = (angles.shape[0],) + (1,) * (vectors.ndim - 2) + (half,)
    cosine = jnp.cos(angles).reshape(shape)
    sine = jnp.sin(angles).reshape(shape)
    first = vectors[..., :half]
    second = vectors[..., half:]
    return jnp.concatenate(
        [first * cosine - second * sine, second * cosine + first * sine], axis=-1
    )


def body(tokens, norm_gain, w_query, w_key, w_value, links):
    lanes = lax.all_gather(tokens, "kvh", axis=0, tiled=False)
    sub_total = lax.axis_size("sub")
    lane_index = lax.axis_index("sub")
    copies = swap_halves(lanes, sub_total, lane_index)
    ordered = [
        lax.select_n((lane_index - lane) % sub_total, *copies) for lane in range(sub_total)
    ]
    stacked = jnp.stack(ordered, axis=1)
    gathered = jnp.transpose(stacked, (2, 0, 1, 3)).reshape(tokens.shape[0], -1)
    widened = gathered.astype(jnp.float32)
    mean_square = jnp.mean(widened * widened, axis=-1, keepdims=True)
    normed = (widened * lax.rsqrt(mean_square + 1e-05) * norm_gain).astype(jnp.bfloat16)
    row_count = normed.shape[0]
    block_len = row_count // 2
    width = normed.shape[1]
    seq_index = lax.axis_index("seq")
    local_rows = jnp.arange(row_count, dtype=jnp.int32)
    positions = seq_index * row_count + local_rows
    head_size = w_key.shape[2]
    local_groups = w_key.shape[1]
    per_group = w_query.shape[2] // head_size
    queries = jnp.einsum("td,dgc->tgc", normed, w_query, preferred_element_type=jnp.float32)
    queries = rotate(
        queries.reshape(row_count, local_groups, per_group, head_size), positions
    ).astype(jnp.bfloat16)
    sub_count = lax.axis_size("sub")
    sub_index = lax.axis_index("sub")
    row_share = w_key.shape[0]
    key_more = None
    value_more = None
    for shift in range(sub_count):
        if shift == 0:
            key_part, value_part = w_key, w_value
        else:
            route = [(j, (j + shift) % sub_count) for j in range(sub_count)]
            key_part, value_part = lax.ppermute((w_key, w_value), "sub", route)
        source = (sub_index - shift) % sub_count
        rows = lax.dynamic_slice_in_dim(normed, source * row_share, row_share, 1)
        key_step = jnp.einsum("td,dgh->tgh", rows, key_part, preferred_element_type=jnp.float32)
        value_step = jnp.einsum("td,dgh->tgh", rows, value_part, preferred_element_type=jnp.float32)
        key_more = key_step if key_more is None else key_more + key_step
        value_more = value_step if value_more is None else value_more + value_step
    keys = rotate(key_more, positions).astype(jnp.bfloat16)
    values = value_more.astype(jnp.bfloat16)
    block_ids = seq_index * 2 + jnp.arange(2, dtype=jnp.int32)
    query_block = local_rows // block_len
    scale = 1.0 / math.sqrt(head_size)
    scores = jnp.einsum("tgrh,ugh->grtu", queries, keys, preferred_element_type=jnp.float32) * scale
    near_linked = lax.dynamic_slice_in_dim(links[0], seq_index * 2, 2) != block_ids
    same_block = query_block[:, None] == query_block[None, :]
    causal = same_block & (local_rows[None, :] <= local_rows[:, None])
    across = ~same_block & near_linked[query_block][:, None]
    allowed = causal | across
    scores = jnp.where(allowed[None, None], scores, -jnp.inf)
    running_max = jnp.max(scores, axis=-1)
    weights = jnp.exp(scores - running_max[..., None])
    total = jnp.sum(weights, axis=-1)
    accum = jnp.einsum(
        "grtu,ugh->tgrh", weights.astype(jnp.bfloat16), values, preferred_element_type=jnp.float32
    )
    query_pairs = queries.reshape(2, block_len, local_groups, per_group, head_size)
    for section in range(1, lax.axis_size("seq").bit_length()):
        far_keys, far_values = split_send((keys, values), "seq", section - 1)
        far_keys = far_keys.reshape(2, block_len, local_groups, head_size)
        far_values = far_values.reshape(2, block_len, local_groups, head_size)
        linked = lax.dynamic_slice_in_dim(links[section], seq_index * 2, 2) != block_ids
        offset = jnp.where(linked, 0.0, -1e30).astype(jnp.float32)[query_block]
        far_scores = jnp.einsum(
            "jtgrh,jugh->grjtu", query_pairs, far_keys, preferred_element_type=jnp.float32
        )
        far_scores = (
            far_scores.reshape(local_groups, per_group, row_count, block_len) * scale
            + offset[None, None, :, None]
        )
        new_max = jnp.maximum(running_max, jnp.max(far_scores, axis=-1))
        shrink = jnp.exp(running_max - new_max)
        far_weights = jnp.exp(far_scores - new_max[..., None])
        total = total * shrink + jnp.sum(far_weights, axis=-1)
        paired = far_weights.astype(jnp.bfloat16).reshape(
            local_groups, per_group, 2, block_len, block_len
        )
        far_sum = jnp.einsum(
            "grjtu,jugh->jtgrh", paired, far_values, preferred_element_type=jnp.float32
        )
        far_sum = far_sum.reshape(row_count, local_groups, per_group, head_size)
        accum = accum * jnp.transpose(shrink, (2, 0, 1))[..., None] + far_sum
        running_max = new_max
    attended = (accum / jnp.transpose(total, (2, 0, 1))[..., None]).astype(jnp.bfloat16)
    attended = attended.reshape(row_count, local_groups, per_group * head_size)
    tile_count = lax.axis_size("kvh") * lax.axis_size("sub")
    tile_cols = width // tile_count
    owner_index = lax.axis_index("kvh") * lax.axis_size("sub") + lax.axis_index("sub")
    owned = lax.dynamic_slice_in_dim(normed, owner_index * tile_cols, tile_cols, 1)
    seq_count = lax.axis_size("seq")
    inverse_count = 1.0 / (row_count * seq_count)
    gram_sum = lax.psum_scatter(
        (
            jnp.einsum("tc,tr->cr", normed, owned, preferred_element_type=jnp.float32)
            * inverse_count
        ).astype(jnp.bfloat16),
        "seq",
        scatter_dimension=0,
        tiled=True,
    ).astype(jnp.float32)
    gram_tile = gram_sum
    return (attended, gram_tile)


def solution(mesh):
    placed = (
        P(("grp", "seq"), ("kvh", "sub")),
        P(),
        P(None, "kvh", "sub"),
        P("sub", "kvh", None),
        P("sub", "kvh", None),
        P(),
    )
    return jax.shard_map(
        body,
        mesh=mesh,
        in_specs=placed,
        out_specs=(P(("grp", "seq"), "kvh", "sub"), P(("grp", "seq"), ("kvh", "sub"))),
        check_vma=False,
    )
```

```python
import math

import jax
import jax.numpy as jnp
from jax import lax
from jax.sharding import PartitionSpec as P

rope_base = 500000.0


def from_partner(block, axis, bit):
    count = lax.axis_size(axis)
    route = []
    for low in range(count):
        high = low | 1 << bit
        if high != low and high < count:
            route += [(low, high), (high, low)]
    return lax.ppermute(block, axis, route)


def swap_halves(pieces, count, index):
    whole = [None] * count
    whole[0] = pieces
    for shift in range(1, count):
        route = [(j, (j + shift) % count) for j in range(count)]
        whole[shift] = lax.ppermute(pieces, "sub", route)
    return whole


def split_send(blocks, axis, bit):
    count = lax.axis_size("sub")
    index = lax.axis_index("sub")
    share = blocks[0].shape[0] // count
    mine = tuple(lax.dynamic_slice_in_dim(b, index * share, share, 0) for b in blocks)
    got = from_partner(mine, axis, bit)
    whole = swap_halves(got, count, index)
    out = []
    for n, b in enumerate(blocks):
        full = jnp.zeros_like(b)
        for shift in range(count):
            source = (index - shift) % count
            full = lax.dynamic_update_slice_in_dim(full, whole[shift][n], source * share, 0)
        out.append(full)
    return tuple(out)


def rotate(vectors, positions):
    width = vectors.shape[-1]
    half = width // 2
    inverse = jnp.exp(jnp.arange(half, dtype=jnp.float32) * (-2.0 * math.log(rope_base) / width))
    angles = positions.astype(jnp.float32)[:, None] * inverse[None, :]
    shape = (angles.shape[0],) + (1,) * (vectors.ndim - 2) + (half,)
    cosine = jnp.cos(angles).reshape(shape)
    sine = jnp.sin(angles).reshape(shape)
    first = vectors[..., :half]
    second = vectors[..., half:]
    return jnp.concatenate(
        [first * cosine - second * sine, second * cosine + first * sine], axis=-1
    )


def body(tokens, norm_gain, w_query, w_key, w_value, links):
    kvh_total = lax.axis_size("kvh")
    kvh_at = lax.axis_index("kvh")
    sub_total = lax.axis_size("sub")
    lane_index = lax.axis_index("sub")
    across = [tokens]
    for shift in range(1, kvh_total):
        route = [(j, (j + shift) % kvh_total) for j in range(kvh_total)]
        across.append(lax.ppermute(tokens, "kvh", route))
    pieces = []
    for shift in range(kvh_total):
        pieces.extend(swap_halves(across[shift], sub_total, lane_index))
    blocks = []
    for owner_kvh in range(kvh_total):
        for owner_sub in range(sub_total):
            pick = ((kvh_at - owner_kvh) % kvh_total) * sub_total + (lane_index - owner_sub) % sub_total
            blocks.append(lax.select_n(pick, *pieces))
    gathered = jnp.concatenate(blocks, axis=1)
    widened = gathered.astype(jnp.float32)
    mean_square = jnp.mean(widened * widened, axis=-1, keepdims=True)
    normed = (widened * lax.rsqrt(mean_square + 1e-05) * norm_gain).astype(jnp.bfloat16)
    row_count = normed.shape[0]
    block_len = row_count // 2
    width = normed.shape[1]
    seq_index = lax.axis_index("seq")
    local_rows = jnp.arange(row_count, dtype=jnp.int32)
    positions = seq_index * row_count + local_rows
    head_size = w_key.shape[2]
    local_groups = w_key.shape[1]
    per_group = w_query.shape[2] // head_size
    queries = jnp.einsum("td,dgc->tgc", normed, w_query, preferred_element_type=jnp.float32)
    queries = rotate(
        queries.reshape(row_count, local_groups, per_group, head_size), positions
    ).astype(jnp.bfloat16)
    sub_count = lax.axis_size("sub")
    sub_index = lax.axis_index("sub")
    row_share = w_key.shape[0]
    key_more = None
    value_more = None
    for shift in range(sub_count):
        if shift == 0:
            key_part, value_part = w_key, w_value
        else:
            route = [(j, (j + shift) % sub_count) for j in range(sub_count)]
            key_part, value_part = lax.ppermute((w_key, w_value), "sub", route)
        source = (sub_index - shift) % sub_count
        rows = lax.dynamic_slice_in_dim(normed, source * row_share, row_share, 1)
        key_step = jnp.einsum("td,dgh->tgh", rows, key_part, preferred_element_type=jnp.float32)
        value_step = jnp.einsum("td,dgh->tgh", rows, value_part, preferred_element_type=jnp.float32)
        key_more = key_step if key_more is None else key_more + key_step
        value_more = value_step if value_more is None else value_more + value_step
    keys = rotate(key_more, positions).astype(jnp.bfloat16)
    values = value_more.astype(jnp.bfloat16)
    block_ids = seq_index * 2 + jnp.arange(2, dtype=jnp.int32)
    query_block = local_rows // block_len
    scale = 1.0 / math.sqrt(head_size)
    scores = jnp.einsum("tgrh,ugh->grtu", queries, keys, preferred_element_type=jnp.float32) * scale
    near_linked = lax.dynamic_slice_in_dim(links[0], seq_index * 2, 2) != block_ids
    same_block = query_block[:, None] == query_block[None, :]
    causal = same_block & (local_rows[None, :] <= local_rows[:, None])
    across = ~same_block & near_linked[query_block][:, None]
    allowed = causal | across
    scores = jnp.where(allowed[None, None], scores, -jnp.inf)
    running_max = jnp.max(scores, axis=-1)
    weights = jnp.exp(scores - running_max[..., None])
    total = jnp.sum(weights, axis=-1)
    accum = jnp.einsum(
        "grtu,ugh->tgrh", weights.astype(jnp.bfloat16), values, preferred_element_type=jnp.float32
    )
    query_pairs = queries.reshape(2, block_len, local_groups, per_group, head_size)
    for section in range(1, lax.axis_size("seq").bit_length()):
        far_keys, far_values = split_send((keys, values), "seq", section - 1)
        far_keys = far_keys.reshape(2, block_len, local_groups, head_size)
        far_values = far_values.reshape(2, block_len, local_groups, head_size)
        linked = lax.dynamic_slice_in_dim(links[section], seq_index * 2, 2) != block_ids
        offset = jnp.where(linked, 0.0, -1e30).astype(jnp.float32)[query_block]
        far_scores = jnp.einsum(
            "jtgrh,jugh->grjtu", query_pairs, far_keys, preferred_element_type=jnp.float32
        )
        far_scores = (
            far_scores.reshape(local_groups, per_group, row_count, block_len) * scale
            + offset[None, None, :, None]
        )
        new_max = jnp.maximum(running_max, jnp.max(far_scores, axis=-1))
        shrink = jnp.exp(running_max - new_max)
        far_weights = jnp.exp(far_scores - new_max[..., None])
        total = total * shrink + jnp.sum(far_weights, axis=-1)
        paired = far_weights.astype(jnp.bfloat16).reshape(
            local_groups, per_group, 2, block_len, block_len
        )
        far_sum = jnp.einsum(
            "grjtu,jugh->jtgrh", paired, far_values, preferred_element_type=jnp.float32
        )
        far_sum = far_sum.reshape(row_count, local_groups, per_group, head_size)
        accum = accum * jnp.transpose(shrink, (2, 0, 1))[..., None] + far_sum
        running_max = new_max
    attended = (accum / jnp.transpose(total, (2, 0, 1))[..., None]).astype(jnp.bfloat16)
    attended = attended.reshape(row_count, local_groups, per_group * head_size)
    tile_count = lax.axis_size("kvh") * lax.axis_size("sub")
    tile_cols = width // tile_count
    owner_index = lax.axis_index("kvh") * lax.axis_size("sub") + lax.axis_index("sub")
    owned = lax.dynamic_slice_in_dim(normed, owner_index * tile_cols, tile_cols, 1)
    seq_count = lax.axis_size("seq")
    inverse_count = 1.0 / (row_count * seq_count)
    gram_sum = lax.psum_scatter(
        (
            jnp.einsum("tc,tr->cr", normed, owned, preferred_element_type=jnp.float32)
            * inverse_count
        ).astype(jnp.bfloat16),
        "seq",
        scatter_dimension=0,
        tiled=True,
    ).astype(jnp.float32)
    gram_tile = gram_sum
    return (attended, gram_tile)


def solution(mesh):
    placed = (
        P(("grp", "seq"), ("kvh", "sub")),
        P(),
        P(None, "kvh", "sub"),
        P("sub", "kvh", None),
        P("sub", "kvh", None),
        P(),
    )
    return jax.shard_map(
        body,
        mesh=mesh,
        in_specs=placed,
        out_specs=(P(("grp", "seq"), "kvh", "sub"), P(("grp", "seq"), ("kvh", "sub"))),
        check_vma=False,
    )
```

```python
import math

import jax
import jax.numpy as jnp
from jax import lax
from jax.sharding import PartitionSpec as P

rope_base = 500000.0


def from_partner(block, axis, bit):
    count = lax.axis_size(axis)
    route = []
    for low in range(count):
        high = low | 1 << bit
        if high != low and high < count:
            route += [(low, high), (high, low)]
    return lax.ppermute(block, axis, route)


def swap_halves(pieces, count, index):
    whole = [None] * count
    whole[0] = pieces
    for shift in range(1, count):
        route = [(j, (j + shift) % count) for j in range(count)]
        whole[shift] = lax.ppermute(pieces, "sub", route)
    return whole


def split_send(blocks, axis, bit):
    count = lax.axis_size("sub")
    index = lax.axis_index("sub")
    share = blocks[0].shape[0] // count
    mine = tuple(lax.dynamic_slice_in_dim(b, index * share, share, 0) for b in blocks)
    got = from_partner(mine, axis, bit)
    whole = swap_halves(got, count, index)
    out = []
    for n, b in enumerate(blocks):
        full = jnp.zeros_like(b)
        for shift in range(count):
            source = (index - shift) % count
            full = lax.dynamic_update_slice_in_dim(full, whole[shift][n], source * share, 0)
        out.append(full)
    return tuple(out)


def rotate(vectors, positions):
    width = vectors.shape[-1]
    half = width // 2
    inverse = jnp.exp(jnp.arange(half, dtype=jnp.float32) * (-2.0 * math.log(rope_base) / width))
    angles = positions.astype(jnp.float32)[:, None] * inverse[None, :]
    shape = (angles.shape[0],) + (1,) * (vectors.ndim - 2) + (half,)
    cosine = jnp.cos(angles).reshape(shape)
    sine = jnp.sin(angles).reshape(shape)
    first = vectors[..., :half]
    second = vectors[..., half:]
    return jnp.concatenate(
        [first * cosine - second * sine, second * cosine + first * sine], axis=-1
    )


def body(tokens, norm_gain, w_query, w_key, w_value, links):
    kvh_total = lax.axis_size("kvh")
    kvh_at = lax.axis_index("kvh")
    sub_total = lax.axis_size("sub")
    lane_index = lax.axis_index("sub")
    across = [tokens]
    for shift in range(1, kvh_total):
        route = [(j, (j + shift) % kvh_total) for j in range(kvh_total)]
        across.append(lax.ppermute(tokens, "kvh", route))
    pieces = []
    for shift in range(kvh_total):
        pieces.extend(swap_halves(across[shift], sub_total, lane_index))
    blocks = []
    for owner_kvh in range(kvh_total):
        for owner_sub in range(sub_total):
            pick = ((kvh_at - owner_kvh) % kvh_total) * sub_total + (lane_index - owner_sub) % sub_total
            blocks.append(lax.select_n(pick, *pieces))
    gathered = jnp.concatenate(blocks, axis=1)
    widened = gathered.astype(jnp.float32)
    mean_square = jnp.mean(widened * widened, axis=-1, keepdims=True)
    normed = (widened * lax.rsqrt(mean_square + 1e-05) * norm_gain).astype(jnp.bfloat16)
    row_count = normed.shape[0]
    block_len = row_count // 2
    width = normed.shape[1]
    seq_index = lax.axis_index("seq")
    local_rows = jnp.arange(row_count, dtype=jnp.int32)
    positions = seq_index * row_count + local_rows
    head_size = w_key.shape[2]
    local_groups = w_key.shape[1]
    per_group = w_query.shape[2] // head_size
    queries = jnp.einsum("td,dgc->tgc", normed, w_query, preferred_element_type=jnp.float32)
    queries = rotate(
        queries.reshape(row_count, local_groups, per_group, head_size), positions
    ).astype(jnp.bfloat16)
    sub_count = lax.axis_size("sub")
    sub_index = lax.axis_index("sub")
    row_share = w_key.shape[0]
    key_more = None
    value_more = None
    for shift in range(sub_count):
        if shift == 0:
            key_part, value_part = w_key, w_value
        else:
            route = [(j, (j + shift) % sub_count) for j in range(sub_count)]
            key_part, value_part = lax.ppermute((w_key, w_value), "sub", route)
        source = (sub_index - shift) % sub_count
        rows = lax.dynamic_slice_in_dim(normed, source * row_share, row_share, 1)
        key_step = jnp.einsum("td,dgh->tgh", rows, key_part, preferred_element_type=jnp.float32)
        value_step = jnp.einsum("td,dgh->tgh", rows, value_part, preferred_element_type=jnp.float32)
        key_more = key_step if key_more is None else key_more + key_step
        value_more = value_step if value_more is None else value_more + value_step
    keys = rotate(key_more, positions).astype(jnp.bfloat16)
    values = value_more.astype(jnp.bfloat16)
    block_ids = seq_index * 2 + jnp.arange(2, dtype=jnp.int32)
    query_block = local_rows // block_len
    scale = 1.0 / math.sqrt(head_size)
    scores = jnp.einsum("tgrh,ugh->grtu", queries, keys, preferred_element_type=jnp.float32) * scale
    near_linked = lax.dynamic_slice_in_dim(links[0], seq_index * 2, 2) != block_ids
    same_block = query_block[:, None] == query_block[None, :]
    causal = same_block & (local_rows[None, :] <= local_rows[:, None])
    across = ~same_block & near_linked[query_block][:, None]
    allowed = causal | across
    scores = jnp.where(allowed[None, None], scores, -jnp.inf)
    running_max = jnp.max(scores, axis=-1)
    weights = jnp.exp(scores - running_max[..., None])
    total = jnp.sum(weights, axis=-1)
    accum = jnp.einsum(
        "grtu,ugh->tgrh", weights.astype(jnp.bfloat16), values, preferred_element_type=jnp.float32
    )
    query_pairs = queries.reshape(2, block_len, local_groups, per_group, head_size)
    for section in range(1, lax.axis_size("seq").bit_length()):
        far_keys, far_values = split_send((keys, values), "seq", section - 1)
        far_keys = far_keys.reshape(2, block_len, local_groups, head_size)
        far_values = far_values.reshape(2, block_len, local_groups, head_size)
        linked = lax.dynamic_slice_in_dim(links[section], seq_index * 2, 2) != block_ids
        offset = jnp.where(linked, 0.0, -1e30).astype(jnp.float32)[query_block]
        far_scores = jnp.einsum(
            "jtgrh,jugh->grjtu", query_pairs, far_keys, preferred_element_type=jnp.float32
        )
        far_scores = (
            far_scores.reshape(local_groups, per_group, row_count, block_len) * scale
            + offset[None, None, :, None]
        )
        new_max = jnp.maximum(running_max, jnp.max(far_scores, axis=-1))
        shrink = jnp.exp(running_max - new_max)
        far_weights = jnp.exp(far_scores - new_max[..., None])
        total = total * shrink + jnp.sum(far_weights, axis=-1)
        paired = far_weights.astype(jnp.bfloat16).reshape(
            local_groups, per_group, 2, block_len, block_len
        )
        far_sum = jnp.einsum(
            "grjtu,jugh->jtgrh", paired, far_values, preferred_element_type=jnp.float32
        )
        far_sum = far_sum.reshape(row_count, local_groups, per_group, head_size)
        accum = accum * jnp.transpose(shrink, (2, 0, 1))[..., None] + far_sum
        running_max = new_max
    attended = (accum / jnp.transpose(total, (2, 0, 1))[..., None]).astype(jnp.bfloat16)
    attended = attended.reshape(row_count, local_groups, per_group * head_size)
    tile_count = lax.axis_size("kvh") * lax.axis_size("sub")
    tile_cols = width // tile_count
    owner_index = lax.axis_index("kvh") * lax.axis_size("sub") + lax.axis_index("sub")
    owned = lax.dynamic_slice_in_dim(normed, owner_index * tile_cols, tile_cols, 1)
    seq_count = lax.axis_size("seq")
    band = width // seq_count
    inverse_count = 1.0 / (row_count * seq_count)
    partial = (
        jnp.einsum("tc,tr->cr", normed, owned, preferred_element_type=jnp.float32)
        * inverse_count
    )
    split = tile_cols // 2
    offloaded = lax.psum_scatter(
        partial[:, :split].astype(jnp.bfloat16), "seq", scatter_dimension=0, tiled=True
    ).astype(jnp.float32)
    rest = partial[:, split:]

    def piece(dest):
        dest = jnp.clip(dest, 0, seq_count - 1)
        return lax.dynamic_slice_in_dim(rest, dest * band, band, 0)

    from_left = jnp.zeros((band, tile_cols - split), jnp.bfloat16)
    from_right = jnp.zeros((band, tile_cols - split), jnp.bfloat16)
    for step in range(1, seq_count):
        up = piece(seq_index + seq_count - step) + from_left.astype(jnp.float32)
        down = piece(seq_index - seq_count + step) + from_right.astype(jnp.float32)
        up_route = [(c, c + 1) for c in range(step) if c + 1 < seq_count]
        down_route = [(c, c - 1) for c in range(seq_count - step, seq_count) if c >= 1]
        from_left = lax.ppermute(up.astype(jnp.bfloat16), "seq", up_route)
        from_right = lax.ppermute(down.astype(jnp.bfloat16), "seq", down_route)
    stepped = piece(seq_index) + from_left.astype(jnp.float32) + from_right.astype(jnp.float32)
    gram_sum = jnp.concatenate([offloaded, stepped], axis=1)
    gram_tile = gram_sum
    return (attended, gram_tile)


def solution(mesh):
    placed = (
        P(("grp", "seq"), ("kvh", "sub")),
        P(),
        P(None, "kvh", "sub"),
        P("sub", "kvh", None),
        P("sub", "kvh", None),
        P(),
    )
    return jax.shard_map(
        body,
        mesh=mesh,
        in_specs=placed,
        out_specs=(P(("grp", "seq"), "kvh", "sub"), P(("grp", "seq"), ("kvh", "sub"))),
        check_vma=False,
    )
```

```python
import math

import jax
import jax.numpy as jnp
from jax import lax
from jax.sharding import PartitionSpec as P

rope_base = 500000.0


def from_partner(block, axis, bit):
    count = lax.axis_size(axis)
    route = []
    for low in range(count):
        high = low | 1 << bit
        if high != low and high < count:
            route += [(low, high), (high, low)]
    return lax.ppermute(block, axis, route)


def swap_halves(pieces, count, index):
    whole = [None] * count
    whole[0] = pieces
    for shift in range(1, count):
        route = [(j, (j + shift) % count) for j in range(count)]
        whole[shift] = lax.ppermute(pieces, "sub", route)
    return whole


def split_send(blocks, axis, bit):
    count = lax.axis_size("sub")
    index = lax.axis_index("sub")
    share = blocks[0].shape[0] // count
    mine = tuple(lax.dynamic_slice_in_dim(b, index * share, share, 0) for b in blocks)
    got = from_partner(mine, axis, bit)
    whole = swap_halves(got, count, index)
    out = []
    for n, b in enumerate(blocks):
        full = jnp.zeros_like(b)
        for shift in range(count):
            source = (index - shift) % count
            full = lax.dynamic_update_slice_in_dim(full, whole[shift][n], source * share, 0)
        out.append(full)
    return tuple(out)


def rotate(vectors, positions):
    width = vectors.shape[-1]
    half = width // 2
    inverse = jnp.exp(jnp.arange(half, dtype=jnp.float32) * (-2.0 * math.log(rope_base) / width))
    angles = positions.astype(jnp.float32)[:, None] * inverse[None, :]
    shape = (angles.shape[0],) + (1,) * (vectors.ndim - 2) + (half,)
    cosine = jnp.cos(angles).reshape(shape)
    sine = jnp.sin(angles).reshape(shape)
    first = vectors[..., :half]
    second = vectors[..., half:]
    return jnp.concatenate(
        [first * cosine - second * sine, second * cosine + first * sine], axis=-1
    )


def body(tokens, norm_gain, w_query, w_key, w_value, links):
    kvh_total = lax.axis_size("kvh")
    kvh_at = lax.axis_index("kvh")
    sub_total = lax.axis_size("sub")
    lane_index = lax.axis_index("sub")
    lane_width = tokens.shape[1]
    width = lane_width * kvh_total * sub_total
    own_wide = tokens.astype(jnp.float32)
    own_square = jnp.sum(own_wide * own_wide, axis=-1)
    square_across = [own_square]
    across = [tokens]
    for shift in range(1, kvh_total):
        route = [(j, (j + shift) % kvh_total) for j in range(kvh_total)]
        square_across.append(lax.ppermute(own_square, "kvh", route))
        across.append(lax.ppermute(tokens, "kvh", route))
    square_pieces = []
    pieces = []
    places = []
    for shift in range(kvh_total):
        square_pieces.extend(swap_halves(square_across[shift], sub_total, lane_index))
        pieces.extend(swap_halves(across[shift], sub_total, lane_index))
        for lane_shift in range(sub_total):
            owner = ((kvh_at - shift) % kvh_total) * sub_total + (lane_index - lane_shift) % sub_total
            places.append(owner)
    square_total = square_pieces[0]
    for extra in square_pieces[1:]:
        square_total = square_total + extra
    scale_rows = lax.rsqrt(square_total / width + 1e-05)[:, None]
    normed_pieces = []
    for piece_at, owner in zip(pieces, places):
        gain_part = lax.dynamic_slice_in_dim(norm_gain, owner * lane_width, lane_width, 0)
        normed_pieces.append(
            (piece_at.astype(jnp.float32) * scale_rows * gain_part).astype(jnp.bfloat16)
        )
    owned = normed_pieces[0]
    inverse_total = 1.0 / (tokens.shape[0] * lax.axis_size("seq"))
    stacked_gram = jnp.zeros((width, lane_width), jnp.bfloat16)
    for normed_at, owner in zip(normed_pieces, places):
        rows_part = (
            jnp.einsum("tc,tr->cr", normed_at, owned, preferred_element_type=jnp.float32)
            * inverse_total
        ).astype(jnp.bfloat16)
        stacked_gram = lax.dynamic_update_slice_in_dim(stacked_gram, rows_part, owner * lane_width, 0)
    blocks = []
    for owner_kvh in range(kvh_total):
        for owner_sub in range(sub_total):
            pick = ((kvh_at - owner_kvh) % kvh_total) * sub_total + (lane_index - owner_sub) % sub_total
            blocks.append(lax.select_n(pick, *normed_pieces))
    normed = jnp.concatenate(blocks, axis=1)
    row_count = normed.shape[0]
    block_len = row_count // 2
    width = normed.shape[1]
    seq_index = lax.axis_index("seq")
    local_rows = jnp.arange(row_count, dtype=jnp.int32)
    positions = seq_index * row_count + local_rows
    head_size = w_key.shape[2]
    local_groups = w_key.shape[1]
    per_group = w_query.shape[2] // head_size
    queries = jnp.einsum("td,dgc->tgc", normed, w_query, preferred_element_type=jnp.float32)
    queries = rotate(
        queries.reshape(row_count, local_groups, per_group, head_size), positions
    ).astype(jnp.bfloat16)
    sub_count = lax.axis_size("sub")
    sub_index = lax.axis_index("sub")
    row_share = w_key.shape[0]
    key_more = None
    value_more = None
    for shift in range(sub_count):
        if shift == 0:
            key_part, value_part = w_key, w_value
        else:
            route = [(j, (j + shift) % sub_count) for j in range(sub_count)]
            key_part, value_part = lax.ppermute((w_key, w_value), "sub", route)
        source = (sub_index - shift) % sub_count
        rows = lax.dynamic_slice_in_dim(normed, source * row_share, row_share, 1)
        key_step = jnp.einsum("td,dgh->tgh", rows, key_part, preferred_element_type=jnp.float32)
        value_step = jnp.einsum("td,dgh->tgh", rows, value_part, preferred_element_type=jnp.float32)
        key_more = key_step if key_more is None else key_more + key_step
        value_more = value_step if value_more is None else value_more + value_step
    keys = rotate(key_more, positions).astype(jnp.bfloat16)
    values = value_more.astype(jnp.bfloat16)
    block_ids = seq_index * 2 + jnp.arange(2, dtype=jnp.int32)
    query_block = local_rows // block_len
    scale = 1.0 / math.sqrt(head_size)
    scores = jnp.einsum("tgrh,ugh->grtu", queries, keys, preferred_element_type=jnp.float32) * scale
    near_linked = lax.dynamic_slice_in_dim(links[0], seq_index * 2, 2) != block_ids
    same_block = query_block[:, None] == query_block[None, :]
    causal = same_block & (local_rows[None, :] <= local_rows[:, None])
    across = ~same_block & near_linked[query_block][:, None]
    allowed = causal | across
    scores = jnp.where(allowed[None, None], scores, -jnp.inf)
    running_max = jnp.max(scores, axis=-1)
    weights = jnp.exp(scores - running_max[..., None])
    total = jnp.sum(weights, axis=-1)
    accum = jnp.einsum(
        "grtu,ugh->tgrh", weights.astype(jnp.bfloat16), values, preferred_element_type=jnp.float32
    )
    query_pairs = queries.reshape(2, block_len, local_groups, per_group, head_size)
    for section in range(1, lax.axis_size("seq").bit_length()):
        far_keys, far_values = split_send((keys, values), "seq", section - 1)
        far_keys = far_keys.reshape(2, block_len, local_groups, head_size)
        far_values = far_values.reshape(2, block_len, local_groups, head_size)
        linked = lax.dynamic_slice_in_dim(links[section], seq_index * 2, 2) != block_ids
        offset = jnp.where(linked, 0.0, -1e30).astype(jnp.float32)[query_block]
        far_scores = jnp.einsum(
            "jtgrh,jugh->grjtu", query_pairs, far_keys, preferred_element_type=jnp.float32
        )
        far_scores = (
            far_scores.reshape(local_groups, per_group, row_count, block_len) * scale
            + offset[None, None, :, None]
        )
        new_max = jnp.maximum(running_max, jnp.max(far_scores, axis=-1))
        shrink = jnp.exp(running_max - new_max)
        far_weights = jnp.exp(far_scores - new_max[..., None])
        total = total * shrink + jnp.sum(far_weights, axis=-1)
        paired = far_weights.astype(jnp.bfloat16).reshape(
            local_groups, per_group, 2, block_len, block_len
        )
        far_sum = jnp.einsum(
            "grjtu,jugh->jtgrh", paired, far_values, preferred_element_type=jnp.float32
        )
        far_sum = far_sum.reshape(row_count, local_groups, per_group, head_size)
        accum = accum * jnp.transpose(shrink, (2, 0, 1))[..., None] + far_sum
        running_max = new_max
    attended = (accum / jnp.transpose(total, (2, 0, 1))[..., None]).astype(jnp.bfloat16)
    attended = attended.reshape(row_count, local_groups, per_group * head_size)
    gram_sum = lax.psum_scatter(
        stacked_gram, "seq", scatter_dimension=0, tiled=True
    ).astype(jnp.float32)
    gram_tile = gram_sum
    return (attended, gram_tile)


def solution(mesh):
    placed = (
        P(("grp", "seq"), ("kvh", "sub")),
        P(),
        P(None, "kvh", "sub"),
        P("sub", "kvh", None),
        P("sub", "kvh", None),
        P(),
    )
    return jax.shard_map(
        body,
        mesh=mesh,
        in_specs=placed,
        out_specs=(P(("grp", "seq"), "kvh", "sub"), P(("grp", "seq"), ("kvh", "sub"))),
        check_vma=False,
    )
```

```python
import math

import jax
import jax.numpy as jnp
from jax import lax
from jax.sharding import PartitionSpec as P

rope_base = 500000.0


def from_partner(block, axis, bit):
    count = lax.axis_size(axis)
    route = []
    for low in range(count):
        high = low | 1 << bit
        if high != low and high < count:
            route += [(low, high), (high, low)]
    return lax.ppermute(block, axis, route)


def swap_halves(pieces, count, index):
    whole = [None] * count
    whole[0] = pieces
    for shift in range(1, count):
        route = [(j, (j + shift) % count) for j in range(count)]
        whole[shift] = lax.ppermute(pieces, "sub", route)
    return whole


def split_send(blocks, axis, bit):
    count = lax.axis_size("sub")
    index = lax.axis_index("sub")
    share = blocks[0].shape[0] // count
    mine = tuple(lax.dynamic_slice_in_dim(b, index * share, share, 0) for b in blocks)
    got = from_partner(mine, axis, bit)
    whole = swap_halves(got, count, index)
    out = []
    for n, b in enumerate(blocks):
        full = jnp.zeros_like(b)
        for shift in range(count):
            source = (index - shift) % count
            full = lax.dynamic_update_slice_in_dim(full, whole[shift][n], source * share, 0)
        out.append(full)
    return tuple(out)


def rotate(vectors, positions):
    width = vectors.shape[-1]
    half = width // 2
    inverse = jnp.exp(jnp.arange(half, dtype=jnp.float32) * (-2.0 * math.log(rope_base) / width))
    angles = positions.astype(jnp.float32)[:, None] * inverse[None, :]
    shape = (angles.shape[0],) + (1,) * (vectors.ndim - 2) + (half,)
    cosine = jnp.cos(angles).reshape(shape)
    sine = jnp.sin(angles).reshape(shape)
    first = vectors[..., :half]
    second = vectors[..., half:]
    return jnp.concatenate(
        [first * cosine - second * sine, second * cosine + first * sine], axis=-1
    )


def body(tokens, norm_gain, w_query, w_key, w_value, links):
    kvh_total = lax.axis_size("kvh")
    kvh_at = lax.axis_index("kvh")
    sub_total = lax.axis_size("sub")
    lane_index = lax.axis_index("sub")
    across = [tokens]
    for shift in range(1, kvh_total):
        route = [(j, (j + shift) % kvh_total) for j in range(kvh_total)]
        across.append(lax.ppermute(tokens, "kvh", route))
    pieces = []
    for shift in range(kvh_total):
        pieces.extend(swap_halves(across[shift], sub_total, lane_index))
    blocks = []
    for owner_kvh in range(kvh_total):
        for owner_sub in range(sub_total):
            pick = ((kvh_at - owner_kvh) % kvh_total) * sub_total + (lane_index - owner_sub) % sub_total
            blocks.append(lax.select_n(pick, *pieces))
    gathered = jnp.concatenate(blocks, axis=1)
    widened = gathered.astype(jnp.float32)
    mean_square = jnp.mean(widened * widened, axis=-1, keepdims=True)
    normed = (widened * lax.rsqrt(mean_square + 1e-05) * norm_gain).astype(jnp.bfloat16)
    row_count = normed.shape[0]
    block_len = row_count // 2
    width = normed.shape[1]
    seq_index = lax.axis_index("seq")
    local_rows = jnp.arange(row_count, dtype=jnp.int32)
    positions = seq_index * row_count + local_rows
    head_size = w_key.shape[2]
    local_groups = w_key.shape[1]
    per_group = w_query.shape[2] // head_size
    queries = jnp.einsum("td,dgc->tgc", normed, w_query, preferred_element_type=jnp.float32)
    queries = rotate(
        queries.reshape(row_count, local_groups, per_group, head_size), positions
    ).astype(jnp.bfloat16)
    sub_count = lax.axis_size("sub")
    sub_index = lax.axis_index("sub")
    row_share = w_key.shape[0]
    key_more = None
    value_more = None
    for shift in range(sub_count):
        if shift == 0:
            key_part, value_part = w_key, w_value
        else:
            route = [(j, (j + shift) % sub_count) for j in range(sub_count)]
            key_part, value_part = lax.ppermute((w_key, w_value), "sub", route)
        source = (sub_index - shift) % sub_count
        rows = lax.dynamic_slice_in_dim(normed, source * row_share, row_share, 1)
        key_step = jnp.einsum("td,dgh->tgh", rows, key_part, preferred_element_type=jnp.float32)
        value_step = jnp.einsum("td,dgh->tgh", rows, value_part, preferred_element_type=jnp.float32)
        key_more = key_step if key_more is None else key_more + key_step
        value_more = value_step if value_more is None else value_more + value_step
    keys = rotate(key_more, positions).astype(jnp.bfloat16)
    values = value_more.astype(jnp.bfloat16)
    block_ids = seq_index * 2 + jnp.arange(2, dtype=jnp.int32)
    query_block = local_rows // block_len
    scale = 1.0 / math.sqrt(head_size)
    scores = jnp.einsum("tgrh,ugh->grtu", queries, keys, preferred_element_type=jnp.float32) * scale
    near_linked = lax.dynamic_slice_in_dim(links[0], seq_index * 2, 2) != block_ids
    same_block = query_block[:, None] == query_block[None, :]
    causal = same_block & (local_rows[None, :] <= local_rows[:, None])
    across = ~same_block & near_linked[query_block][:, None]
    allowed = causal | across
    scores = jnp.where(allowed[None, None], scores, -jnp.inf)
    running_max = jnp.max(scores, axis=-1)
    weights = jnp.exp(scores - running_max[..., None])
    total = jnp.sum(weights, axis=-1)
    accum = jnp.einsum(
        "grtu,ugh->tgrh", weights.astype(jnp.bfloat16), values, preferred_element_type=jnp.float32
    )
    query_pairs = queries.reshape(2, block_len, local_groups, per_group, head_size)
    for section in range(1, lax.axis_size("seq").bit_length()):
        far_keys, far_values = split_send((keys, values), "seq", section - 1)
        far_keys = far_keys.reshape(2, block_len, local_groups, head_size)
        far_values = far_values.reshape(2, block_len, local_groups, head_size)
        linked = lax.dynamic_slice_in_dim(links[section], seq_index * 2, 2) != block_ids
        offset = jnp.where(linked, 0.0, -1e30).astype(jnp.float32)[query_block]
        far_scores = jnp.einsum(
            "jtgrh,jugh->grjtu", query_pairs, far_keys, preferred_element_type=jnp.float32
        )
        far_scores = (
            far_scores.reshape(local_groups, per_group, row_count, block_len) * scale
            + offset[None, None, :, None]
        )
        new_max = jnp.maximum(running_max, jnp.max(far_scores, axis=-1))
        shrink = jnp.exp(running_max - new_max)
        far_weights = jnp.exp(far_scores - new_max[..., None])
        total = total * shrink + jnp.sum(far_weights, axis=-1)
        paired = far_weights.astype(jnp.bfloat16).reshape(
            local_groups, per_group, 2, block_len, block_len
        )
        far_sum = jnp.einsum(
            "grjtu,jugh->jtgrh", paired, far_values, preferred_element_type=jnp.float32
        )
        far_sum = far_sum.reshape(row_count, local_groups, per_group, head_size)
        accum = accum * jnp.transpose(shrink, (2, 0, 1))[..., None] + far_sum
        running_max = new_max
    attended = (accum / jnp.transpose(total, (2, 0, 1))[..., None]).astype(jnp.bfloat16)
    attended = attended.reshape(row_count, local_groups, per_group * head_size)
    tile_count = lax.axis_size("kvh") * lax.axis_size("sub")
    tile_cols = width // tile_count
    owner_index = lax.axis_index("kvh") * lax.axis_size("sub") + lax.axis_index("sub")
    owned = lax.dynamic_slice_in_dim(normed, owner_index * tile_cols, tile_cols, 1)
    seq_count = lax.axis_size("seq")
    band = width // seq_count
    inverse_count = 1.0 / (row_count * seq_count)
    share = row_count // sub_count
    all_owned = lax.all_gather(owned, "seq", axis=0, tiled=True)
    mine = lax.dynamic_slice_in_dim(normed, seq_index * band, band, 1)
    gram_sum = jnp.einsum("tc,tr->cr", mine, owned, preferred_element_type=jnp.float32)
    my_rows = lax.dynamic_slice_in_dim(normed, sub_index * share, share, 0)
    for shift in range(1, seq_count):
        target = (seq_index + shift) % seq_count
        outgoing = lax.dynamic_slice_in_dim(my_rows, target * band, band, 1)
        route = [(j, (j + shift) % seq_count) for j in range(seq_count)]
        incoming = lax.ppermute(outgoing, "seq", route)
        halves = swap_halves(incoming, sub_count, sub_index)
        source = (seq_index - shift) % seq_count
        their_owned = lax.dynamic_slice_in_dim(all_owned, source * row_count, row_count, 0)
        for lane_shift in range(sub_count):
            half_at = (sub_index - lane_shift) % sub_count
            their_rows = lax.dynamic_slice_in_dim(their_owned, half_at * share, share, 0)
            gram_sum = gram_sum + jnp.einsum(
                "tc,tr->cr", halves[lane_shift], their_rows, preferred_element_type=jnp.float32
            )
    gram_sum = gram_sum * inverse_count
    gram_tile = gram_sum
    return (attended, gram_tile)


def solution(mesh):
    placed = (
        P(("grp", "seq"), ("kvh", "sub")),
        P(),
        P(None, "kvh", "sub"),
        P("sub", "kvh", None),
        P("sub", "kvh", None),
        P(),
    )
    return jax.shard_map(
        body,
        mesh=mesh,
        in_specs=placed,
        out_specs=(P(("grp", "seq"), "kvh", "sub"), P(("grp", "seq"), ("kvh", "sub"))),
        check_vma=False,
    )
```

```python
import math

import jax
import jax.numpy as jnp
from jax import lax
from jax.sharding import PartitionSpec as P

rope_base = 500000.0


def from_partner(block, axis, bit):
    count = lax.axis_size(axis)
    route = []
    for low in range(count):
        high = low | 1 << bit
        if high != low and high < count:
            route += [(low, high), (high, low)]
    return lax.ppermute(block, axis, route)


def swap_halves(pieces, count, index):
    whole = [None] * count
    whole[0] = pieces
    for shift in range(1, count):
        route = [(j, (j + shift) % count) for j in range(count)]
        whole[shift] = lax.ppermute(pieces, "sub", route)
    return whole


def split_send(blocks, axis, bit):
    count = lax.axis_size("sub")
    index = lax.axis_index("sub")
    share = blocks[0].shape[0] // count
    mine = tuple(lax.dynamic_slice_in_dim(b, index * share, share, 0) for b in blocks)
    got = from_partner(mine, axis, bit)
    whole = swap_halves(got, count, index)
    out = []
    for n, b in enumerate(blocks):
        full = jnp.zeros_like(b)
        for shift in range(count):
            source = (index - shift) % count
            full = lax.dynamic_update_slice_in_dim(full, whole[shift][n], source * share, 0)
        out.append(full)
    return tuple(out)


def rotate(vectors, positions):
    width = vectors.shape[-1]
    half = width // 2
    inverse = jnp.exp(jnp.arange(half, dtype=jnp.float32) * (-2.0 * math.log(rope_base) / width))
    angles = positions.astype(jnp.float32)[:, None] * inverse[None, :]
    shape = (angles.shape[0],) + (1,) * (vectors.ndim - 2) + (half,)
    cosine = jnp.cos(angles).reshape(shape)
    sine = jnp.sin(angles).reshape(shape)
    first = vectors[..., :half]
    second = vectors[..., half:]
    return jnp.concatenate(
        [first * cosine - second * sine, second * cosine + first * sine], axis=-1
    )


def body(tokens, norm_gain, w_query, w_key, w_value, links):
    kvh_total = lax.axis_size("kvh")
    kvh_at = lax.axis_index("kvh")
    sub_total = lax.axis_size("sub")
    lane_index = lax.axis_index("sub")
    across = [tokens]
    for shift in range(1, kvh_total):
        route = [(j, (j + shift) % kvh_total) for j in range(kvh_total)]
        across.append(lax.ppermute(tokens, "kvh", route))
    pieces = []
    for shift in range(kvh_total):
        pieces.extend(swap_halves(across[shift], sub_total, lane_index))
    blocks = []
    for owner_kvh in range(kvh_total):
        for owner_sub in range(sub_total):
            pick = ((kvh_at - owner_kvh) % kvh_total) * sub_total + (lane_index - owner_sub) % sub_total
            blocks.append(lax.select_n(pick, *pieces))
    gathered = jnp.concatenate(blocks, axis=1)
    widened = gathered.astype(jnp.float32)
    mean_square = jnp.mean(widened * widened, axis=-1, keepdims=True)
    row_scale = lax.rsqrt(mean_square + 1e-05)[:, 0]
    normed = (widened * row_scale[:, None] * norm_gain).astype(jnp.bfloat16)
    row_count = normed.shape[0]
    block_len = row_count // 2
    width = normed.shape[1]
    seq_index = lax.axis_index("seq")
    local_rows = jnp.arange(row_count, dtype=jnp.int32)
    positions = seq_index * row_count + local_rows
    head_size = w_key.shape[2]
    local_groups = w_key.shape[1]
    per_group = w_query.shape[2] // head_size
    queries = jnp.einsum("td,dgc->tgc", normed, w_query, preferred_element_type=jnp.float32)
    queries = rotate(
        queries.reshape(row_count, local_groups, per_group, head_size), positions
    ).astype(jnp.bfloat16)
    sub_count = lax.axis_size("sub")
    sub_index = lax.axis_index("sub")
    row_share = w_key.shape[0]
    key_more = None
    value_more = None
    for shift in range(sub_count):
        if shift == 0:
            key_part, value_part = w_key, w_value
        else:
            route = [(j, (j + shift) % sub_count) for j in range(sub_count)]
            key_part, value_part = lax.ppermute((w_key, w_value), "sub", route)
        source = (sub_index - shift) % sub_count
        rows = lax.dynamic_slice_in_dim(normed, source * row_share, row_share, 1)
        key_step = jnp.einsum("td,dgh->tgh", rows, key_part, preferred_element_type=jnp.float32)
        value_step = jnp.einsum("td,dgh->tgh", rows, value_part, preferred_element_type=jnp.float32)
        key_more = key_step if key_more is None else key_more + key_step
        value_more = value_step if value_more is None else value_more + value_step
    keys = rotate(key_more, positions).astype(jnp.bfloat16)
    values = value_more.astype(jnp.bfloat16)
    block_ids = seq_index * 2 + jnp.arange(2, dtype=jnp.int32)
    query_block = local_rows // block_len
    scale = 1.0 / math.sqrt(head_size)
    scores = jnp.einsum("tgrh,ugh->grtu", queries, keys, preferred_element_type=jnp.float32) * scale
    near_linked = lax.dynamic_slice_in_dim(links[0], seq_index * 2, 2) != block_ids
    same_block = query_block[:, None] == query_block[None, :]
    causal = same_block & (local_rows[None, :] <= local_rows[:, None])
    across = ~same_block & near_linked[query_block][:, None]
    allowed = causal | across
    scores = jnp.where(allowed[None, None], scores, -jnp.inf)
    running_max = jnp.max(scores, axis=-1)
    weights = jnp.exp(scores - running_max[..., None])
    total = jnp.sum(weights, axis=-1)
    accum = jnp.einsum(
        "grtu,ugh->tgrh", weights.astype(jnp.bfloat16), values, preferred_element_type=jnp.float32
    )
    query_pairs = queries.reshape(2, block_len, local_groups, per_group, head_size)
    for section in range(1, lax.axis_size("seq").bit_length()):
        far_keys, far_values = split_send((keys, values), "seq", section - 1)
        far_keys = far_keys.reshape(2, block_len, local_groups, head_size)
        far_values = far_values.reshape(2, block_len, local_groups, head_size)
        linked = lax.dynamic_slice_in_dim(links[section], seq_index * 2, 2) != block_ids
        offset = jnp.where(linked, 0.0, -1e30).astype(jnp.float32)[query_block]
        far_scores = jnp.einsum(
            "jtgrh,jugh->grjtu", query_pairs, far_keys, preferred_element_type=jnp.float32
        )
        far_scores = (
            far_scores.reshape(local_groups, per_group, row_count, block_len) * scale
            + offset[None, None, :, None]
        )
        new_max = jnp.maximum(running_max, jnp.max(far_scores, axis=-1))
        shrink = jnp.exp(running_max - new_max)
        far_weights = jnp.exp(far_scores - new_max[..., None])
        total = total * shrink + jnp.sum(far_weights, axis=-1)
        paired = far_weights.astype(jnp.bfloat16).reshape(
            local_groups, per_group, 2, block_len, block_len
        )
        far_sum = jnp.einsum(
            "grjtu,jugh->jtgrh", paired, far_values, preferred_element_type=jnp.float32
        )
        far_sum = far_sum.reshape(row_count, local_groups, per_group, head_size)
        accum = accum * jnp.transpose(shrink, (2, 0, 1))[..., None] + far_sum
        running_max = new_max
    attended = (accum / jnp.transpose(total, (2, 0, 1))[..., None]).astype(jnp.bfloat16)
    attended = attended.reshape(row_count, local_groups, per_group * head_size)
    tile_count = lax.axis_size("kvh") * lax.axis_size("sub")
    tile_cols = width // tile_count
    owner_index = lax.axis_index("kvh") * lax.axis_size("sub") + lax.axis_index("sub")
    owned = lax.dynamic_slice_in_dim(normed, owner_index * tile_cols, tile_cols, 1)
    seq_count = lax.axis_size("seq")
    band = width // seq_count
    inverse_count = 1.0 / (row_count * seq_count)
    share = row_count // sub_count
    raw_columns = lax.all_gather(tokens, "seq", axis=0, tiled=True)
    column_gain = lax.dynamic_slice_in_dim(norm_gain, owner_index * tile_cols, tile_cols, 0)
    mine = lax.dynamic_slice_in_dim(normed, seq_index * band, band, 1)
    gram_sum = jnp.einsum("tc,tr->cr", mine, owned, preferred_element_type=jnp.float32)
    my_rows = lax.dynamic_slice_in_dim(normed, sub_index * share, share, 0)
    for shift in range(1, seq_count):
        target = (seq_index + shift) % seq_count
        outgoing = lax.dynamic_slice_in_dim(my_rows, target * band, band, 1)
        route = [(j, (j + shift) % seq_count) for j in range(seq_count)]
        incoming, their_scale = lax.ppermute((outgoing, row_scale), "seq", route)
        halves = swap_halves(incoming, sub_count, sub_index)
        source = (seq_index - shift) % seq_count
        their_raw = lax.dynamic_slice_in_dim(raw_columns, source * row_count, row_count, 0)
        their_owned = (
            their_raw.astype(jnp.float32) * their_scale[:, None] * column_gain
        ).astype(jnp.bfloat16)
        for lane_shift in range(sub_count):
            half_at = (sub_index - lane_shift) % sub_count
            their_rows = lax.dynamic_slice_in_dim(their_owned, half_at * share, share, 0)
            gram_sum = gram_sum + jnp.einsum(
                "tc,tr->cr", halves[lane_shift], their_rows, preferred_element_type=jnp.float32
            )
    gram_sum = gram_sum * inverse_count
    gram_tile = gram_sum
    return (attended, gram_tile)


def solution(mesh):
    placed = (
        P(("grp", "seq"), ("kvh", "sub")),
        P(),
        P(None, "kvh", "sub"),
        P("sub", "kvh", None),
        P("sub", "kvh", None),
        P(),
    )
    return jax.shard_map(
        body,
        mesh=mesh,
        in_specs=placed,
        out_specs=(P(("grp", "seq"), "kvh", "sub"), P(("grp", "seq"), ("kvh", "sub"))),
        check_vma=False,
    )
```

```python
import math

import jax
import jax.numpy as jnp
from jax import lax
from jax.sharding import PartitionSpec as P

rope_base = 500000.0


def from_partner(block, axis, bit):
    count = lax.axis_size(axis)
    route = []
    for low in range(count):
        high = low | 1 << bit
        if high != low and high < count:
            route += [(low, high), (high, low)]
    return lax.ppermute(block, axis, route)


def swap_halves(pieces, count, index):
    whole = [None] * count
    whole[0] = pieces
    for shift in range(1, count):
        route = [(j, (j + shift) % count) for j in range(count)]
        whole[shift] = lax.ppermute(pieces, "sub", route)
    return whole


def split_send(blocks, axis, bit):
    count = lax.axis_size("sub")
    index = lax.axis_index("sub")
    share = blocks[0].shape[0] // count
    mine = tuple(lax.dynamic_slice_in_dim(b, index * share, share, 0) for b in blocks)
    got = from_partner(mine, axis, bit)
    whole = swap_halves(got, count, index)
    out = []
    for n, b in enumerate(blocks):
        full = jnp.zeros_like(b)
        for shift in range(count):
            source = (index - shift) % count
            full = lax.dynamic_update_slice_in_dim(full, whole[shift][n], source * share, 0)
        out.append(full)
    return tuple(out)


def rotate(vectors, positions):
    width = vectors.shape[-1]
    half = width // 2
    inverse = jnp.exp(jnp.arange(half, dtype=jnp.float32) * (-2.0 * math.log(rope_base) / width))
    angles = positions.astype(jnp.float32)[:, None] * inverse[None, :]
    shape = (angles.shape[0],) + (1,) * (vectors.ndim - 2) + (half,)
    cosine = jnp.cos(angles).reshape(shape)
    sine = jnp.sin(angles).reshape(shape)
    first = vectors[..., :half]
    second = vectors[..., half:]
    return jnp.concatenate(
        [first * cosine - second * sine, second * cosine + first * sine], axis=-1
    )


def body(tokens, norm_gain, w_query, w_key, w_value, links):
    kvh_total = lax.axis_size("kvh")
    kvh_at = lax.axis_index("kvh")
    sub_total = lax.axis_size("sub")
    lane_index = lax.axis_index("sub")
    across = [tokens]
    for shift in range(1, kvh_total):
        route = [(j, (j + shift) % kvh_total) for j in range(kvh_total)]
        across.append(lax.ppermute(tokens, "kvh", route))
    pieces = []
    for shift in range(kvh_total):
        pieces.extend(swap_halves(across[shift], sub_total, lane_index))
    blocks = []
    for owner_kvh in range(kvh_total):
        for owner_sub in range(sub_total):
            pick = ((kvh_at - owner_kvh) % kvh_total) * sub_total + (lane_index - owner_sub) % sub_total
            blocks.append(lax.select_n(pick, *pieces))
    gathered = jnp.concatenate(blocks, axis=1)
    widened = gathered.astype(jnp.float32)
    mean_square = jnp.mean(widened * widened, axis=-1, keepdims=True)
    row_scale = lax.rsqrt(mean_square + 1e-05)[:, 0]
    normed = (widened * row_scale[:, None] * norm_gain).astype(jnp.bfloat16)
    row_count = normed.shape[0]
    block_len = row_count // 2
    width = normed.shape[1]
    seq_index = lax.axis_index("seq")
    local_rows = jnp.arange(row_count, dtype=jnp.int32)
    positions = seq_index * row_count + local_rows
    head_size = w_key.shape[2]
    local_groups = w_key.shape[1]
    per_group = w_query.shape[2] // head_size
    queries = jnp.einsum("td,dgc->tgc", normed, w_query, preferred_element_type=jnp.float32)
    queries = rotate(
        queries.reshape(row_count, local_groups, per_group, head_size), positions
    ).astype(jnp.bfloat16)
    sub_count = lax.axis_size("sub")
    sub_index = lax.axis_index("sub")
    tile_count = lax.axis_size("kvh") * lax.axis_size("sub")
    tile_cols = width // tile_count
    owner_index = lax.axis_index("kvh") * lax.axis_size("sub") + lax.axis_index("sub")
    owned = lax.dynamic_slice_in_dim(normed, owner_index * tile_cols, tile_cols, 1)
    seq_count = lax.axis_size("seq")
    band = width // seq_count
    inverse_count = 1.0 / (row_count * seq_count)
    share = row_count // sub_count
    raw_parts = [tokens]
    for shift in range(1, seq_count):
        route = [(j, (j + shift) % seq_count) for j in range(seq_count)]
        raw_parts.append(lax.ppermute(tokens, "seq", route))
    column_gain = lax.dynamic_slice_in_dim(norm_gain, owner_index * tile_cols, tile_cols, 0)
    mine = lax.dynamic_slice_in_dim(normed, seq_index * band, band, 1)
    gram_sum = jnp.einsum("tc,tr->cr", mine, owned, preferred_element_type=jnp.float32)
    my_rows = lax.dynamic_slice_in_dim(normed, sub_index * share, share, 0)
    for shift in range(1, seq_count):
        target = (seq_index + shift) % seq_count
        outgoing = lax.dynamic_slice_in_dim(my_rows, target * band, band, 1)
        route = [(j, (j + shift) % seq_count) for j in range(seq_count)]
        incoming, their_scale = lax.ppermute((outgoing, row_scale), "seq", route)
        halves = swap_halves(incoming, sub_count, sub_index)
        source = (seq_index - shift) % seq_count
        their_raw = raw_parts[shift]
        their_owned = (
            their_raw.astype(jnp.float32) * their_scale[:, None] * column_gain
        ).astype(jnp.bfloat16)
        for lane_shift in range(sub_count):
            half_at = (sub_index - lane_shift) % sub_count
            their_rows = lax.dynamic_slice_in_dim(their_owned, half_at * share, share, 0)
            gram_sum = gram_sum + jnp.einsum(
                "tc,tr->cr", halves[lane_shift], their_rows, preferred_element_type=jnp.float32
            )
    gram_sum = gram_sum * inverse_count
    row_share = w_key.shape[0]
    key_more = None
    value_more = None
    for shift in range(sub_count):
        if shift == 0:
            key_part, value_part = w_key, w_value
        else:
            route = [(j, (j + shift) % sub_count) for j in range(sub_count)]
            key_part, value_part = lax.ppermute((w_key, w_value), "sub", route)
        source = (sub_index - shift) % sub_count
        rows = lax.dynamic_slice_in_dim(normed, source * row_share, row_share, 1)
        key_step = jnp.einsum("td,dgh->tgh", rows, key_part, preferred_element_type=jnp.float32)
        value_step = jnp.einsum("td,dgh->tgh", rows, value_part, preferred_element_type=jnp.float32)
        key_more = key_step if key_more is None else key_more + key_step
        value_more = value_step if value_more is None else value_more + value_step
    keys = rotate(key_more, positions).astype(jnp.bfloat16)
    values = value_more.astype(jnp.bfloat16)
    block_ids = seq_index * 2 + jnp.arange(2, dtype=jnp.int32)
    query_block = local_rows // block_len
    scale = 1.0 / math.sqrt(head_size)
    scores = jnp.einsum("tgrh,ugh->grtu", queries, keys, preferred_element_type=jnp.float32) * scale
    near_linked = lax.dynamic_slice_in_dim(links[0], seq_index * 2, 2) != block_ids
    same_block = query_block[:, None] == query_block[None, :]
    causal = same_block & (local_rows[None, :] <= local_rows[:, None])
    across = ~same_block & near_linked[query_block][:, None]
    allowed = causal | across
    scores = jnp.where(allowed[None, None], scores, -jnp.inf)
    running_max = jnp.max(scores, axis=-1)
    weights = jnp.exp(scores - running_max[..., None])
    total = jnp.sum(weights, axis=-1)
    accum = jnp.einsum(
        "grtu,ugh->tgrh", weights.astype(jnp.bfloat16), values, preferred_element_type=jnp.float32
    )
    query_pairs = queries.reshape(2, block_len, local_groups, per_group, head_size)
    for section in range(1, lax.axis_size("seq").bit_length()):
        far_keys, far_values = split_send((keys, values), "seq", section - 1)
        far_keys = far_keys.reshape(2, block_len, local_groups, head_size)
        far_values = far_values.reshape(2, block_len, local_groups, head_size)
        linked = lax.dynamic_slice_in_dim(links[section], seq_index * 2, 2) != block_ids
        offset = jnp.where(linked, 0.0, -1e30).astype(jnp.float32)[query_block]
        far_scores = jnp.einsum(
            "jtgrh,jugh->grjtu", query_pairs, far_keys, preferred_element_type=jnp.float32
        )
        far_scores = (
            far_scores.reshape(local_groups, per_group, row_count, block_len) * scale
            + offset[None, None, :, None]
        )
        new_max = jnp.maximum(running_max, jnp.max(far_scores, axis=-1))
        shrink = jnp.exp(running_max - new_max)
        far_weights = jnp.exp(far_scores - new_max[..., None])
        total = total * shrink + jnp.sum(far_weights, axis=-1)
        paired = far_weights.astype(jnp.bfloat16).reshape(
            local_groups, per_group, 2, block_len, block_len
        )
        far_sum = jnp.einsum(
            "grjtu,jugh->jtgrh", paired, far_values, preferred_element_type=jnp.float32
        )
        far_sum = far_sum.reshape(row_count, local_groups, per_group, head_size)
        accum = accum * jnp.transpose(shrink, (2, 0, 1))[..., None] + far_sum
        running_max = new_max
    attended = (accum / jnp.transpose(total, (2, 0, 1))[..., None]).astype(jnp.bfloat16)
    attended = attended.reshape(row_count, local_groups, per_group * head_size)
    gram_tile = gram_sum
    return (attended, gram_tile)


def solution(mesh):
    placed = (
        P(("grp", "seq"), ("kvh", "sub")),
        P(),
        P(None, "kvh", "sub"),
        P("sub", "kvh", None),
        P("sub", "kvh", None),
        P(),
    )
    return jax.shard_map(
        body,
        mesh=mesh,
        in_specs=placed,
        out_specs=(P(("grp", "seq"), "kvh", "sub"), P(("grp", "seq"), ("kvh", "sub"))),
        check_vma=False,
    )
```

```python
import math

import jax
import jax.numpy as jnp
from jax import lax
from jax.sharding import PartitionSpec as P

rope_base = 500000.0


def from_partner(block, axis, bit):
    count = lax.axis_size(axis)
    route = []
    for low in range(count):
        high = low | 1 << bit
        if high != low and high < count:
            route += [(low, high), (high, low)]
    return lax.ppermute(block, axis, route)


def swap_halves(pieces, count, index):
    whole = [None] * count
    whole[0] = pieces
    for shift in range(1, count):
        route = [(j, (j + shift) % count) for j in range(count)]
        whole[shift] = lax.ppermute(pieces, "sub", route)
    return whole


def split_send(blocks, axis, bit):
    count = lax.axis_size("sub")
    index = lax.axis_index("sub")
    share = blocks[0].shape[0] // count
    mine = tuple(lax.dynamic_slice_in_dim(b, index * share, share, 0) for b in blocks)
    got = from_partner(mine, axis, bit)
    whole = swap_halves(got, count, index)
    out = []
    for n, b in enumerate(blocks):
        full = jnp.zeros_like(b)
        for shift in range(count):
            source = (index - shift) % count
            full = lax.dynamic_update_slice_in_dim(full, whole[shift][n], source * share, 0)
        out.append(full)
    return tuple(out)


def rotate(vectors, positions):
    width = vectors.shape[-1]
    half = width // 2
    inverse = jnp.exp(jnp.arange(half, dtype=jnp.float32) * (-2.0 * math.log(rope_base) / width))
    angles = positions.astype(jnp.float32)[:, None] * inverse[None, :]
    shape = (angles.shape[0],) + (1,) * (vectors.ndim - 2) + (half,)
    cosine = jnp.cos(angles).reshape(shape)
    sine = jnp.sin(angles).reshape(shape)
    first = vectors[..., :half]
    second = vectors[..., half:]
    return jnp.concatenate(
        [first * cosine - second * sine, second * cosine + first * sine], axis=-1
    )


def body(tokens, norm_gain, w_query, w_key, w_value, links):
    kvh_total = lax.axis_size("kvh")
    kvh_at = lax.axis_index("kvh")
    sub_total = lax.axis_size("sub")
    lane_index = lax.axis_index("sub")
    across = [tokens]
    for shift in range(1, kvh_total):
        route = [(j, (j + shift) % kvh_total) for j in range(kvh_total)]
        across.append(lax.ppermute(tokens, "kvh", route))
    pieces = []
    for shift in range(kvh_total):
        pieces.extend(swap_halves(across[shift], sub_total, lane_index))
    blocks = []
    for owner_kvh in range(kvh_total):
        for owner_sub in range(sub_total):
            pick = ((kvh_at - owner_kvh) % kvh_total) * sub_total + (lane_index - owner_sub) % sub_total
            blocks.append(lax.select_n(pick, *pieces))
    gathered = jnp.concatenate(blocks, axis=1)
    widened = gathered.astype(jnp.float32)
    mean_square = jnp.mean(widened * widened, axis=-1, keepdims=True)
    row_scale = lax.rsqrt(mean_square + 1e-05)[:, 0]
    normed = (widened * row_scale[:, None] * norm_gain).astype(jnp.bfloat16)
    row_count = normed.shape[0]
    block_len = row_count // 2
    width = normed.shape[1]
    seq_index = lax.axis_index("seq")
    local_rows = jnp.arange(row_count, dtype=jnp.int32)
    positions = seq_index * row_count + local_rows
    head_size = w_key.shape[2]
    local_groups = w_key.shape[1]
    per_group = w_query.shape[2] // head_size
    queries = jnp.einsum("td,dgc->tgc", normed, w_query, preferred_element_type=jnp.float32)
    queries = rotate(
        queries.reshape(row_count, local_groups, per_group, head_size), positions
    ).astype(jnp.bfloat16)
    sub_count = lax.axis_size("sub")
    sub_index = lax.axis_index("sub")
    row_share = w_key.shape[0]
    key_more = None
    value_more = None
    for shift in range(sub_count):
        if shift == 0:
            key_part, value_part = w_key, w_value
        else:
            route = [(j, (j + shift) % sub_count) for j in range(sub_count)]
            weight_pair = lax.ppermute(jnp.stack([w_key, w_value]), "sub", route)
            key_part, value_part = weight_pair[0], weight_pair[1]
        source = (sub_index - shift) % sub_count
        rows = lax.dynamic_slice_in_dim(normed, source * row_share, row_share, 1)
        key_step = jnp.einsum("td,dgh->tgh", rows, key_part, preferred_element_type=jnp.float32)
        value_step = jnp.einsum("td,dgh->tgh", rows, value_part, preferred_element_type=jnp.float32)
        key_more = key_step if key_more is None else key_more + key_step
        value_more = value_step if value_more is None else value_more + value_step
    keys = rotate(key_more, positions).astype(jnp.bfloat16)
    values = value_more.astype(jnp.bfloat16)
    block_ids = seq_index * 2 + jnp.arange(2, dtype=jnp.int32)
    query_block = local_rows // block_len
    scale = 1.0 / math.sqrt(head_size)
    scores = jnp.einsum("tgrh,ugh->grtu", queries, keys, preferred_element_type=jnp.float32) * scale
    near_linked = lax.dynamic_slice_in_dim(links[0], seq_index * 2, 2) != block_ids
    same_block = query_block[:, None] == query_block[None, :]
    causal = same_block & (local_rows[None, :] <= local_rows[:, None])
    across = ~same_block & near_linked[query_block][:, None]
    allowed = causal | across
    scores = jnp.where(allowed[None, None], scores, -jnp.inf)
    running_max = jnp.max(scores, axis=-1)
    weights = jnp.exp(scores - running_max[..., None])
    total = jnp.sum(weights, axis=-1)
    accum = jnp.einsum(
        "grtu,ugh->tgrh", weights.astype(jnp.bfloat16), values, preferred_element_type=jnp.float32
    )
    query_pairs = queries.reshape(2, block_len, local_groups, per_group, head_size)
    for section in range(1, lax.axis_size("seq").bit_length()):
        (far_pair,) = split_send((jnp.stack([keys, values]).swapaxes(0, 1),), "seq", section - 1)
        far_keys = far_pair[:, 0]
        far_values = far_pair[:, 1]
        far_keys = far_keys.reshape(2, block_len, local_groups, head_size)
        far_values = far_values.reshape(2, block_len, local_groups, head_size)
        linked = lax.dynamic_slice_in_dim(links[section], seq_index * 2, 2) != block_ids
        offset = jnp.where(linked, 0.0, -1e30).astype(jnp.float32)[query_block]
        far_scores = jnp.einsum(
            "jtgrh,jugh->grjtu", query_pairs, far_keys, preferred_element_type=jnp.float32
        )
        far_scores = (
            far_scores.reshape(local_groups, per_group, row_count, block_len) * scale
            + offset[None, None, :, None]
        )
        new_max = jnp.maximum(running_max, jnp.max(far_scores, axis=-1))
        shrink = jnp.exp(running_max - new_max)
        far_weights = jnp.exp(far_scores - new_max[..., None])
        total = total * shrink + jnp.sum(far_weights, axis=-1)
        paired = far_weights.astype(jnp.bfloat16).reshape(
            local_groups, per_group, 2, block_len, block_len
        )
        far_sum = jnp.einsum(
            "grjtu,jugh->jtgrh", paired, far_values, preferred_element_type=jnp.float32
        )
        far_sum = far_sum.reshape(row_count, local_groups, per_group, head_size)
        accum = accum * jnp.transpose(shrink, (2, 0, 1))[..., None] + far_sum
        running_max = new_max
    attended = (accum / jnp.transpose(total, (2, 0, 1))[..., None]).astype(jnp.bfloat16)
    attended = attended.reshape(row_count, local_groups, per_group * head_size)
    tile_count = lax.axis_size("kvh") * lax.axis_size("sub")
    tile_cols = width // tile_count
    owner_index = lax.axis_index("kvh") * lax.axis_size("sub") + lax.axis_index("sub")
    owned = lax.dynamic_slice_in_dim(normed, owner_index * tile_cols, tile_cols, 1)
    seq_count = lax.axis_size("seq")
    band = width // seq_count
    inverse_count = 1.0 / (row_count * seq_count)
    share = row_count // sub_count
    raw_columns = lax.all_gather(tokens, "seq", axis=0, tiled=True)
    column_gain = lax.dynamic_slice_in_dim(norm_gain, owner_index * tile_cols, tile_cols, 0)
    mine = lax.dynamic_slice_in_dim(normed, seq_index * band, band, 1)
    gram_sum = jnp.einsum("tc,tr->cr", mine, owned, preferred_element_type=jnp.float32)
    my_rows = lax.dynamic_slice_in_dim(normed, sub_index * share, share, 0)
    for shift in range(1, seq_count):
        target = (seq_index + shift) % seq_count
        outgoing = lax.dynamic_slice_in_dim(my_rows, target * band, band, 1)
        route = [(j, (j + shift) % seq_count) for j in range(seq_count)]
        incoming, their_scale = lax.ppermute((outgoing, row_scale), "seq", route)
        halves = swap_halves(incoming, sub_count, sub_index)
        source = (seq_index - shift) % seq_count
        their_raw = lax.dynamic_slice_in_dim(raw_columns, source * row_count, row_count, 0)
        their_owned = (
            their_raw.astype(jnp.float32) * their_scale[:, None] * column_gain
        ).astype(jnp.bfloat16)
        for lane_shift in range(sub_count):
            half_at = (sub_index - lane_shift) % sub_count
            their_rows = lax.dynamic_slice_in_dim(their_owned, half_at * share, share, 0)
            gram_sum = gram_sum + jnp.einsum(
                "tc,tr->cr", halves[lane_shift], their_rows, preferred_element_type=jnp.float32
            )
    gram_sum = gram_sum * inverse_count
    gram_tile = gram_sum
    return (attended, gram_tile)


def solution(mesh):
    placed = (
        P(("grp", "seq"), ("kvh", "sub")),
        P(),
        P(None, "kvh", "sub"),
        P("sub", "kvh", None),
        P("sub", "kvh", None),
        P(),
    )
    return jax.shard_map(
        body,
        mesh=mesh,
        in_specs=placed,
        out_specs=(P(("grp", "seq"), "kvh", "sub"), P(("grp", "seq"), ("kvh", "sub"))),
        check_vma=False,
    )
```

```python
import math

import jax
import jax.numpy as jnp
from jax import lax
from jax.sharding import PartitionSpec as P

rope_base = 500000.0


def from_partner(block, axis, bit):
    count = lax.axis_size(axis)
    route = []
    for low in range(count):
        high = low | 1 << bit
        if high != low and high < count:
            route += [(low, high), (high, low)]
    return lax.ppermute(block, axis, route)


def swap_halves(pieces, count, index):
    whole = [None] * count
    whole[0] = pieces
    for shift in range(1, count):
        route = [(j, (j + shift) % count) for j in range(count)]
        whole[shift] = lax.ppermute(pieces, "sub", route)
    return whole


def split_send(blocks, axis, bit):
    count = lax.axis_size("sub")
    index = lax.axis_index("sub")
    share = blocks[0].shape[0] // count
    mine = tuple(lax.dynamic_slice_in_dim(b, index * share, share, 0) for b in blocks)
    got = from_partner(mine, axis, bit)
    whole = swap_halves(got, count, index)
    out = []
    for n, b in enumerate(blocks):
        full = jnp.zeros_like(b)
        for shift in range(count):
            source = (index - shift) % count
            full = lax.dynamic_update_slice_in_dim(full, whole[shift][n], source * share, 0)
        out.append(full)
    return tuple(out)


def rotate(vectors, positions):
    width = vectors.shape[-1]
    half = width // 2
    inverse = jnp.exp(jnp.arange(half, dtype=jnp.float32) * (-2.0 * math.log(rope_base) / width))
    angles = positions.astype(jnp.float32)[:, None] * inverse[None, :]
    shape = (angles.shape[0],) + (1,) * (vectors.ndim - 2) + (half,)
    cosine = jnp.cos(angles).reshape(shape)
    sine = jnp.sin(angles).reshape(shape)
    first = vectors[..., :half]
    second = vectors[..., half:]
    return jnp.concatenate(
        [first * cosine - second * sine, second * cosine + first * sine], axis=-1
    )


def body(tokens, norm_gain, w_query, w_key, w_value, links):
    kvh_total = lax.axis_size("kvh")
    kvh_at = lax.axis_index("kvh")
    sub_total = lax.axis_size("sub")
    lane_index = lax.axis_index("sub")
    across = [tokens]
    for shift in range(1, kvh_total):
        route = [(j, (j + shift) % kvh_total) for j in range(kvh_total)]
        across.append(lax.ppermute(tokens, "kvh", route))
    pieces = []
    for shift in range(kvh_total):
        pieces.extend(swap_halves(across[shift], sub_total, lane_index))
    blocks = []
    for owner_kvh in range(kvh_total):
        for owner_sub in range(sub_total):
            pick = ((kvh_at - owner_kvh) % kvh_total) * sub_total + (lane_index - owner_sub) % sub_total
            blocks.append(lax.select_n(pick, *pieces))
    gathered = jnp.concatenate(blocks, axis=1)
    widened = gathered.astype(jnp.float32)
    mean_square = jnp.mean(widened * widened, axis=-1, keepdims=True)
    row_scale = lax.rsqrt(mean_square + 1e-05)[:, 0]
    normed = (widened * row_scale[:, None] * norm_gain).astype(jnp.bfloat16)
    row_count = normed.shape[0]
    block_len = row_count // 2
    width = normed.shape[1]
    seq_index = lax.axis_index("seq")
    local_rows = jnp.arange(row_count, dtype=jnp.int32)
    positions = seq_index * row_count + local_rows
    head_size = w_key.shape[2]
    local_groups = w_key.shape[1]
    per_group = w_query.shape[2] // head_size
    queries = jnp.einsum("td,dgc->tgc", normed, w_query, preferred_element_type=jnp.float32)
    queries = rotate(
        queries.reshape(row_count, local_groups, per_group, head_size), positions
    ).astype(jnp.bfloat16)
    sub_count = lax.axis_size("sub")
    sub_index = lax.axis_index("sub")
    row_share = w_key.shape[0]
    key_more = None
    value_more = None
    for shift in range(sub_count):
        if shift == 0:
            key_part, value_part = w_key, w_value
        else:
            route = [(j, (j + shift) % sub_count) for j in range(sub_count)]
            weight_pair = lax.ppermute(jnp.stack([w_key, w_value]), "sub", route)
            key_part, value_part = weight_pair[0], weight_pair[1]
        source = (sub_index - shift) % sub_count
        rows = lax.dynamic_slice_in_dim(normed, source * row_share, row_share, 1)
        key_step = jnp.einsum("td,dgh->tgh", rows, key_part, preferred_element_type=jnp.float32)
        value_step = jnp.einsum("td,dgh->tgh", rows, value_part, preferred_element_type=jnp.float32)
        key_more = key_step if key_more is None else key_more + key_step
        value_more = value_step if value_more is None else value_more + value_step
    keys = rotate(key_more, positions).astype(jnp.bfloat16)
    values = value_more.astype(jnp.bfloat16)
    block_ids = seq_index * 2 + jnp.arange(2, dtype=jnp.int32)
    query_block = local_rows // block_len
    scale = 1.0 / math.sqrt(head_size)
    scores = jnp.einsum("tgrh,ugh->grtu", queries, keys, preferred_element_type=jnp.float32) * scale
    near_linked = lax.dynamic_slice_in_dim(links[0], seq_index * 2, 2) != block_ids
    same_block = query_block[:, None] == query_block[None, :]
    causal = same_block & (local_rows[None, :] <= local_rows[:, None])
    across = ~same_block & near_linked[query_block][:, None]
    allowed = causal | across
    scores = jnp.where(allowed[None, None], scores, -jnp.inf)
    running_max = jnp.max(scores, axis=-1)
    weights = jnp.exp(scores - running_max[..., None])
    total = jnp.sum(weights, axis=-1)
    accum = jnp.einsum(
        "grtu,ugh->tgrh", weights.astype(jnp.bfloat16), values, preferred_element_type=jnp.float32
    )
    query_pairs = queries.reshape(2, block_len, local_groups, per_group, head_size)
    for section in range(1, lax.axis_size("seq").bit_length()):
        (far_pair,) = split_send((jnp.stack([keys, values]).swapaxes(0, 1),), "seq", section - 1)
        far_keys = far_pair[:, 0]
        far_values = far_pair[:, 1]
        far_keys = far_keys.reshape(2, block_len, local_groups, head_size)
        far_values = far_values.reshape(2, block_len, local_groups, head_size)
        linked = lax.dynamic_slice_in_dim(links[section], seq_index * 2, 2) != block_ids
        offset = jnp.where(linked, 0.0, -1e30).astype(jnp.float32)[query_block]
        far_scores = jnp.einsum(
            "jtgrh,jugh->grjtu", query_pairs, far_keys, preferred_element_type=jnp.float32
        )
        far_scores = (
            far_scores.reshape(local_groups, per_group, row_count, block_len) * scale
            + offset[None, None, :, None]
        )
        new_max = jnp.maximum(running_max, jnp.max(far_scores, axis=-1))
        shrink = jnp.exp(running_max - new_max)
        far_weights = jnp.exp(far_scores - new_max[..., None])
        total = total * shrink + jnp.sum(far_weights, axis=-1)
        paired = far_weights.astype(jnp.bfloat16).reshape(
            local_groups, per_group, 2, block_len, block_len
        )
        far_sum = jnp.einsum(
            "grjtu,jugh->jtgrh", paired, far_values, preferred_element_type=jnp.float32
        )
        far_sum = far_sum.reshape(row_count, local_groups, per_group, head_size)
        accum = accum * jnp.transpose(shrink, (2, 0, 1))[..., None] + far_sum
        running_max = new_max
    attended = (accum / jnp.transpose(total, (2, 0, 1))[..., None]).astype(jnp.bfloat16)
    attended = attended.reshape(row_count, local_groups, per_group * head_size)
    tile_count = lax.axis_size("kvh") * lax.axis_size("sub")
    tile_cols = width // tile_count
    owner_index = lax.axis_index("kvh") * lax.axis_size("sub") + lax.axis_index("sub")
    owned = lax.dynamic_slice_in_dim(normed, owner_index * tile_cols, tile_cols, 1)
    seq_count = lax.axis_size("seq")
    band = width // seq_count
    inverse_count = 1.0 / (row_count * seq_count)
    share = row_count // sub_count
    raw_columns = lax.all_gather(tokens, "seq", axis=0, tiled=True)
    column_gain = lax.dynamic_slice_in_dim(norm_gain, owner_index * tile_cols, tile_cols, 0)
    mine = lax.dynamic_slice_in_dim(normed, seq_index * band, band, 1)
    gram_sum = jnp.einsum("tc,tr->cr", mine, owned, preferred_element_type=jnp.float32)
    my_rows = lax.dynamic_slice_in_dim(normed, sub_index * share, share, 0)
    my_scale = lax.dynamic_slice_in_dim(row_scale, sub_index * share, share, 0)
    scale_high = my_scale.astype(jnp.bfloat16)
    scale_rest = my_scale - scale_high.astype(jnp.float32)
    scale_mid = scale_rest.astype(jnp.bfloat16)
    scale_low = (scale_rest - scale_mid.astype(jnp.float32)).astype(jnp.bfloat16)
    scale_cols = jnp.stack([scale_high, scale_mid, scale_low], axis=1)
    for shift in range(1, seq_count):
        target = (seq_index + shift) % seq_count
        outgoing = lax.dynamic_slice_in_dim(my_rows, target * band, band, 1)
        outgoing = jnp.concatenate([outgoing, scale_cols], axis=1)
        route = [(j, (j + shift) % seq_count) for j in range(seq_count)]
        incoming = lax.ppermute(outgoing, "seq", route)
        halves = swap_halves(incoming, sub_count, sub_index)
        source = (seq_index - shift) % seq_count
        their_raw = lax.dynamic_slice_in_dim(raw_columns, source * row_count, row_count, 0)
        for lane_shift in range(sub_count):
            half_at = (sub_index - lane_shift) % sub_count
            got = halves[lane_shift]
            packed = got[:, band:].astype(jnp.float32)
            their_scale = (packed[:, 0] + packed[:, 1]) + packed[:, 2]
            raw_rows = lax.dynamic_slice_in_dim(their_raw, half_at * share, share, 0)
            their_rows = (
                raw_rows.astype(jnp.float32) * their_scale[:, None] * column_gain
            ).astype(jnp.bfloat16)
            gram_sum = gram_sum + jnp.einsum(
                "tc,tr->cr", got[:, :band], their_rows, preferred_element_type=jnp.float32
            )
    gram_sum = gram_sum * inverse_count
    gram_tile = gram_sum
    return (attended, gram_tile)


def solution(mesh):
    placed = (
        P(("grp", "seq"), ("kvh", "sub")),
        P(),
        P(None, "kvh", "sub"),
        P("sub", "kvh", None),
        P("sub", "kvh", None),
        P(),
    )
    return jax.shard_map(
        body,
        mesh=mesh,
        in_specs=placed,
        out_specs=(P(("grp", "seq"), "kvh", "sub"), P(("grp", "seq"), ("kvh", "sub"))),
        check_vma=False,
    )
```

```python
import math

import jax
import jax.numpy as jnp
from jax import lax
from jax.sharding import PartitionSpec as P

rope_base = 500000.0


def from_partner(block, axis, bit):
    count = lax.axis_size(axis)
    route = []
    for low in range(count):
        high = low | 1 << bit
        if high != low and high < count:
            route += [(low, high), (high, low)]
    return lax.ppermute(block, axis, route)


def swap_halves(pieces, count, index):
    whole = [None] * count
    whole[0] = pieces
    for shift in range(1, count):
        route = [(j, (j + shift) % count) for j in range(count)]
        whole[shift] = lax.ppermute(pieces, "sub", route)
    return whole


def split_send(blocks, axis, bit):
    count = lax.axis_size("sub")
    index = lax.axis_index("sub")
    share = blocks[0].shape[0] // count
    mine = tuple(lax.dynamic_slice_in_dim(b, index * share, share, 0) for b in blocks)
    got = from_partner(mine, axis, bit)
    whole = swap_halves(got, count, index)
    out = []
    for n, b in enumerate(blocks):
        full = jnp.zeros_like(b)
        for shift in range(count):
            source = (index - shift) % count
            full = lax.dynamic_update_slice_in_dim(full, whole[shift][n], source * share, 0)
        out.append(full)
    return tuple(out)


def xor_route(count, pattern):
    return [(j, j ^ pattern) for j in range(count) if (j ^ pattern) < count]


def send_with_rows(kv_pair, rows_out, pattern):
    count = lax.axis_size("sub")
    index = lax.axis_index("sub")
    share = kv_pair.shape[0] // count
    mine_kv = lax.dynamic_slice_in_dim(kv_pair, index * share, share, 0)
    kv_width = mine_kv.size // share
    packed = jnp.concatenate([mine_kv.reshape(share, kv_width), rows_out], axis=1)
    got = lax.ppermute(packed, "seq", xor_route(lax.axis_size("seq"), pattern))
    whole = swap_halves(got, count, index)
    full = jnp.zeros_like(kv_pair)
    for shift in range(count):
        source = (index - shift) % count
        part = whole[shift][:, :kv_width].reshape(mine_kv.shape)
        full = lax.dynamic_update_slice_in_dim(full, part, source * share, 0)
    return full, [w[:, kv_width:] for w in whole]


def rotate(vectors, positions):
    width = vectors.shape[-1]
    half = width // 2
    inverse = jnp.exp(jnp.arange(half, dtype=jnp.float32) * (-2.0 * math.log(rope_base) / width))
    angles = positions.astype(jnp.float32)[:, None] * inverse[None, :]
    shape = (angles.shape[0],) + (1,) * (vectors.ndim - 2) + (half,)
    cosine = jnp.cos(angles).reshape(shape)
    sine = jnp.sin(angles).reshape(shape)
    first = vectors[..., :half]
    second = vectors[..., half:]
    return jnp.concatenate(
        [first * cosine - second * sine, second * cosine + first * sine], axis=-1
    )


def body(tokens, norm_gain, w_query, w_key, w_value, links):
    kvh_total = lax.axis_size("kvh")
    kvh_at = lax.axis_index("kvh")
    sub_total = lax.axis_size("sub")
    lane_index = lax.axis_index("sub")
    across = [tokens]
    for shift in range(1, kvh_total):
        route = [(j, (j + shift) % kvh_total) for j in range(kvh_total)]
        across.append(lax.ppermute(tokens, "kvh", route))
    pieces = []
    for shift in range(kvh_total):
        pieces.extend(swap_halves(across[shift], sub_total, lane_index))
    blocks = []
    for owner_kvh in range(kvh_total):
        for owner_sub in range(sub_total):
            pick = ((kvh_at - owner_kvh) % kvh_total) * sub_total + (lane_index - owner_sub) % sub_total
            blocks.append(lax.select_n(pick, *pieces))
    gathered = jnp.concatenate(blocks, axis=1)
    widened = gathered.astype(jnp.float32)
    mean_square = jnp.mean(widened * widened, axis=-1, keepdims=True)
    row_scale = lax.rsqrt(mean_square + 1e-05)[:, 0]
    normed = (widened * row_scale[:, None] * norm_gain).astype(jnp.bfloat16)
    row_count = normed.shape[0]
    block_len = row_count // 2
    width = normed.shape[1]
    seq_index = lax.axis_index("seq")
    local_rows = jnp.arange(row_count, dtype=jnp.int32)
    positions = seq_index * row_count + local_rows
    head_size = w_key.shape[2]
    local_groups = w_key.shape[1]
    per_group = w_query.shape[2] // head_size
    queries = jnp.einsum("td,dgc->tgc", normed, w_query, preferred_element_type=jnp.float32)
    queries = rotate(
        queries.reshape(row_count, local_groups, per_group, head_size), positions
    ).astype(jnp.bfloat16)
    sub_count = lax.axis_size("sub")
    sub_index = lax.axis_index("sub")
    row_share = w_key.shape[0]
    key_more = None
    value_more = None
    for shift in range(sub_count):
        if shift == 0:
            key_part, value_part = w_key, w_value
        else:
            route = [(j, (j + shift) % sub_count) for j in range(sub_count)]
            weight_pair = lax.ppermute(jnp.stack([w_key, w_value]), "sub", route)
            key_part, value_part = weight_pair[0], weight_pair[1]
        source = (sub_index - shift) % sub_count
        rows = lax.dynamic_slice_in_dim(normed, source * row_share, row_share, 1)
        key_step = jnp.einsum("td,dgh->tgh", rows, key_part, preferred_element_type=jnp.float32)
        value_step = jnp.einsum("td,dgh->tgh", rows, value_part, preferred_element_type=jnp.float32)
        key_more = key_step if key_more is None else key_more + key_step
        value_more = value_step if value_more is None else value_more + value_step
    keys = rotate(key_more, positions).astype(jnp.bfloat16)
    values = value_more.astype(jnp.bfloat16)
    block_ids = seq_index * 2 + jnp.arange(2, dtype=jnp.int32)
    query_block = local_rows // block_len
    scale = 1.0 / math.sqrt(head_size)
    scores = jnp.einsum("tgrh,ugh->grtu", queries, keys, preferred_element_type=jnp.float32) * scale
    near_linked = lax.dynamic_slice_in_dim(links[0], seq_index * 2, 2) != block_ids
    same_block = query_block[:, None] == query_block[None, :]
    causal = same_block & (local_rows[None, :] <= local_rows[:, None])
    across = ~same_block & near_linked[query_block][:, None]
    allowed = causal | across
    scores = jnp.where(allowed[None, None], scores, -jnp.inf)
    running_max = jnp.max(scores, axis=-1)
    weights = jnp.exp(scores - running_max[..., None])
    total = jnp.sum(weights, axis=-1)
    accum = jnp.einsum(
        "grtu,ugh->tgrh", weights.astype(jnp.bfloat16), values, preferred_element_type=jnp.float32
    )
    query_pairs = queries.reshape(2, block_len, local_groups, per_group, head_size)
    seq_count = lax.axis_size("seq")
    band = width // seq_count
    share = row_count // sub_count
    my_rows = lax.dynamic_slice_in_dim(normed, sub_index * share, share, 0)
    kv_pair = jnp.stack([keys, values]).swapaxes(0, 1)
    carried = {}
    for section in range(1, seq_count.bit_length()):
        pattern = 1 << (section - 1)
        rider = lax.dynamic_slice_in_dim(my_rows, (seq_index ^ pattern) * band, band, 1)
        far_pair, carried[pattern] = send_with_rows(kv_pair, rider, pattern)
        far_keys = far_pair[:, 0]
        far_values = far_pair[:, 1]
        far_keys = far_keys.reshape(2, block_len, local_groups, head_size)
        far_values = far_values.reshape(2, block_len, local_groups, head_size)
        linked = lax.dynamic_slice_in_dim(links[section], seq_index * 2, 2) != block_ids
        offset = jnp.where(linked, 0.0, -1e30).astype(jnp.float32)[query_block]
        far_scores = jnp.einsum(
            "jtgrh,jugh->grjtu", query_pairs, far_keys, preferred_element_type=jnp.float32
        )
        far_scores = (
            far_scores.reshape(local_groups, per_group, row_count, block_len) * scale
            + offset[None, None, :, None]
        )
        new_max = jnp.maximum(running_max, jnp.max(far_scores, axis=-1))
        shrink = jnp.exp(running_max - new_max)
        far_weights = jnp.exp(far_scores - new_max[..., None])
        total = total * shrink + jnp.sum(far_weights, axis=-1)
        paired = far_weights.astype(jnp.bfloat16).reshape(
            local_groups, per_group, 2, block_len, block_len
        )
        far_sum = jnp.einsum(
            "grjtu,jugh->jtgrh", paired, far_values, preferred_element_type=jnp.float32
        )
        far_sum = far_sum.reshape(row_count, local_groups, per_group, head_size)
        accum = accum * jnp.transpose(shrink, (2, 0, 1))[..., None] + far_sum
        running_max = new_max
    attended = (accum / jnp.transpose(total, (2, 0, 1))[..., None]).astype(jnp.bfloat16)
    attended = attended.reshape(row_count, local_groups, per_group * head_size)
    tile_count = lax.axis_size("kvh") * lax.axis_size("sub")
    tile_cols = width // tile_count
    owner_index = lax.axis_index("kvh") * lax.axis_size("sub") + lax.axis_index("sub")
    owned = lax.dynamic_slice_in_dim(normed, owner_index * tile_cols, tile_cols, 1)
    seq_count = lax.axis_size("seq")
    band = width // seq_count
    inverse_count = 1.0 / (row_count * seq_count)
    share = row_count // sub_count
    raw_columns = lax.all_gather(tokens, "seq", axis=0, tiled=True)
    column_gain = lax.dynamic_slice_in_dim(norm_gain, owner_index * tile_cols, tile_cols, 0)
    mine = lax.dynamic_slice_in_dim(normed, seq_index * band, band, 1)
    gram_sum = jnp.einsum("tc,tr->cr", mine, owned, preferred_element_type=jnp.float32)
    for pattern in range(1, seq_count):
        route = xor_route(seq_count, pattern)
        their_scale = lax.ppermute(row_scale, "seq", route)
        if pattern in carried:
            halves = carried[pattern]
        else:
            outgoing = lax.dynamic_slice_in_dim(my_rows, (seq_index ^ pattern) * band, band, 1)
            incoming = lax.ppermute(outgoing, "seq", route)
            halves = swap_halves(incoming, sub_count, sub_index)
        source = seq_index ^ pattern
        their_raw = lax.dynamic_slice_in_dim(raw_columns, source * row_count, row_count, 0)
        their_owned = (
            their_raw.astype(jnp.float32) * their_scale[:, None] * column_gain
        ).astype(jnp.bfloat16)
        for lane_shift in range(sub_count):
            half_at = (sub_index - lane_shift) % sub_count
            their_rows = lax.dynamic_slice_in_dim(their_owned, half_at * share, share, 0)
            gram_sum = gram_sum + jnp.einsum(
                "tc,tr->cr", halves[lane_shift], their_rows, preferred_element_type=jnp.float32
            )
    gram_sum = gram_sum * inverse_count
    gram_tile = gram_sum
    return (attended, gram_tile)


def solution(mesh):
    placed = (
        P(("grp", "seq"), ("kvh", "sub")),
        P(),
        P(None, "kvh", "sub"),
        P("sub", "kvh", None),
        P("sub", "kvh", None),
        P(),
    )
    return jax.shard_map(
        body,
        mesh=mesh,
        in_specs=placed,
        out_specs=(P(("grp", "seq"), "kvh", "sub"), P(("grp", "seq"), ("kvh", "sub"))),
        check_vma=False,
    )
```

```python
import math

import jax
import jax.numpy as jnp
from jax import lax
from jax.sharding import PartitionSpec as P

rope_base = 500000.0


def from_partner(block, axis, bit):
    count = lax.axis_size(axis)
    route = []
    for low in range(count):
        high = low | 1 << bit
        if high != low and high < count:
            route += [(low, high), (high, low)]
    return lax.ppermute(block, axis, route)


def swap_halves(pieces, count, index):
    whole = [None] * count
    whole[0] = pieces
    for shift in range(1, count):
        route = [(j, (j + shift) % count) for j in range(count)]
        whole[shift] = lax.ppermute(pieces, "sub", route)
    return whole


def split_send(blocks, axis, bit):
    count = lax.axis_size("sub")
    index = lax.axis_index("sub")
    share = blocks[0].shape[0] // count
    mine = tuple(lax.dynamic_slice_in_dim(b, index * share, share, 0) for b in blocks)
    got = from_partner(mine, axis, bit)
    whole = swap_halves(got, count, index)
    out = []
    for n, b in enumerate(blocks):
        full = jnp.zeros_like(b)
        for shift in range(count):
            source = (index - shift) % count
            full = lax.dynamic_update_slice_in_dim(full, whole[shift][n], source * share, 0)
        out.append(full)
    return tuple(out)


def rotate(vectors, positions):
    width = vectors.shape[-1]
    half = width // 2
    inverse = jnp.exp(jnp.arange(half, dtype=jnp.float32) * (-2.0 * math.log(rope_base) / width))
    angles = positions.astype(jnp.float32)[:, None] * inverse[None, :]
    shape = (angles.shape[0],) + (1,) * (vectors.ndim - 2) + (half,)
    cosine = jnp.cos(angles).reshape(shape)
    sine = jnp.sin(angles).reshape(shape)
    first = vectors[..., :half]
    second = vectors[..., half:]
    return jnp.concatenate(
        [first * cosine - second * sine, second * cosine + first * sine], axis=-1
    )


def body(tokens, norm_gain, w_query, w_key, w_value, links):
    kvh_total = lax.axis_size("kvh")
    kvh_at = lax.axis_index("kvh")
    sub_total = lax.axis_size("sub")
    lane_index = lax.axis_index("sub")
    across = [tokens]
    for shift in range(1, kvh_total):
        route = [(j, (j + shift) % kvh_total) for j in range(kvh_total)]
        across.append(lax.ppermute(tokens, "kvh", route))
    pieces = []
    for shift in range(kvh_total):
        pieces.extend(swap_halves(across[shift], sub_total, lane_index))
    blocks = []
    for owner_kvh in range(kvh_total):
        for owner_sub in range(sub_total):
            pick = ((kvh_at - owner_kvh) % kvh_total) * sub_total + (lane_index - owner_sub) % sub_total
            blocks.append(lax.select_n(pick, *pieces))
    gathered = jnp.concatenate(blocks, axis=1)
    widened = gathered.astype(jnp.float32)
    mean_square = jnp.mean(widened * widened, axis=-1, keepdims=True)
    row_scale = lax.rsqrt(mean_square + 1e-05)[:, 0]
    normed = (widened * row_scale[:, None] * norm_gain).astype(jnp.bfloat16)
    row_count = normed.shape[0]
    block_len = row_count // 2
    width = normed.shape[1]
    seq_index = lax.axis_index("seq")
    local_rows = jnp.arange(row_count, dtype=jnp.int32)
    positions = seq_index * row_count + local_rows
    head_size = w_key.shape[2]
    local_groups = w_key.shape[1]
    per_group = w_query.shape[2] // head_size
    queries = jnp.einsum("td,dgc->tgc", normed, w_query, preferred_element_type=jnp.float32)
    queries = rotate(
        queries.reshape(row_count, local_groups, per_group, head_size), positions
    ).astype(jnp.bfloat16)
    sub_count = lax.axis_size("sub")
    sub_index = lax.axis_index("sub")
    row_share = w_key.shape[0]
    key_more = None
    value_more = None
    for shift in range(sub_count):
        if shift == 0:
            key_part, value_part = w_key, w_value
        else:
            route = [(j, (j + shift) % sub_count) for j in range(sub_count)]
            weight_pair = lax.ppermute(jnp.stack([w_key, w_value]), "sub", route)
            key_part, value_part = weight_pair[0], weight_pair[1]
        source = (sub_index - shift) % sub_count
        rows = lax.dynamic_slice_in_dim(normed, source * row_share, row_share, 1)
        key_step = jnp.einsum("td,dgh->tgh", rows, key_part, preferred_element_type=jnp.float32)
        value_step = jnp.einsum("td,dgh->tgh", rows, value_part, preferred_element_type=jnp.float32)
        key_more = key_step if key_more is None else key_more + key_step
        value_more = value_step if value_more is None else value_more + value_step
    keys = rotate(key_more, positions).astype(jnp.bfloat16)
    values = value_more.astype(jnp.bfloat16)
    block_ids = seq_index * 2 + jnp.arange(2, dtype=jnp.int32)
    query_block = local_rows // block_len
    scale = 1.0 / math.sqrt(head_size)
    scores = jnp.einsum("tgrh,ugh->grtu", queries, keys, preferred_element_type=jnp.float32) * scale
    near_linked = lax.dynamic_slice_in_dim(links[0], seq_index * 2, 2) != block_ids
    same_block = query_block[:, None] == query_block[None, :]
    causal = same_block & (local_rows[None, :] <= local_rows[:, None])
    across = ~same_block & near_linked[query_block][:, None]
    allowed = causal | across
    scores = jnp.where(allowed[None, None], scores, -jnp.inf)
    running_max = jnp.max(scores, axis=-1)
    weights = jnp.exp(scores - running_max[..., None])
    total = jnp.sum(weights, axis=-1)
    accum = jnp.einsum(
        "grtu,ugh->tgrh", weights.astype(jnp.bfloat16), values, preferred_element_type=jnp.float32
    )
    query_pairs = queries.reshape(2, block_len, local_groups, per_group, head_size)
    seq_count = lax.axis_size("seq")
    band = width // seq_count
    share = row_count // sub_count
    my_rows = lax.dynamic_slice_in_dim(normed, sub_index * share, share, 0)
    outgoing_rows = [
        lax.dynamic_slice_in_dim(my_rows, ((seq_index + shift) % seq_count) * band, band, 1)
        for shift in range(1, seq_count)
    ]
    kv_pair = jnp.stack([keys, values]).swapaxes(0, 1)
    outgoing_rows, kv_pair = lax.optimization_barrier((outgoing_rows, kv_pair))
    for section in range(1, seq_count.bit_length()):
        (far_pair,) = split_send((kv_pair,), "seq", section - 1)
        far_keys = far_pair[:, 0]
        far_values = far_pair[:, 1]
        far_keys = far_keys.reshape(2, block_len, local_groups, head_size)
        far_values = far_values.reshape(2, block_len, local_groups, head_size)
        linked = lax.dynamic_slice_in_dim(links[section], seq_index * 2, 2) != block_ids
        offset = jnp.where(linked, 0.0, -1e30).astype(jnp.float32)[query_block]
        far_scores = jnp.einsum(
            "jtgrh,jugh->grjtu", query_pairs, far_keys, preferred_element_type=jnp.float32
        )
        far_scores = (
            far_scores.reshape(local_groups, per_group, row_count, block_len) * scale
            + offset[None, None, :, None]
        )
        new_max = jnp.maximum(running_max, jnp.max(far_scores, axis=-1))
        shrink = jnp.exp(running_max - new_max)
        far_weights = jnp.exp(far_scores - new_max[..., None])
        total = total * shrink + jnp.sum(far_weights, axis=-1)
        paired = far_weights.astype(jnp.bfloat16).reshape(
            local_groups, per_group, 2, block_len, block_len
        )
        far_sum = jnp.einsum(
            "grjtu,jugh->jtgrh", paired, far_values, preferred_element_type=jnp.float32
        )
        far_sum = far_sum.reshape(row_count, local_groups, per_group, head_size)
        accum = accum * jnp.transpose(shrink, (2, 0, 1))[..., None] + far_sum
        running_max = new_max
    attended = (accum / jnp.transpose(total, (2, 0, 1))[..., None]).astype(jnp.bfloat16)
    attended = attended.reshape(row_count, local_groups, per_group * head_size)
    tile_count = lax.axis_size("kvh") * lax.axis_size("sub")
    tile_cols = width // tile_count
    owner_index = lax.axis_index("kvh") * lax.axis_size("sub") + lax.axis_index("sub")
    owned = lax.dynamic_slice_in_dim(normed, owner_index * tile_cols, tile_cols, 1)
    seq_count = lax.axis_size("seq")
    band = width // seq_count
    inverse_count = 1.0 / (row_count * seq_count)
    share = row_count // sub_count
    raw_columns = lax.all_gather(tokens, "seq", axis=0, tiled=True)
    column_gain = lax.dynamic_slice_in_dim(norm_gain, owner_index * tile_cols, tile_cols, 0)
    mine = lax.dynamic_slice_in_dim(normed, seq_index * band, band, 1)
    gram_sum = jnp.einsum("tc,tr->cr", mine, owned, preferred_element_type=jnp.float32)
    for shift in range(1, seq_count):
        outgoing = outgoing_rows[shift - 1]
        route = [(j, (j + shift) % seq_count) for j in range(seq_count)]
        incoming, their_scale = lax.ppermute((outgoing, row_scale), "seq", route)
        halves = swap_halves(incoming, sub_count, sub_index)
        source = (seq_index - shift) % seq_count
        their_raw = lax.dynamic_slice_in_dim(raw_columns, source * row_count, row_count, 0)
        their_owned = (
            their_raw.astype(jnp.float32) * their_scale[:, None] * column_gain
        ).astype(jnp.bfloat16)
        for lane_shift in range(sub_count):
            half_at = (sub_index - lane_shift) % sub_count
            their_rows = lax.dynamic_slice_in_dim(their_owned, half_at * share, share, 0)
            gram_sum = gram_sum + jnp.einsum(
                "tc,tr->cr", halves[lane_shift], their_rows, preferred_element_type=jnp.float32
            )
    gram_sum = gram_sum * inverse_count
    gram_tile = gram_sum
    return (attended, gram_tile)


def solution(mesh):
    placed = (
        P(("grp", "seq"), ("kvh", "sub")),
        P(),
        P(None, "kvh", "sub"),
        P("sub", "kvh", None),
        P("sub", "kvh", None),
        P(),
    )
    return jax.shard_map(
        body,
        mesh=mesh,
        in_specs=placed,
        out_specs=(P(("grp", "seq"), "kvh", "sub"), P(("grp", "seq"), ("kvh", "sub"))),
        check_vma=False,
    )
```

```python
import math

import jax
import jax.numpy as jnp
from jax import lax
from jax.sharding import PartitionSpec as P

rope_base = 500000.0


def from_partner(block, axis, bit):
    count = lax.axis_size(axis)
    route = []
    for low in range(count):
        high = low | 1 << bit
        if high != low and high < count:
            route += [(low, high), (high, low)]
    return lax.ppermute(block, axis, route)


def swap_halves(pieces, count, index):
    whole = [None] * count
    whole[0] = pieces
    for shift in range(1, count):
        route = [(j, (j + shift) % count) for j in range(count)]
        whole[shift] = lax.ppermute(pieces, "sub", route)
    return whole


def split_send(blocks, axis, bit):
    count = lax.axis_size("sub")
    index = lax.axis_index("sub")
    share = blocks[0].shape[0] // count
    mine = tuple(lax.dynamic_slice_in_dim(b, index * share, share, 0) for b in blocks)
    got = from_partner(mine, axis, bit)
    whole = swap_halves(got, count, index)
    out = []
    for n, b in enumerate(blocks):
        full = jnp.zeros_like(b)
        for shift in range(count):
            source = (index - shift) % count
            full = lax.dynamic_update_slice_in_dim(full, whole[shift][n], source * share, 0)
        out.append(full)
    return tuple(out)


def rotate(vectors, positions):
    width = vectors.shape[-1]
    half = width // 2
    inverse = jnp.exp(jnp.arange(half, dtype=jnp.float32) * (-2.0 * math.log(rope_base) / width))
    angles = positions.astype(jnp.float32)[:, None] * inverse[None, :]
    shape = (angles.shape[0],) + (1,) * (vectors.ndim - 2) + (half,)
    cosine = jnp.cos(angles).reshape(shape)
    sine = jnp.sin(angles).reshape(shape)
    first = vectors[..., :half]
    second = vectors[..., half:]
    return jnp.concatenate(
        [first * cosine - second * sine, second * cosine + first * sine], axis=-1
    )


def body(tokens, norm_gain, w_query, w_key, w_value, links):
    kvh_total = lax.axis_size("kvh")
    kvh_at = lax.axis_index("kvh")
    sub_total = lax.axis_size("sub")
    lane_index = lax.axis_index("sub")
    across = [tokens]
    for shift in range(1, kvh_total):
        route = [(j, (j + shift) % kvh_total) for j in range(kvh_total)]
        across.append(lax.ppermute(tokens, "kvh", route))
    pieces = []
    for shift in range(kvh_total):
        pieces.extend(swap_halves(across[shift], sub_total, lane_index))
    blocks = []
    for owner_kvh in range(kvh_total):
        for owner_sub in range(sub_total):
            pick = ((kvh_at - owner_kvh) % kvh_total) * sub_total + (lane_index - owner_sub) % sub_total
            blocks.append(lax.select_n(pick, *pieces))
    gathered = jnp.concatenate(blocks, axis=1)
    widened = gathered.astype(jnp.float32)
    mean_square = jnp.mean(widened * widened, axis=-1, keepdims=True)
    row_scale = lax.rsqrt(mean_square + 1e-05)[:, 0]
    normed = (widened * row_scale[:, None] * norm_gain).astype(jnp.bfloat16)
    row_count = normed.shape[0]
    block_len = row_count // 2
    width = normed.shape[1]
    seq_index = lax.axis_index("seq")
    local_rows = jnp.arange(row_count, dtype=jnp.int32)
    positions = seq_index * row_count + local_rows
    head_size = w_key.shape[2]
    local_groups = w_key.shape[1]
    per_group = w_query.shape[2] // head_size
    queries = jnp.einsum("td,dgc->tgc", normed, w_query, preferred_element_type=jnp.float32)
    queries = rotate(
        queries.reshape(row_count, local_groups, per_group, head_size), positions
    ).astype(jnp.bfloat16)
    sub_count = lax.axis_size("sub")
    sub_index = lax.axis_index("sub")
    row_share = w_key.shape[0]
    key_more = None
    value_more = None
    for shift in range(sub_count):
        if shift == 0:
            key_part, value_part = w_key, w_value
        else:
            route = [(j, (j + shift) % sub_count) for j in range(sub_count)]
            weight_pair = lax.ppermute(jnp.stack([w_key, w_value]), "sub", route)
            key_part, value_part = weight_pair[0], weight_pair[1]
        source = (sub_index - shift) % sub_count
        rows = lax.dynamic_slice_in_dim(normed, source * row_share, row_share, 1)
        key_step = jnp.einsum("td,dgh->tgh", rows, key_part, preferred_element_type=jnp.float32)
        value_step = jnp.einsum("td,dgh->tgh", rows, value_part, preferred_element_type=jnp.float32)
        key_more = key_step if key_more is None else key_more + key_step
        value_more = value_step if value_more is None else value_more + value_step
    keys = rotate(key_more, positions).astype(jnp.bfloat16)
    values = value_more.astype(jnp.bfloat16)
    block_ids = seq_index * 2 + jnp.arange(2, dtype=jnp.int32)
    query_block = local_rows // block_len
    scale = 1.0 / math.sqrt(head_size)
    scores = jnp.einsum("tgrh,ugh->grtu", queries, keys, preferred_element_type=jnp.float32) * scale
    near_linked = lax.dynamic_slice_in_dim(links[0], seq_index * 2, 2) != block_ids
    same_block = query_block[:, None] == query_block[None, :]
    causal = same_block & (local_rows[None, :] <= local_rows[:, None])
    across = ~same_block & near_linked[query_block][:, None]
    allowed = causal | across
    scores = jnp.where(allowed[None, None], scores, -jnp.inf)
    running_max = jnp.max(scores, axis=-1)
    weights = jnp.exp(scores - running_max[..., None])
    total = jnp.sum(weights, axis=-1)
    accum = jnp.einsum(
        "grtu,ugh->tgrh", weights.astype(jnp.bfloat16), values, preferred_element_type=jnp.float32
    )
    query_pairs = queries.reshape(2, block_len, local_groups, per_group, head_size)
    seq_count = lax.axis_size("seq")
    band = width // seq_count
    share = row_count // sub_count
    my_rows = lax.dynamic_slice_in_dim(normed, sub_index * share, share, 0)
    outgoing_rows = [
        lax.dynamic_slice_in_dim(my_rows, ((seq_index + shift) % seq_count) * band, band, 1)
        for shift in range(1, seq_count)
    ]
    kv_pair = jnp.stack([keys, values]).swapaxes(0, 1)
    received_scales = [
        lax.ppermute(row_scale, "seq", [(j, (j + shift) % seq_count) for j in range(seq_count)])
        for shift in range(1, seq_count)
    ]
    outgoing_rows, received_scales, kv_pair = lax.optimization_barrier(
        (outgoing_rows, received_scales, kv_pair)
    )
    for section in range(1, seq_count.bit_length()):
        (far_pair,) = split_send((kv_pair,), "seq", section - 1)
        far_keys = far_pair[:, 0]
        far_values = far_pair[:, 1]
        far_keys = far_keys.reshape(2, block_len, local_groups, head_size)
        far_values = far_values.reshape(2, block_len, local_groups, head_size)
        linked = lax.dynamic_slice_in_dim(links[section], seq_index * 2, 2) != block_ids
        offset = jnp.where(linked, 0.0, -1e30).astype(jnp.float32)[query_block]
        far_scores = jnp.einsum(
            "jtgrh,jugh->grjtu", query_pairs, far_keys, preferred_element_type=jnp.float32
        )
        far_scores = (
            far_scores.reshape(local_groups, per_group, row_count, block_len) * scale
            + offset[None, None, :, None]
        )
        new_max = jnp.maximum(running_max, jnp.max(far_scores, axis=-1))
        shrink = jnp.exp(running_max - new_max)
        far_weights = jnp.exp(far_scores - new_max[..., None])
        total = total * shrink + jnp.sum(far_weights, axis=-1)
        paired = far_weights.astype(jnp.bfloat16).reshape(
            local_groups, per_group, 2, block_len, block_len
        )
        far_sum = jnp.einsum(
            "grjtu,jugh->jtgrh", paired, far_values, preferred_element_type=jnp.float32
        )
        far_sum = far_sum.reshape(row_count, local_groups, per_group, head_size)
        accum = accum * jnp.transpose(shrink, (2, 0, 1))[..., None] + far_sum
        running_max = new_max
    attended = (accum / jnp.transpose(total, (2, 0, 1))[..., None]).astype(jnp.bfloat16)
    attended = attended.reshape(row_count, local_groups, per_group * head_size)
    tile_count = lax.axis_size("kvh") * lax.axis_size("sub")
    tile_cols = width // tile_count
    owner_index = lax.axis_index("kvh") * lax.axis_size("sub") + lax.axis_index("sub")
    owned = lax.dynamic_slice_in_dim(normed, owner_index * tile_cols, tile_cols, 1)
    seq_count = lax.axis_size("seq")
    band = width // seq_count
    inverse_count = 1.0 / (row_count * seq_count)
    share = row_count // sub_count
    raw_columns = lax.all_gather(tokens, "seq", axis=0, tiled=True)
    column_gain = lax.dynamic_slice_in_dim(norm_gain, owner_index * tile_cols, tile_cols, 0)
    mine = lax.dynamic_slice_in_dim(normed, seq_index * band, band, 1)
    gram_sum = jnp.einsum("tc,tr->cr", mine, owned, preferred_element_type=jnp.float32)
    for shift in range(1, seq_count):
        outgoing = outgoing_rows[shift - 1]
        route = [(j, (j + shift) % seq_count) for j in range(seq_count)]
        incoming = lax.ppermute(outgoing, "seq", route)
        their_scale = received_scales[shift - 1]
        halves = swap_halves(incoming, sub_count, sub_index)
        source = (seq_index - shift) % seq_count
        their_raw = lax.dynamic_slice_in_dim(raw_columns, source * row_count, row_count, 0)
        their_owned = (
            their_raw.astype(jnp.float32) * their_scale[:, None] * column_gain
        ).astype(jnp.bfloat16)
        for lane_shift in range(sub_count):
            half_at = (sub_index - lane_shift) % sub_count
            their_rows = lax.dynamic_slice_in_dim(their_owned, half_at * share, share, 0)
            gram_sum = gram_sum + jnp.einsum(
                "tc,tr->cr", halves[lane_shift], their_rows, preferred_element_type=jnp.float32
            )
    gram_sum = gram_sum * inverse_count
    gram_tile = gram_sum
    return (attended, gram_tile)


def solution(mesh):
    placed = (
        P(("grp", "seq"), ("kvh", "sub")),
        P(),
        P(None, "kvh", "sub"),
        P("sub", "kvh", None),
        P("sub", "kvh", None),
        P(),
    )
    return jax.shard_map(
        body,
        mesh=mesh,
        in_specs=placed,
        out_specs=(P(("grp", "seq"), "kvh", "sub"), P(("grp", "seq"), ("kvh", "sub"))),
        check_vma=False,
    )
```

```python
import math

import jax
import jax.numpy as jnp
from jax import lax
from jax.sharding import PartitionSpec as P

rope_base = 500000.0


def from_partner(block, axis, bit):
    count = lax.axis_size(axis)
    route = []
    for low in range(count):
        high = low | 1 << bit
        if high != low and high < count:
            route += [(low, high), (high, low)]
    return lax.ppermute(block, axis, route)


def swap_halves(pieces, count, index):
    whole = [None] * count
    whole[0] = pieces
    for shift in range(1, count):
        route = [(j, (j + shift) % count) for j in range(count)]
        whole[shift] = lax.ppermute(pieces, "sub", route)
    return whole


def split_send(blocks, axis, bit):
    count = lax.axis_size("sub")
    index = lax.axis_index("sub")
    share = blocks[0].shape[0] // count
    mine = tuple(lax.dynamic_slice_in_dim(b, index * share, share, 0) for b in blocks)
    got = from_partner(mine, axis, bit)
    whole = swap_halves(got, count, index)
    out = []
    for n, b in enumerate(blocks):
        full = jnp.zeros_like(b)
        for shift in range(count):
            source = (index - shift) % count
            full = lax.dynamic_update_slice_in_dim(full, whole[shift][n], source * share, 0)
        out.append(full)
    return tuple(out)


def rotate(vectors, positions):
    width = vectors.shape[-1]
    half = width // 2
    inverse = jnp.exp(jnp.arange(half, dtype=jnp.float32) * (-2.0 * math.log(rope_base) / width))
    angles = positions.astype(jnp.float32)[:, None] * inverse[None, :]
    shape = (angles.shape[0],) + (1,) * (vectors.ndim - 2) + (half,)
    cosine = jnp.cos(angles).reshape(shape)
    sine = jnp.sin(angles).reshape(shape)
    first = vectors[..., :half]
    second = vectors[..., half:]
    return jnp.concatenate(
        [first * cosine - second * sine, second * cosine + first * sine], axis=-1
    )


def body(tokens, norm_gain, w_query, w_key, w_value, links):
    kvh_total = lax.axis_size("kvh")
    kvh_at = lax.axis_index("kvh")
    sub_total = lax.axis_size("sub")
    lane_index = lax.axis_index("sub")
    across = [tokens]
    for shift in range(1, kvh_total):
        route = [(j, (j + shift) % kvh_total) for j in range(kvh_total)]
        across.append(lax.ppermute(tokens, "kvh", route))
    pieces = []
    for shift in range(kvh_total):
        pieces.extend(swap_halves(across[shift], sub_total, lane_index))
    blocks = []
    for owner_kvh in range(kvh_total):
        for owner_sub in range(sub_total):
            pick = ((kvh_at - owner_kvh) % kvh_total) * sub_total + (lane_index - owner_sub) % sub_total
            blocks.append(lax.select_n(pick, *pieces))
    gathered = jnp.concatenate(blocks, axis=1)
    widened = gathered.astype(jnp.float32)
    mean_square = jnp.mean(widened * widened, axis=-1, keepdims=True)
    row_scale = lax.rsqrt(mean_square + 1e-05)[:, 0]
    normed = (widened * row_scale[:, None] * norm_gain).astype(jnp.bfloat16)
    row_count = normed.shape[0]
    block_len = row_count // 2
    width = normed.shape[1]
    seq_index = lax.axis_index("seq")
    local_rows = jnp.arange(row_count, dtype=jnp.int32)
    positions = seq_index * row_count + local_rows
    head_size = w_key.shape[2]
    local_groups = w_key.shape[1]
    per_group = w_query.shape[2] // head_size
    queries = jnp.einsum("td,dgc->tgc", normed, w_query, preferred_element_type=jnp.float32)
    queries = rotate(
        queries.reshape(row_count, local_groups, per_group, head_size), positions
    ).astype(jnp.bfloat16)
    sub_count = lax.axis_size("sub")
    sub_index = lax.axis_index("sub")
    row_share = w_key.shape[0]
    key_more = None
    value_more = None
    for shift in range(sub_count):
        if shift == 0:
            key_part, value_part = w_key, w_value
        else:
            route = [(j, (j + shift) % sub_count) for j in range(sub_count)]
            weight_pair = lax.ppermute(jnp.stack([w_key, w_value]), "sub", route)
            key_part, value_part = weight_pair[0], weight_pair[1]
        source = (sub_index - shift) % sub_count
        rows = lax.dynamic_slice_in_dim(normed, source * row_share, row_share, 1)
        key_step = jnp.einsum("td,dgh->tgh", rows, key_part, preferred_element_type=jnp.float32)
        value_step = jnp.einsum("td,dgh->tgh", rows, value_part, preferred_element_type=jnp.float32)
        key_more = key_step if key_more is None else key_more + key_step
        value_more = value_step if value_more is None else value_more + value_step
    keys = rotate(key_more, positions).astype(jnp.bfloat16)
    values = value_more.astype(jnp.bfloat16)
    block_ids = seq_index * 2 + jnp.arange(2, dtype=jnp.int32)
    query_block = local_rows // block_len
    scale = 1.0 / math.sqrt(head_size)
    scores = jnp.einsum("tgrh,ugh->grtu", queries, keys, preferred_element_type=jnp.float32) * scale
    near_linked = lax.dynamic_slice_in_dim(links[0], seq_index * 2, 2) != block_ids
    same_block = query_block[:, None] == query_block[None, :]
    causal = same_block & (local_rows[None, :] <= local_rows[:, None])
    across = ~same_block & near_linked[query_block][:, None]
    allowed = causal | across
    scores = jnp.where(allowed[None, None], scores, -jnp.inf)
    running_max = jnp.max(scores, axis=-1)
    weights = jnp.exp(scores - running_max[..., None])
    total = jnp.sum(weights, axis=-1)
    accum = jnp.einsum(
        "grtu,ugh->tgrh", weights.astype(jnp.bfloat16), values, preferred_element_type=jnp.float32
    )
    query_pairs = queries.reshape(2, block_len, local_groups, per_group, head_size)
    for section in range(1, lax.axis_size("seq").bit_length()):
        (far_pair,) = split_send((jnp.stack([keys, values]).swapaxes(0, 1),), "seq", section - 1)
        far_keys = far_pair[:, 0]
        far_values = far_pair[:, 1]
        far_keys = far_keys.reshape(2, block_len, local_groups, head_size)
        far_values = far_values.reshape(2, block_len, local_groups, head_size)
        linked = lax.dynamic_slice_in_dim(links[section], seq_index * 2, 2) != block_ids
        offset = jnp.where(linked, 0.0, -1e30).astype(jnp.float32)[query_block]
        far_scores = jnp.einsum(
            "jtgrh,jugh->grjtu", query_pairs, far_keys, preferred_element_type=jnp.float32
        )
        far_scores = (
            far_scores.reshape(local_groups, per_group, row_count, block_len) * scale
            + offset[None, None, :, None]
        )
        new_max = jnp.maximum(running_max, jnp.max(far_scores, axis=-1))
        shrink = jnp.exp(running_max - new_max)
        far_weights = jnp.exp(far_scores - new_max[..., None])
        total = total * shrink + jnp.sum(far_weights, axis=-1)
        paired = far_weights.astype(jnp.bfloat16).reshape(
            local_groups, per_group, 2, block_len, block_len
        )
        far_sum = jnp.einsum(
            "grjtu,jugh->jtgrh", paired, far_values, preferred_element_type=jnp.float32
        )
        far_sum = far_sum.reshape(row_count, local_groups, per_group, head_size)
        accum = accum * jnp.transpose(shrink, (2, 0, 1))[..., None] + far_sum
        running_max = new_max
    attended = (accum / jnp.transpose(total, (2, 0, 1))[..., None]).astype(jnp.bfloat16)
    attended = attended.reshape(row_count, local_groups, per_group * head_size)
    tile_count = lax.axis_size("kvh") * lax.axis_size("sub")
    tile_cols = width // tile_count
    owner_index = lax.axis_index("kvh") * lax.axis_size("sub") + lax.axis_index("sub")
    owned = lax.dynamic_slice_in_dim(normed, owner_index * tile_cols, tile_cols, 1)
    seq_count = lax.axis_size("seq")
    band = width // seq_count
    inverse_count = 1.0 / (row_count * seq_count)
    share = row_count // sub_count
    raw_columns = lax.all_gather(tokens, "seq", axis=0, tiled=True)
    column_gain = lax.dynamic_slice_in_dim(norm_gain, owner_index * tile_cols, tile_cols, 0)
    mine = lax.dynamic_slice_in_dim(normed, seq_index * band, band, 1)
    gram_sum = jnp.einsum("tc,tr->cr", mine, owned, preferred_element_type=jnp.float32)
    lane_count = kvh_total * sub_count
    part = row_count // lane_count
    lane_id = kvh_at * sub_count + sub_index
    my_rows = lax.dynamic_slice_in_dim(normed, lane_id * part, part, 0)
    for shift in range(1, seq_count):
        target = (seq_index + shift) % seq_count
        outgoing = lax.dynamic_slice_in_dim(my_rows, target * band, band, 1)
        route = [(j, (j + shift) % seq_count) for j in range(seq_count)]
        incoming, their_scale = lax.ppermute((outgoing, row_scale), "seq", route)
        source = (seq_index - shift) % seq_count
        their_raw = lax.dynamic_slice_in_dim(raw_columns, source * row_count, row_count, 0)
        their_owned = (
            their_raw.astype(jnp.float32) * their_scale[:, None] * column_gain
        ).astype(jnp.bfloat16)
        across = [incoming]
        for kvh_shift in range(1, kvh_total):
            kvh_route = [(j, (j + kvh_shift) % kvh_total) for j in range(kvh_total)]
            across.append(lax.ppermute(incoming, "kvh", kvh_route))
        for kvh_shift in range(kvh_total):
            quarters = swap_halves(across[kvh_shift], sub_count, sub_index)
            for lane_shift in range(sub_count):
                source_lane = ((kvh_at - kvh_shift) % kvh_total) * sub_count + (
                    sub_index - lane_shift
                ) % sub_count
                their_rows = lax.dynamic_slice_in_dim(their_owned, source_lane * part, part, 0)
                gram_sum = gram_sum + jnp.einsum(
                    "tc,tr->cr", quarters[lane_shift], their_rows, preferred_element_type=jnp.float32
                )
    gram_sum = gram_sum * inverse_count
    gram_tile = gram_sum
    return (attended, gram_tile)


def solution(mesh):
    placed = (
        P(("grp", "seq"), ("kvh", "sub")),
        P(),
        P(None, "kvh", "sub"),
        P("sub", "kvh", None),
        P("sub", "kvh", None),
        P(),
    )
    return jax.shard_map(
        body,
        mesh=mesh,
        in_specs=placed,
        out_specs=(P(("grp", "seq"), "kvh", "sub"), P(("grp", "seq"), ("kvh", "sub"))),
        check_vma=False,
    )
```

```python
import math

import jax
import jax.numpy as jnp
from jax import lax
from jax.sharding import PartitionSpec as P

rope_base = 500000.0


def from_partner(block, axis, bit):
    count = lax.axis_size(axis)
    route = []
    for low in range(count):
        high = low | 1 << bit
        if high != low and high < count:
            route += [(low, high), (high, low)]
    return lax.ppermute(block, axis, route)


def swap_halves(pieces, count, index):
    whole = [None] * count
    whole[0] = pieces
    for shift in range(1, count):
        route = [(j, (j + shift) % count) for j in range(count)]
        whole[shift] = lax.ppermute(pieces, "sub", route)
    return whole


def split_send(blocks, axis, bit):
    count = lax.axis_size("sub")
    index = lax.axis_index("sub")
    share = blocks[0].shape[0] // count
    mine = tuple(lax.dynamic_slice_in_dim(b, index * share, share, 0) for b in blocks)
    got = from_partner(mine, axis, bit)
    whole = swap_halves(got, count, index)
    out = []
    for n, b in enumerate(blocks):
        full = jnp.zeros_like(b)
        for shift in range(count):
            source = (index - shift) % count
            full = lax.dynamic_update_slice_in_dim(full, whole[shift][n], source * share, 0)
        out.append(full)
    return tuple(out)


def rotate(vectors, positions):
    width = vectors.shape[-1]
    half = width // 2
    inverse = jnp.exp(jnp.arange(half, dtype=jnp.float32) * (-2.0 * math.log(rope_base) / width))
    angles = positions.astype(jnp.float32)[:, None] * inverse[None, :]
    shape = (angles.shape[0],) + (1,) * (vectors.ndim - 2) + (half,)
    cosine = jnp.cos(angles).reshape(shape)
    sine = jnp.sin(angles).reshape(shape)
    first = vectors[..., :half]
    second = vectors[..., half:]
    return jnp.concatenate(
        [first * cosine - second * sine, second * cosine + first * sine], axis=-1
    )


def body(tokens, norm_gain, w_query, w_key, w_value, links):
    kvh_total = lax.axis_size("kvh")
    kvh_at = lax.axis_index("kvh")
    sub_total = lax.axis_size("sub")
    lane_index = lax.axis_index("sub")
    across = [tokens]
    for shift in range(1, kvh_total):
        route = [(j, (j + shift) % kvh_total) for j in range(kvh_total)]
        across.append(lax.ppermute(tokens, "kvh", route))
    pieces = []
    for shift in range(kvh_total):
        pieces.extend(swap_halves(across[shift], sub_total, lane_index))
    blocks = []
    for owner_kvh in range(kvh_total):
        for owner_sub in range(sub_total):
            pick = ((kvh_at - owner_kvh) % kvh_total) * sub_total + (lane_index - owner_sub) % sub_total
            blocks.append(lax.select_n(pick, *pieces))
    gathered = jnp.concatenate(blocks, axis=1)
    widened = gathered.astype(jnp.float32)
    mean_square = jnp.mean(widened * widened, axis=-1, keepdims=True)
    row_scale = lax.rsqrt(mean_square + 1e-05)[:, 0]
    normed = (widened * row_scale[:, None] * norm_gain).astype(jnp.bfloat16)
    row_count = normed.shape[0]
    block_len = row_count // 2
    width = normed.shape[1]
    seq_index = lax.axis_index("seq")
    local_rows = jnp.arange(row_count, dtype=jnp.int32)
    positions = seq_index * row_count + local_rows
    head_size = w_key.shape[2]
    local_groups = w_key.shape[1]
    per_group = w_query.shape[2] // head_size
    queries = jnp.einsum("td,dgc->tgc", normed, w_query, preferred_element_type=jnp.float32)
    queries = rotate(
        queries.reshape(row_count, local_groups, per_group, head_size), positions
    ).astype(jnp.bfloat16)
    sub_count = lax.axis_size("sub")
    sub_index = lax.axis_index("sub")
    row_share = w_key.shape[0]
    key_more = None
    value_more = None
    for shift in range(sub_count):
        if shift == 0:
            key_part, value_part = w_key, w_value
        else:
            route = [(j, (j + shift) % sub_count) for j in range(sub_count)]
            weight_pair = lax.ppermute(jnp.stack([w_key, w_value]), "sub", route)
            key_part, value_part = weight_pair[0], weight_pair[1]
        source = (sub_index - shift) % sub_count
        rows = lax.dynamic_slice_in_dim(normed, source * row_share, row_share, 1)
        key_step = jnp.einsum("td,dgh->tgh", rows, key_part, preferred_element_type=jnp.float32)
        value_step = jnp.einsum("td,dgh->tgh", rows, value_part, preferred_element_type=jnp.float32)
        key_more = key_step if key_more is None else key_more + key_step
        value_more = value_step if value_more is None else value_more + value_step
    keys = rotate(key_more, positions).astype(jnp.bfloat16)
    values = value_more.astype(jnp.bfloat16)
    block_ids = seq_index * 2 + jnp.arange(2, dtype=jnp.int32)
    query_block = local_rows // block_len
    scale = 1.0 / math.sqrt(head_size)
    scores = jnp.einsum("tgrh,ugh->grtu", queries, keys, preferred_element_type=jnp.float32) * scale
    near_linked = lax.dynamic_slice_in_dim(links[0], seq_index * 2, 2) != block_ids
    same_block = query_block[:, None] == query_block[None, :]
    causal = same_block & (local_rows[None, :] <= local_rows[:, None])
    across = ~same_block & near_linked[query_block][:, None]
    allowed = causal | across
    scores = jnp.where(allowed[None, None], scores, -jnp.inf)
    running_max = jnp.max(scores, axis=-1)
    weights = jnp.exp(scores - running_max[..., None])
    total = jnp.sum(weights, axis=-1)
    accum = jnp.einsum(
        "grtu,ugh->tgrh", weights.astype(jnp.bfloat16), values, preferred_element_type=jnp.float32
    )
    query_pairs = queries.reshape(2, block_len, local_groups, per_group, head_size)
    for section in range(1, lax.axis_size("seq").bit_length()):
        far_pair = from_partner(jnp.stack([keys, values]).swapaxes(0, 1), "seq", section - 1)
        far_keys = far_pair[:, 0]
        far_values = far_pair[:, 1]
        far_keys = far_keys.reshape(2, block_len, local_groups, head_size)
        far_values = far_values.reshape(2, block_len, local_groups, head_size)
        linked = lax.dynamic_slice_in_dim(links[section], seq_index * 2, 2) != block_ids
        offset = jnp.where(linked, 0.0, -1e30).astype(jnp.float32)[query_block]
        far_scores = jnp.einsum(
            "jtgrh,jugh->grjtu", query_pairs, far_keys, preferred_element_type=jnp.float32
        )
        far_scores = (
            far_scores.reshape(local_groups, per_group, row_count, block_len) * scale
            + offset[None, None, :, None]
        )
        new_max = jnp.maximum(running_max, jnp.max(far_scores, axis=-1))
        shrink = jnp.exp(running_max - new_max)
        far_weights = jnp.exp(far_scores - new_max[..., None])
        total = total * shrink + jnp.sum(far_weights, axis=-1)
        paired = far_weights.astype(jnp.bfloat16).reshape(
            local_groups, per_group, 2, block_len, block_len
        )
        far_sum = jnp.einsum(
            "grjtu,jugh->jtgrh", paired, far_values, preferred_element_type=jnp.float32
        )
        far_sum = far_sum.reshape(row_count, local_groups, per_group, head_size)
        accum = accum * jnp.transpose(shrink, (2, 0, 1))[..., None] + far_sum
        running_max = new_max
    attended = (accum / jnp.transpose(total, (2, 0, 1))[..., None]).astype(jnp.bfloat16)
    attended = attended.reshape(row_count, local_groups, per_group * head_size)
    tile_count = lax.axis_size("kvh") * lax.axis_size("sub")
    tile_cols = width // tile_count
    owner_index = lax.axis_index("kvh") * lax.axis_size("sub") + lax.axis_index("sub")
    owned = lax.dynamic_slice_in_dim(normed, owner_index * tile_cols, tile_cols, 1)
    seq_count = lax.axis_size("seq")
    band = width // seq_count
    inverse_count = 1.0 / (row_count * seq_count)
    share = row_count // sub_count
    raw_columns = lax.all_gather(tokens, "seq", axis=0, tiled=True)
    column_gain = lax.dynamic_slice_in_dim(norm_gain, owner_index * tile_cols, tile_cols, 0)
    mine = lax.dynamic_slice_in_dim(normed, seq_index * band, band, 1)
    gram_sum = jnp.einsum("tc,tr->cr", mine, owned, preferred_element_type=jnp.float32)
    my_rows = lax.dynamic_slice_in_dim(normed, sub_index * share, share, 0)
    for shift in range(1, seq_count):
        target = (seq_index + shift) % seq_count
        outgoing = lax.dynamic_slice_in_dim(my_rows, target * band, band, 1)
        route = [(j, (j + shift) % seq_count) for j in range(seq_count)]
        incoming, their_scale = lax.ppermute((outgoing, row_scale), "seq", route)
        halves = swap_halves(incoming, sub_count, sub_index)
        source = (seq_index - shift) % seq_count
        their_raw = lax.dynamic_slice_in_dim(raw_columns, source * row_count, row_count, 0)
        their_owned = (
            their_raw.astype(jnp.float32) * their_scale[:, None] * column_gain
        ).astype(jnp.bfloat16)
        for lane_shift in range(sub_count):
            half_at = (sub_index - lane_shift) % sub_count
            their_rows = lax.dynamic_slice_in_dim(their_owned, half_at * share, share, 0)
            gram_sum = gram_sum + jnp.einsum(
                "tc,tr->cr", halves[lane_shift], their_rows, preferred_element_type=jnp.float32
            )
    gram_sum = gram_sum * inverse_count
    gram_tile = gram_sum
    return (attended, gram_tile)


def solution(mesh):
    placed = (
        P(("grp", "seq"), ("kvh", "sub")),
        P(),
        P(None, "kvh", "sub"),
        P("sub", "kvh", None),
        P("sub", "kvh", None),
        P(),
    )
    return jax.shard_map(
        body,
        mesh=mesh,
        in_specs=placed,
        out_specs=(P(("grp", "seq"), "kvh", "sub"), P(("grp", "seq"), ("kvh", "sub"))),
        check_vma=False,
    )
```

```python
import math

import jax
import jax.numpy as jnp
from jax import lax
from jax.sharding import PartitionSpec as P

rope_base = 500000.0


def from_partner(block, axis, bit):
    count = lax.axis_size(axis)
    route = []
    for low in range(count):
        high = low | 1 << bit
        if high != low and high < count:
            route += [(low, high), (high, low)]
    return lax.ppermute(block, axis, route)


def swap_halves(pieces, count, index):
    whole = [None] * count
    whole[0] = pieces
    for shift in range(1, count):
        route = [(j, (j + shift) % count) for j in range(count)]
        whole[shift] = lax.ppermute(pieces, "sub", route)
    return whole


def split_send(blocks, axis, bit):
    count = lax.axis_size("sub")
    index = lax.axis_index("sub")
    share = blocks[0].shape[0] // count
    mine = tuple(lax.dynamic_slice_in_dim(b, index * share, share, 0) for b in blocks)
    got = from_partner(mine, axis, bit)
    whole = swap_halves(got, count, index)
    out = []
    for n, b in enumerate(blocks):
        full = jnp.zeros_like(b)
        for shift in range(count):
            source = (index - shift) % count
            full = lax.dynamic_update_slice_in_dim(full, whole[shift][n], source * share, 0)
        out.append(full)
    return tuple(out)


def rotate(vectors, positions):
    width = vectors.shape[-1]
    half = width // 2
    inverse = jnp.exp(jnp.arange(half, dtype=jnp.float32) * (-2.0 * math.log(rope_base) / width))
    angles = positions.astype(jnp.float32)[:, None] * inverse[None, :]
    shape = (angles.shape[0],) + (1,) * (vectors.ndim - 2) + (half,)
    cosine = jnp.cos(angles).reshape(shape)
    sine = jnp.sin(angles).reshape(shape)
    first = vectors[..., :half]
    second = vectors[..., half:]
    return jnp.concatenate(
        [first * cosine - second * sine, second * cosine + first * sine], axis=-1
    )


def body(tokens, norm_gain, w_query, w_key, w_value, links):
    kvh_total = lax.axis_size("kvh")
    kvh_at = lax.axis_index("kvh")
    sub_total = lax.axis_size("sub")
    lane_index = lax.axis_index("sub")
    across = [tokens]
    for shift in range(1, kvh_total):
        route = [(j, (j + shift) % kvh_total) for j in range(kvh_total)]
        across.append(lax.ppermute(tokens, "kvh", route))
    pieces = []
    for shift in range(kvh_total):
        pieces.extend(swap_halves(across[shift], sub_total, lane_index))
    blocks = []
    for owner_kvh in range(kvh_total):
        for owner_sub in range(sub_total):
            pick = ((kvh_at - owner_kvh) % kvh_total) * sub_total + (lane_index - owner_sub) % sub_total
            blocks.append(lax.select_n(pick, *pieces))
    gathered = jnp.concatenate(blocks, axis=1)
    widened = gathered.astype(jnp.float32)
    mean_square = jnp.mean(widened * widened, axis=-1, keepdims=True)
    row_scale = lax.rsqrt(mean_square + 1e-05)[:, 0]
    normed = (widened * row_scale[:, None] * norm_gain).astype(jnp.bfloat16)
    row_count = normed.shape[0]
    block_len = row_count // 2
    width = normed.shape[1]
    seq_index = lax.axis_index("seq")
    local_rows = jnp.arange(row_count, dtype=jnp.int32)
    positions = seq_index * row_count + local_rows
    head_size = w_key.shape[2]
    local_groups = w_key.shape[1]
    per_group = w_query.shape[2] // head_size
    queries = jnp.einsum("td,dgc->tgc", normed, w_query, preferred_element_type=jnp.float32)
    queries = rotate(
        queries.reshape(row_count, local_groups, per_group, head_size), positions
    ).astype(jnp.bfloat16)
    sub_count = lax.axis_size("sub")
    sub_index = lax.axis_index("sub")
    row_share = w_key.shape[0]
    key_more = None
    value_more = None
    for shift in range(sub_count):
        if shift == 0:
            key_part, value_part = w_key, w_value
        else:
            route = [(j, (j + shift) % sub_count) for j in range(sub_count)]
            weight_pair = lax.ppermute(jnp.stack([w_key, w_value]), "sub", route)
            key_part, value_part = weight_pair[0], weight_pair[1]
        source = (sub_index - shift) % sub_count
        rows = lax.dynamic_slice_in_dim(normed, source * row_share, row_share, 1)
        key_step = jnp.einsum("td,dgh->tgh", rows, key_part, preferred_element_type=jnp.float32)
        value_step = jnp.einsum("td,dgh->tgh", rows, value_part, preferred_element_type=jnp.float32)
        key_more = key_step if key_more is None else key_more + key_step
        value_more = value_step if value_more is None else value_more + value_step
    keys = rotate(key_more, positions).astype(jnp.bfloat16)
    values = value_more.astype(jnp.bfloat16)
    block_ids = seq_index * 2 + jnp.arange(2, dtype=jnp.int32)
    query_block = local_rows // block_len
    scale = 1.0 / math.sqrt(head_size)
    scores = jnp.einsum("tgrh,ugh->grtu", queries, keys, preferred_element_type=jnp.float32) * scale
    near_linked = lax.dynamic_slice_in_dim(links[0], seq_index * 2, 2) != block_ids
    same_block = query_block[:, None] == query_block[None, :]
    causal = same_block & (local_rows[None, :] <= local_rows[:, None])
    across = ~same_block & near_linked[query_block][:, None]
    allowed = causal | across
    scores = jnp.where(allowed[None, None], scores, -jnp.inf)
    running_max = jnp.max(scores, axis=-1)
    weights = jnp.exp(scores - running_max[..., None])
    total = jnp.sum(weights, axis=-1)
    accum = jnp.einsum(
        "grtu,ugh->tgrh", weights.astype(jnp.bfloat16), values, preferred_element_type=jnp.float32
    )
    query_pairs = queries.reshape(2, block_len, local_groups, per_group, head_size)
    seq_count = lax.axis_size("seq")
    band = width // seq_count
    share = row_count // sub_count
    my_rows = lax.dynamic_slice_in_dim(normed, sub_index * share, share, 0)
    arrived = []
    for shift in range(1, seq_count):
        target = (seq_index + shift) % seq_count
        outgoing = lax.dynamic_slice_in_dim(my_rows, target * band, band, 1)
        route = [(j, (j + shift) % seq_count) for j in range(seq_count)]
        arrived.append(lax.ppermute((outgoing, row_scale), "seq", route))
    kv_pair = jnp.stack([keys, values]).swapaxes(0, 1)
    arrived, kv_pair = lax.optimization_barrier((arrived, kv_pair))
    for section in range(1, seq_count.bit_length()):
        (far_pair,) = split_send((kv_pair,), "seq", section - 1)
        far_keys = far_pair[:, 0]
        far_values = far_pair[:, 1]
        far_keys = far_keys.reshape(2, block_len, local_groups, head_size)
        far_values = far_values.reshape(2, block_len, local_groups, head_size)
        linked = lax.dynamic_slice_in_dim(links[section], seq_index * 2, 2) != block_ids
        offset = jnp.where(linked, 0.0, -1e30).astype(jnp.float32)[query_block]
        far_scores = jnp.einsum(
            "jtgrh,jugh->grjtu", query_pairs, far_keys, preferred_element_type=jnp.float32
        )
        far_scores = (
            far_scores.reshape(local_groups, per_group, row_count, block_len) * scale
            + offset[None, None, :, None]
        )
        new_max = jnp.maximum(running_max, jnp.max(far_scores, axis=-1))
        shrink = jnp.exp(running_max - new_max)
        far_weights = jnp.exp(far_scores - new_max[..., None])
        total = total * shrink + jnp.sum(far_weights, axis=-1)
        paired = far_weights.astype(jnp.bfloat16).reshape(
            local_groups, per_group, 2, block_len, block_len
        )
        far_sum = jnp.einsum(
            "grjtu,jugh->jtgrh", paired, far_values, preferred_element_type=jnp.float32
        )
        far_sum = far_sum.reshape(row_count, local_groups, per_group, head_size)
        accum = accum * jnp.transpose(shrink, (2, 0, 1))[..., None] + far_sum
        running_max = new_max
    attended = (accum / jnp.transpose(total, (2, 0, 1))[..., None]).astype(jnp.bfloat16)
    attended = attended.reshape(row_count, local_groups, per_group * head_size)
    tile_count = lax.axis_size("kvh") * lax.axis_size("sub")
    tile_cols = width // tile_count
    owner_index = lax.axis_index("kvh") * lax.axis_size("sub") + lax.axis_index("sub")
    owned = lax.dynamic_slice_in_dim(normed, owner_index * tile_cols, tile_cols, 1)
    seq_count = lax.axis_size("seq")
    band = width // seq_count
    inverse_count = 1.0 / (row_count * seq_count)
    share = row_count // sub_count
    raw_columns = lax.all_gather(tokens, "seq", axis=0, tiled=True)
    column_gain = lax.dynamic_slice_in_dim(norm_gain, owner_index * tile_cols, tile_cols, 0)
    mine = lax.dynamic_slice_in_dim(normed, seq_index * band, band, 1)
    gram_sum = jnp.einsum("tc,tr->cr", mine, owned, preferred_element_type=jnp.float32)
    for shift in range(1, seq_count):
        incoming, their_scale = arrived[shift - 1]
        halves = swap_halves(incoming, sub_count, sub_index)
        source = (seq_index - shift) % seq_count
        their_raw = lax.dynamic_slice_in_dim(raw_columns, source * row_count, row_count, 0)
        their_owned = (
            their_raw.astype(jnp.float32) * their_scale[:, None] * column_gain
        ).astype(jnp.bfloat16)
        for lane_shift in range(sub_count):
            half_at = (sub_index - lane_shift) % sub_count
            their_rows = lax.dynamic_slice_in_dim(their_owned, half_at * share, share, 0)
            gram_sum = gram_sum + jnp.einsum(
                "tc,tr->cr", halves[lane_shift], their_rows, preferred_element_type=jnp.float32
            )
    gram_sum = gram_sum * inverse_count
    gram_tile = gram_sum
    return (attended, gram_tile)


def solution(mesh):
    placed = (
        P(("grp", "seq"), ("kvh", "sub")),
        P(),
        P(None, "kvh", "sub"),
        P("sub", "kvh", None),
        P("sub", "kvh", None),
        P(),
    )
    return jax.shard_map(
        body,
        mesh=mesh,
        in_specs=placed,
        out_specs=(P(("grp", "seq"), "kvh", "sub"), P(("grp", "seq"), ("kvh", "sub"))),
        check_vma=False,
    )
```

```python
import math

import jax
import jax.numpy as jnp
from jax import lax
from jax.sharding import PartitionSpec as P

rope_base = 500000.0


def from_partner(block, axis, bit):
    count = lax.axis_size(axis)
    route = []
    for low in range(count):
        high = low | 1 << bit
        if high != low and high < count:
            route += [(low, high), (high, low)]
    return lax.ppermute(block, axis, route)


def swap_halves(pieces, count, index):
    whole = [None] * count
    whole[0] = pieces
    for shift in range(1, count):
        route = [(j, (j + shift) % count) for j in range(count)]
        whole[shift] = lax.ppermute(pieces, "sub", route)
    return whole


def split_send(blocks, axis, bit):
    count = lax.axis_size("sub")
    index = lax.axis_index("sub")
    share = blocks[0].shape[0] // count
    mine = tuple(lax.dynamic_slice_in_dim(b, index * share, share, 0) for b in blocks)
    got = from_partner(mine, axis, bit)
    whole = swap_halves(got, count, index)
    out = []
    for n, b in enumerate(blocks):
        full = jnp.zeros_like(b)
        for shift in range(count):
            source = (index - shift) % count
            full = lax.dynamic_update_slice_in_dim(full, whole[shift][n], source * share, 0)
        out.append(full)
    return tuple(out)


def rotate(vectors, positions):
    width = vectors.shape[-1]
    half = width // 2
    inverse = jnp.exp(jnp.arange(half, dtype=jnp.float32) * (-2.0 * math.log(rope_base) / width))
    angles = positions.astype(jnp.float32)[:, None] * inverse[None, :]
    shape = (angles.shape[0],) + (1,) * (vectors.ndim - 2) + (half,)
    cosine = jnp.cos(angles).reshape(shape)
    sine = jnp.sin(angles).reshape(shape)
    first = vectors[..., :half]
    second = vectors[..., half:]
    return jnp.concatenate(
        [first * cosine - second * sine, second * cosine + first * sine], axis=-1
    )


def body(tokens, norm_gain, w_query, w_key, w_value, links):
    kvh_total = lax.axis_size("kvh")
    kvh_at = lax.axis_index("kvh")
    sub_total = lax.axis_size("sub")
    lane_index = lax.axis_index("sub")
    across = [tokens]
    for shift in range(1, kvh_total):
        route = [(j, (j + shift) % kvh_total) for j in range(kvh_total)]
        across.append(lax.ppermute(tokens, "kvh", route))
    pieces = []
    for shift in range(kvh_total):
        pieces.extend(swap_halves(across[shift], sub_total, lane_index))
    blocks = []
    for owner_kvh in range(kvh_total):
        for owner_sub in range(sub_total):
            pick = ((kvh_at - owner_kvh) % kvh_total) * sub_total + (lane_index - owner_sub) % sub_total
            blocks.append(lax.select_n(pick, *pieces))
    gathered = jnp.concatenate(blocks, axis=1)
    widened = gathered.astype(jnp.float32)
    mean_square = jnp.mean(widened * widened, axis=-1, keepdims=True)
    row_scale = lax.rsqrt(mean_square + 1e-05)[:, 0]
    normed = (widened * row_scale[:, None] * norm_gain).astype(jnp.bfloat16)
    row_count = normed.shape[0]
    block_len = row_count // 2
    width = normed.shape[1]
    seq_index = lax.axis_index("seq")
    local_rows = jnp.arange(row_count, dtype=jnp.int32)
    positions = seq_index * row_count + local_rows
    head_size = w_key.shape[2]
    local_groups = w_key.shape[1]
    per_group = w_query.shape[2] // head_size
    queries = jnp.einsum("td,dgc->tgc", normed, w_query, preferred_element_type=jnp.float32)
    queries = rotate(
        queries.reshape(row_count, local_groups, per_group, head_size), positions
    ).astype(jnp.bfloat16)
    sub_count = lax.axis_size("sub")
    sub_index = lax.axis_index("sub")
    row_share = w_key.shape[0]
    key_more = None
    value_more = None
    for shift in range(sub_count):
        if shift == 0:
            key_part, value_part = w_key, w_value
        else:
            route = [(j, (j + shift) % sub_count) for j in range(sub_count)]
            weight_stack, normed = lax.optimization_barrier((jnp.stack([w_key, w_value]), normed))
            weight_pair = lax.ppermute(weight_stack, "sub", route)
            key_part, value_part = weight_pair[0], weight_pair[1]
        source = (sub_index - shift) % sub_count
        rows = lax.dynamic_slice_in_dim(normed, source * row_share, row_share, 1)
        key_step = jnp.einsum("td,dgh->tgh", rows, key_part, preferred_element_type=jnp.float32)
        value_step = jnp.einsum("td,dgh->tgh", rows, value_part, preferred_element_type=jnp.float32)
        key_more = key_step if key_more is None else key_more + key_step
        value_more = value_step if value_more is None else value_more + value_step
    keys = rotate(key_more, positions).astype(jnp.bfloat16)
    values = value_more.astype(jnp.bfloat16)
    block_ids = seq_index * 2 + jnp.arange(2, dtype=jnp.int32)
    query_block = local_rows // block_len
    scale = 1.0 / math.sqrt(head_size)
    scores = jnp.einsum("tgrh,ugh->grtu", queries, keys, preferred_element_type=jnp.float32) * scale
    near_linked = lax.dynamic_slice_in_dim(links[0], seq_index * 2, 2) != block_ids
    same_block = query_block[:, None] == query_block[None, :]
    causal = same_block & (local_rows[None, :] <= local_rows[:, None])
    across = ~same_block & near_linked[query_block][:, None]
    allowed = causal | across
    scores = jnp.where(allowed[None, None], scores, -jnp.inf)
    running_max = jnp.max(scores, axis=-1)
    weights = jnp.exp(scores - running_max[..., None])
    total = jnp.sum(weights, axis=-1)
    accum = jnp.einsum(
        "grtu,ugh->tgrh", weights.astype(jnp.bfloat16), values, preferred_element_type=jnp.float32
    )
    query_pairs = queries.reshape(2, block_len, local_groups, per_group, head_size)
    for section in range(1, lax.axis_size("seq").bit_length()):
        (far_pair,) = split_send((jnp.stack([keys, values]).swapaxes(0, 1),), "seq", section - 1)
        far_keys = far_pair[:, 0]
        far_values = far_pair[:, 1]
        far_keys = far_keys.reshape(2, block_len, local_groups, head_size)
        far_values = far_values.reshape(2, block_len, local_groups, head_size)
        linked = lax.dynamic_slice_in_dim(links[section], seq_index * 2, 2) != block_ids
        offset = jnp.where(linked, 0.0, -1e30).astype(jnp.float32)[query_block]
        far_scores = jnp.einsum(
            "jtgrh,jugh->grjtu", query_pairs, far_keys, preferred_element_type=jnp.float32
        )
        far_scores = (
            far_scores.reshape(local_groups, per_group, row_count, block_len) * scale
            + offset[None, None, :, None]
        )
        new_max = jnp.maximum(running_max, jnp.max(far_scores, axis=-1))
        shrink = jnp.exp(running_max - new_max)
        far_weights = jnp.exp(far_scores - new_max[..., None])
        total = total * shrink + jnp.sum(far_weights, axis=-1)
        paired = far_weights.astype(jnp.bfloat16).reshape(
            local_groups, per_group, 2, block_len, block_len
        )
        far_sum = jnp.einsum(
            "grjtu,jugh->jtgrh", paired, far_values, preferred_element_type=jnp.float32
        )
        far_sum = far_sum.reshape(row_count, local_groups, per_group, head_size)
        accum = accum * jnp.transpose(shrink, (2, 0, 1))[..., None] + far_sum
        running_max = new_max
    attended = (accum / jnp.transpose(total, (2, 0, 1))[..., None]).astype(jnp.bfloat16)
    attended = attended.reshape(row_count, local_groups, per_group * head_size)
    tile_count = lax.axis_size("kvh") * lax.axis_size("sub")
    tile_cols = width // tile_count
    owner_index = lax.axis_index("kvh") * lax.axis_size("sub") + lax.axis_index("sub")
    owned = lax.dynamic_slice_in_dim(normed, owner_index * tile_cols, tile_cols, 1)
    seq_count = lax.axis_size("seq")
    band = width // seq_count
    inverse_count = 1.0 / (row_count * seq_count)
    share = row_count // sub_count
    raw_columns = lax.all_gather(tokens, "seq", axis=0, tiled=True)
    column_gain = lax.dynamic_slice_in_dim(norm_gain, owner_index * tile_cols, tile_cols, 0)
    mine = lax.dynamic_slice_in_dim(normed, seq_index * band, band, 1)
    gram_sum = jnp.einsum("tc,tr->cr", mine, owned, preferred_element_type=jnp.float32)
    my_rows = lax.dynamic_slice_in_dim(normed, sub_index * share, share, 0)
    for shift in range(1, seq_count):
        target = (seq_index + shift) % seq_count
        outgoing = lax.dynamic_slice_in_dim(my_rows, target * band, band, 1)
        route = [(j, (j + shift) % seq_count) for j in range(seq_count)]
        incoming, their_scale = lax.ppermute((outgoing, row_scale), "seq", route)
        halves = swap_halves(incoming, sub_count, sub_index)
        source = (seq_index - shift) % seq_count
        their_raw = lax.dynamic_slice_in_dim(raw_columns, source * row_count, row_count, 0)
        their_owned = (
            their_raw.astype(jnp.float32) * their_scale[:, None] * column_gain
        ).astype(jnp.bfloat16)
        for lane_shift in range(sub_count):
            half_at = (sub_index - lane_shift) % sub_count
            their_rows = lax.dynamic_slice_in_dim(their_owned, half_at * share, share, 0)
            gram_sum = gram_sum + jnp.einsum(
                "tc,tr->cr", halves[lane_shift], their_rows, preferred_element_type=jnp.float32
            )
    gram_sum = gram_sum * inverse_count
    gram_tile = gram_sum
    return (attended, gram_tile)


def solution(mesh):
    placed = (
        P(("grp", "seq"), ("kvh", "sub")),
        P(),
        P(None, "kvh", "sub"),
        P("sub", "kvh", None),
        P("sub", "kvh", None),
        P(),
    )
    return jax.shard_map(
        body,
        mesh=mesh,
        in_specs=placed,
        out_specs=(P(("grp", "seq"), "kvh", "sub"), P(("grp", "seq"), ("kvh", "sub"))),
        check_vma=False,
    )
```

```python
import math

import jax
import jax.numpy as jnp
from jax import lax
from jax.sharding import PartitionSpec as P

rope_base = 500000.0


def from_partner(block, axis, bit):
    count = lax.axis_size(axis)
    route = []
    for low in range(count):
        high = low | 1 << bit
        if high != low and high < count:
            route += [(low, high), (high, low)]
    return lax.ppermute(block, axis, route)


def swap_halves(pieces, count, index):
    whole = [None] * count
    whole[0] = pieces
    for shift in range(1, count):
        route = [(j, (j + shift) % count) for j in range(count)]
        whole[shift] = lax.ppermute(pieces, "sub", route)
    return whole


def split_send(blocks, axis, bit):
    count = lax.axis_size("sub")
    index = lax.axis_index("sub")
    share = blocks[0].shape[0] // count
    mine = tuple(lax.dynamic_slice_in_dim(b, index * share, share, 0) for b in blocks)
    got = from_partner(mine, axis, bit)
    whole = swap_halves(got, count, index)
    out = []
    for n, b in enumerate(blocks):
        full = jnp.zeros_like(b)
        for shift in range(count):
            source = (index - shift) % count
            full = lax.dynamic_update_slice_in_dim(full, whole[shift][n], source * share, 0)
        out.append(full)
    return tuple(out)


def rotate(vectors, positions):
    width = vectors.shape[-1]
    half = width // 2
    inverse = jnp.exp(jnp.arange(half, dtype=jnp.float32) * (-2.0 * math.log(rope_base) / width))
    angles = positions.astype(jnp.float32)[:, None] * inverse[None, :]
    shape = (angles.shape[0],) + (1,) * (vectors.ndim - 2) + (half,)
    cosine = jnp.cos(angles).reshape(shape)
    sine = jnp.sin(angles).reshape(shape)
    first = vectors[..., :half]
    second = vectors[..., half:]
    return jnp.concatenate(
        [first * cosine - second * sine, second * cosine + first * sine], axis=-1
    )


def body(tokens, norm_gain, w_query, w_key, w_value, links):
    kvh_total = lax.axis_size("kvh")
    kvh_at = lax.axis_index("kvh")
    sub_total = lax.axis_size("sub")
    lane_index = lax.axis_index("sub")
    across = [tokens]
    for shift in range(1, kvh_total):
        route = [(j, (j + shift) % kvh_total) for j in range(kvh_total)]
        across.append(lax.ppermute(tokens, "kvh", route))
    pieces = []
    for shift in range(kvh_total):
        pieces.extend(swap_halves(across[shift], sub_total, lane_index))
    blocks = []
    for owner_kvh in range(kvh_total):
        for owner_sub in range(sub_total):
            pick = ((kvh_at - owner_kvh) % kvh_total) * sub_total + (lane_index - owner_sub) % sub_total
            blocks.append(lax.select_n(pick, *pieces))
    gathered = jnp.concatenate(blocks, axis=1)
    widened = gathered.astype(jnp.float32)
    mean_square = jnp.mean(widened * widened, axis=-1, keepdims=True)
    row_scale = lax.rsqrt(mean_square + 1e-05)[:, 0]
    normed = (widened * row_scale[:, None] * norm_gain).astype(jnp.bfloat16)
    row_count = normed.shape[0]
    block_len = row_count // 2
    width = normed.shape[1]
    seq_index = lax.axis_index("seq")
    local_rows = jnp.arange(row_count, dtype=jnp.int32)
    positions = seq_index * row_count + local_rows
    head_size = w_key.shape[2]
    local_groups = w_key.shape[1]
    per_group = w_query.shape[2] // head_size
    queries = jnp.einsum("td,dgc->tgc", normed, w_query, preferred_element_type=jnp.float32)
    queries = rotate(
        queries.reshape(row_count, local_groups, per_group, head_size), positions
    ).astype(jnp.bfloat16)
    sub_count = lax.axis_size("sub")
    sub_index = lax.axis_index("sub")
    row_share = w_key.shape[0]
    key_more = None
    value_more = None
    for shift in range(sub_count):
        if shift == 0:
            key_part, value_part = w_key, w_value
        else:
            route = [(j, (j + shift) % sub_count) for j in range(sub_count)]
            weight_pair = lax.ppermute(jnp.stack([w_key, w_value]), "sub", route)
            key_part, value_part = weight_pair[0], weight_pair[1]
        source = (sub_index - shift) % sub_count
        rows = lax.dynamic_slice_in_dim(normed, source * row_share, row_share, 1)
        key_step = jnp.einsum("td,dgh->tgh", rows, key_part, preferred_element_type=jnp.float32)
        value_step = jnp.einsum("td,dgh->tgh", rows, value_part, preferred_element_type=jnp.float32)
        key_more = key_step if key_more is None else key_more + key_step
        value_more = value_step if value_more is None else value_more + value_step
    keys = rotate(key_more, positions).astype(jnp.bfloat16)
    values = value_more.astype(jnp.bfloat16)
    block_ids = seq_index * 2 + jnp.arange(2, dtype=jnp.int32)
    query_block = local_rows // block_len
    scale = 1.0 / math.sqrt(head_size)
    scores = jnp.einsum("tgrh,ugh->grtu", queries, keys, preferred_element_type=jnp.float32) * scale
    near_linked = lax.dynamic_slice_in_dim(links[0], seq_index * 2, 2) != block_ids
    same_block = query_block[:, None] == query_block[None, :]
    causal = same_block & (local_rows[None, :] <= local_rows[:, None])
    across = ~same_block & near_linked[query_block][:, None]
    allowed = causal | across
    scores = jnp.where(allowed[None, None], scores, -jnp.inf)
    running_max = jnp.max(scores, axis=-1)
    weights = jnp.exp(scores - running_max[..., None])
    total = jnp.sum(weights, axis=-1)
    accum = jnp.einsum(
        "grtu,ugh->tgrh", weights.astype(jnp.bfloat16), values, preferred_element_type=jnp.float32
    )
    query_pairs = queries.reshape(2, block_len, local_groups, per_group, head_size)
    for section in range(1, lax.axis_size("seq").bit_length()):
        (far_pair,) = split_send((jnp.stack([keys, values]).swapaxes(0, 1),), "seq", section - 1)
        far_keys = far_pair[:, 0]
        far_values = far_pair[:, 1]
        far_keys = far_keys.reshape(2, block_len, local_groups, head_size)
        far_values = far_values.reshape(2, block_len, local_groups, head_size)
        linked = lax.dynamic_slice_in_dim(links[section], seq_index * 2, 2) != block_ids
        offset = jnp.where(linked, 0.0, -1e30).astype(jnp.float32)[query_block]
        far_scores = jnp.einsum(
            "jtgrh,jugh->grjtu", query_pairs, far_keys, preferred_element_type=jnp.float32
        )
        far_scores = (
            far_scores.reshape(local_groups, per_group, row_count, block_len) * scale
            + offset[None, None, :, None]
        )
        new_max = jnp.maximum(running_max, jnp.max(far_scores, axis=-1))
        shrink = jnp.exp(running_max - new_max)
        far_weights = jnp.exp(far_scores - new_max[..., None])
        total = total * shrink + jnp.sum(far_weights, axis=-1)
        paired = far_weights.astype(jnp.bfloat16).reshape(
            local_groups, per_group, 2, block_len, block_len
        )
        far_sum = jnp.einsum(
            "grjtu,jugh->jtgrh", paired, far_values, preferred_element_type=jnp.float32
        )
        far_sum = far_sum.reshape(row_count, local_groups, per_group, head_size)
        accum = accum * jnp.transpose(shrink, (2, 0, 1))[..., None] + far_sum
        running_max = new_max
    attended = (accum / jnp.transpose(total, (2, 0, 1))[..., None]).astype(jnp.bfloat16)
    attended = attended.reshape(row_count, local_groups, per_group * head_size)
    tile_count = lax.axis_size("kvh") * lax.axis_size("sub")
    tile_cols = width // tile_count
    owner_index = lax.axis_index("kvh") * lax.axis_size("sub") + lax.axis_index("sub")
    owned = lax.dynamic_slice_in_dim(normed, owner_index * tile_cols, tile_cols, 1)
    seq_count = lax.axis_size("seq")
    band = width // seq_count
    inverse_count = 1.0 / (row_count * seq_count)
    share = row_count // sub_count
    raw_columns = lax.all_gather(tokens, "seq", axis=0, tiled=True)
    column_gain = lax.dynamic_slice_in_dim(norm_gain, owner_index * tile_cols, tile_cols, 0)
    mine = lax.dynamic_slice_in_dim(normed, seq_index * band, band, 1)
    gram_sum = jnp.einsum("tc,tr->cr", mine, owned, preferred_element_type=jnp.float32)
    my_rows = lax.dynamic_slice_in_dim(normed, sub_index * share, share, 0)
    for shift in range(1, seq_count):
        target = (seq_index + shift) % seq_count
        outgoing = lax.dynamic_slice_in_dim(my_rows, target * band, band, 1)
        route = [(j, (j + shift) % seq_count) for j in range(seq_count)]
        incoming, their_scale = lax.ppermute((outgoing, row_scale), "seq", route)
        halves = swap_halves(incoming, sub_count, sub_index)
        source = (seq_index - shift) % seq_count
        their_raw = lax.dynamic_slice_in_dim(raw_columns, source * row_count, row_count, 0)
        their_owned = (
            their_raw.astype(jnp.float32) * their_scale[:, None] * column_gain
        ).astype(jnp.bfloat16)
        in_order = [
            lax.select_n((sub_index - lane) % sub_count, *halves) for lane in range(sub_count)
        ]
        gram_sum = gram_sum + jnp.einsum(
            "tc,tr->cr",
            jnp.concatenate(in_order, axis=0),
            their_owned,
            preferred_element_type=jnp.float32,
        )
    gram_sum = gram_sum * inverse_count
    gram_tile = gram_sum
    return (attended, gram_tile)


def solution(mesh):
    placed = (
        P(("grp", "seq"), ("kvh", "sub")),
        P(),
        P(None, "kvh", "sub"),
        P("sub", "kvh", None),
        P("sub", "kvh", None),
        P(),
    )
    return jax.shard_map(
        body,
        mesh=mesh,
        in_specs=placed,
        out_specs=(P(("grp", "seq"), "kvh", "sub"), P(("grp", "seq"), ("kvh", "sub"))),
        check_vma=False,
    )
```

```python
import math

import jax
import jax.numpy as jnp
from jax import lax
from jax.sharding import PartitionSpec as P

rope_base = 500000.0


def from_partner(block, axis, bit):
    count = lax.axis_size(axis)
    route = []
    for low in range(count):
        high = low | 1 << bit
        if high != low and high < count:
            route += [(low, high), (high, low)]
    return lax.ppermute(block, axis, route)


def swap_halves(pieces, count, index):
    whole = [None] * count
    whole[0] = pieces
    for shift in range(1, count):
        route = [(j, (j + shift) % count) for j in range(count)]
        whole[shift] = lax.ppermute(pieces, "sub", route)
    return whole


def split_send(blocks, axis, bit):
    count = lax.axis_size("sub")
    index = lax.axis_index("sub")
    share = blocks[0].shape[0] // count
    mine = tuple(lax.dynamic_slice_in_dim(b, index * share, share, 0) for b in blocks)
    got = from_partner(mine, axis, bit)
    whole = swap_halves(got, count, index)
    out = []
    for n, b in enumerate(blocks):
        full = jnp.zeros_like(b)
        for shift in range(count):
            source = (index - shift) % count
            full = lax.dynamic_update_slice_in_dim(full, whole[shift][n], source * share, 0)
        out.append(full)
    return tuple(out)


def rotate(vectors, positions):
    width = vectors.shape[-1]
    half = width // 2
    inverse = jnp.exp(jnp.arange(half, dtype=jnp.float32) * (-2.0 * math.log(rope_base) / width))
    angles = positions.astype(jnp.float32)[:, None] * inverse[None, :]
    shape = (angles.shape[0],) + (1,) * (vectors.ndim - 2) + (half,)
    cosine = jnp.cos(angles).reshape(shape)
    sine = jnp.sin(angles).reshape(shape)
    first = vectors[..., :half]
    second = vectors[..., half:]
    return jnp.concatenate(
        [first * cosine - second * sine, second * cosine + first * sine], axis=-1
    )


def body(tokens, norm_gain, w_query, w_key, w_value, links):
    kvh_total = lax.axis_size("kvh")
    kvh_at = lax.axis_index("kvh")
    sub_total = lax.axis_size("sub")
    lane_index = lax.axis_index("sub")
    across = [tokens]
    for shift in range(1, kvh_total):
        route = [(j, (j + shift) % kvh_total) for j in range(kvh_total)]
        across.append(lax.ppermute(tokens, "kvh", route))
    pieces = []
    for shift in range(kvh_total):
        pieces.extend(swap_halves(across[shift], sub_total, lane_index))
    blocks = []
    for owner_kvh in range(kvh_total):
        for owner_sub in range(sub_total):
            pick = ((kvh_at - owner_kvh) % kvh_total) * sub_total + (lane_index - owner_sub) % sub_total
            blocks.append(lax.select_n(pick, *pieces))
    gathered = jnp.concatenate(blocks, axis=1)
    widened = gathered.astype(jnp.float32)
    mean_square = jnp.mean(widened * widened, axis=-1, keepdims=True)
    row_scale = lax.rsqrt(mean_square + 1e-05)[:, 0]
    normed = (widened * row_scale[:, None] * norm_gain).astype(jnp.bfloat16)
    row_count = normed.shape[0]
    block_len = row_count // 2
    width = normed.shape[1]
    seq_index = lax.axis_index("seq")
    local_rows = jnp.arange(row_count, dtype=jnp.int32)
    positions = seq_index * row_count + local_rows
    head_size = w_key.shape[2]
    local_groups = w_key.shape[1]
    per_group = w_query.shape[2] // head_size
    queries = jnp.einsum("td,dgc->tgc", normed, w_query, preferred_element_type=jnp.float32)
    queries = rotate(
        queries.reshape(row_count, local_groups, per_group, head_size), positions
    ).astype(jnp.bfloat16)
    sub_count = lax.axis_size("sub")
    sub_index = lax.axis_index("sub")
    row_share = w_key.shape[0]
    key_more = None
    value_more = None
    for shift in range(sub_count):
        if shift == 0:
            key_part, value_part = w_key, w_value
        else:
            route = [(j, (j + shift) % sub_count) for j in range(sub_count)]
            weight_pair = lax.ppermute(jnp.stack([w_key, w_value]), "sub", route)
            key_part, value_part = weight_pair[0], weight_pair[1]
        source = (sub_index - shift) % sub_count
        rows = lax.dynamic_slice_in_dim(normed, source * row_share, row_share, 1)
        key_step = jnp.einsum("td,dgh->tgh", rows, key_part, preferred_element_type=jnp.float32)
        value_step = jnp.einsum("td,dgh->tgh", rows, value_part, preferred_element_type=jnp.float32)
        key_more = key_step if key_more is None else key_more + key_step
        value_more = value_step if value_more is None else value_more + value_step
    keys = rotate(key_more, positions).astype(jnp.bfloat16)
    values = value_more.astype(jnp.bfloat16)
    block_ids = seq_index * 2 + jnp.arange(2, dtype=jnp.int32)
    query_block = local_rows // block_len
    scale = 1.0 / math.sqrt(head_size)
    scores = jnp.einsum("tgrh,ugh->grtu", queries, keys, preferred_element_type=jnp.float32) * scale
    near_linked = lax.dynamic_slice_in_dim(links[0], seq_index * 2, 2) != block_ids
    same_block = query_block[:, None] == query_block[None, :]
    causal = same_block & (local_rows[None, :] <= local_rows[:, None])
    across = ~same_block & near_linked[query_block][:, None]
    allowed = causal | across
    scores = jnp.where(allowed[None, None], scores, -jnp.inf)
    running_max = jnp.max(scores, axis=-1)
    weights = jnp.exp(scores - running_max[..., None])
    total = jnp.sum(weights, axis=-1)
    accum = jnp.einsum(
        "grtu,ugh->tgrh", weights.astype(jnp.bfloat16), values, preferred_element_type=jnp.float32
    )
    query_pairs = queries.reshape(2, block_len, local_groups, per_group, head_size)
    for section in range(1, lax.axis_size("seq").bit_length()):
        (far_pair,) = split_send((jnp.stack([keys, values]).swapaxes(0, 1),), "seq", section - 1)
        far_keys = far_pair[:, 0]
        far_values = far_pair[:, 1]
        far_keys = far_keys.reshape(2, block_len, local_groups, head_size)
        far_values = far_values.reshape(2, block_len, local_groups, head_size)
        linked = lax.dynamic_slice_in_dim(links[section], seq_index * 2, 2) != block_ids
        offset = jnp.where(linked, 0.0, -1e30).astype(jnp.float32)[query_block]
        far_scores = jnp.einsum(
            "jtgrh,jugh->grjtu", query_pairs, far_keys, preferred_element_type=jnp.float32
        )
        far_scores = (
            far_scores.reshape(local_groups, per_group, row_count, block_len) * scale
            + offset[None, None, :, None]
        )
        new_max = jnp.maximum(running_max, jnp.max(far_scores, axis=-1))
        shrink = jnp.exp(running_max - new_max)
        far_weights = jnp.exp(far_scores - new_max[..., None])
        total = total * shrink + jnp.sum(far_weights, axis=-1)
        paired = far_weights.astype(jnp.bfloat16).reshape(
            local_groups, per_group, 2, block_len, block_len
        )
        far_sum = jnp.einsum(
            "grjtu,jugh->jtgrh", paired, far_values, preferred_element_type=jnp.float32
        )
        far_sum = far_sum.reshape(row_count, local_groups, per_group, head_size)
        accum = accum * jnp.transpose(shrink, (2, 0, 1))[..., None] + far_sum
        running_max = new_max
    attended = (accum / jnp.transpose(total, (2, 0, 1))[..., None]).astype(jnp.bfloat16)
    attended = attended.reshape(row_count, local_groups, per_group * head_size)
    tile_count = lax.axis_size("kvh") * lax.axis_size("sub")
    tile_cols = width // tile_count
    owner_index = lax.axis_index("kvh") * lax.axis_size("sub") + lax.axis_index("sub")
    owned = lax.dynamic_slice_in_dim(normed, owner_index * tile_cols, tile_cols, 1)
    seq_count = lax.axis_size("seq")
    band = width // seq_count
    inverse_count = 1.0 / (row_count * seq_count)
    share = row_count // sub_count
    raw_columns = lax.all_gather(tokens, "seq", axis=0, tiled=True)
    all_scales = lax.all_gather(row_scale, "seq", axis=0, tiled=True)
    column_gain = lax.dynamic_slice_in_dim(norm_gain, owner_index * tile_cols, tile_cols, 0)
    mine = lax.dynamic_slice_in_dim(normed, seq_index * band, band, 1)
    gram_sum = jnp.einsum("tc,tr->cr", mine, owned, preferred_element_type=jnp.float32)
    my_rows = lax.dynamic_slice_in_dim(normed, sub_index * share, share, 0)
    for shift in range(1, seq_count):
        target = (seq_index + shift) % seq_count
        outgoing = lax.dynamic_slice_in_dim(my_rows, target * band, band, 1)
        route = [(j, (j + shift) % seq_count) for j in range(seq_count)]
        incoming = lax.ppermute(outgoing, "seq", route)
        halves = swap_halves(incoming, sub_count, sub_index)
        source = (seq_index - shift) % seq_count
        their_raw = lax.dynamic_slice_in_dim(raw_columns, source * row_count, row_count, 0)
        their_scale = lax.dynamic_slice_in_dim(all_scales, source * row_count, row_count, 0)
        their_owned = (
            their_raw.astype(jnp.float32) * their_scale[:, None] * column_gain
        ).astype(jnp.bfloat16)
        for lane_shift in range(sub_count):
            half_at = (sub_index - lane_shift) % sub_count
            their_rows = lax.dynamic_slice_in_dim(their_owned, half_at * share, share, 0)
            gram_sum = gram_sum + jnp.einsum(
                "tc,tr->cr", halves[lane_shift], their_rows, preferred_element_type=jnp.float32
            )
    gram_sum = gram_sum * inverse_count
    gram_tile = gram_sum
    return (attended, gram_tile)


def solution(mesh):
    placed = (
        P(("grp", "seq"), ("kvh", "sub")),
        P(),
        P(None, "kvh", "sub"),
        P("sub", "kvh", None),
        P("sub", "kvh", None),
        P(),
    )
    return jax.shard_map(
        body,
        mesh=mesh,
        in_specs=placed,
        out_specs=(P(("grp", "seq"), "kvh", "sub"), P(("grp", "seq"), ("kvh", "sub"))),
        check_vma=False,
    )
```
